32 devices in a mesh: ctx: 8 (over y, x, core), tp: 4 (over z).
Axes of the slice: x: 2, y: 2, z: 4, core: 2. Of those that a mesh axis runs over, the one named last changes fastest.
Arguments:
- tokens: bfloat16 [4096, 4096], P(('ctx', 'tp')), may hold values from -6 to 6
- spike_query: int32 [4096, 32], P('ctx', 'tp'), may hold values 0 or 1
- spike_key: int32 [4096, 32], P('ctx', 'tp'), may hold values 0 or 1
- qkv_weight: bfloat16 [4096, 3, 4096], P(None, None, 'tp'), may hold values from -0.09375 to 0.09375
- qkv_blocks: int32 [3, 32, 32], P(None, None, 'tp'), may hold values 0 or 1
- out_weight: bfloat16 [4096, 4096], P('tp'), may hold values from -0.09375 to 0.09375
- out_blocks: int32 [32, 32], P('tp'), may hold values 0 or 1
- cotangent: bfloat16 [4096, 4096], P(('ctx', 'tp')), may hold values from -6 to 6
Outputs:
- layer_out: bfloat16 [4096, 4096], P(('ctx', 'tp'))
- token_grad: bfloat16 [4096, 4096], P(('ctx', 'tp'))
- qkv_grad: float32 [4096, 3, 4096], P('ctx', None, 'tp')
- out_grad: float32 [4096, 4096], P('tp', 'ctx')
The draws below stay inside these ranges and needn't reach their ends.
All inputs are finite; a program needn't handle non-finite values. No bound on the sum of `spike_query` or of `spike_key` or of `qkv_blocks` or of `out_blocks` on one device may be relied on, other than what follows from the above.
Results may differ from the reference program's by a relative error of at most 0.014.
Values may be sent and summed in bfloat16 or wider, within the bound.
No kernel may reach another device: no remote copies, remote signals or barrier semaphores. Data moves between devices by JAX's collectives and lax.ppermute only.
A program may use at most 320 MiB of HBM per device.

```python
import math
import jax
import jax.numpy as jnp
from jax import lax

D = 4096
HEADS = 32
HEAD = 128
BLOCK = 128
TOK_CTX = 512
TOKENS = 4096
NB = 32
N_CTX = 8
N_TP = 4


def set_ends(values, key, least, high):
    index_at = [jax.random.randint(jax.random.fold_in(key, axis), (), 0, length) for axis, length in enumerate(values.shape)]
    widest = values.shape.index(max(values.shape))
    beside = index_at[:widest] + [(index_at[widest] + 1) % values.shape[widest]] + index_at[widest + 1:]
    return values.at[tuple(index_at)].set(least).at[tuple(beside)].set(high)


def strengthened(values, key, source, target, shards_of, factor):
    owner, partner = [(jnp.arange(values.shape[axis_at]) // (values.shape[axis_at] // shards_of)).reshape([-1 if axis == axis_at else 1 for axis in range(values.ndim)]) for axis_at in (source, target)]
    chosen = jax.random.permutation(key, shards_of)[partner]
    strong = (owner == chosen) | (owner == (partner + shards_of // 2) % shards_of)
    return jnp.where(strong, factor * values, values)


def shard_levels(rng, shape, cuts, low, top_value):
    level = 1.0
    for axis_at, blocks in cuts:
        draws = jax.random.uniform(jax.random.fold_in(jax.random.fold_in(rng, 6), axis_at), (blocks,), jnp.float32, low / len(cuts), top_value / len(cuts))
        level = level * jnp.repeat(jnp.exp(draws), shape[axis_at] // blocks).reshape((-1,) + (1,) * (len(shape) - 1 - axis_at))
    return level


def gaussian(own_key, shape, scale, most, shards=(), held_as=jnp.bfloat16):
    values = scale * jax.random.normal(own_key, shape, jnp.float32)
    if shards:
        values = values * shard_levels(own_key, shape, shards, -0.22, 0.18)
    return jnp.clip(values, -most, most).astype(held_as)


def gaussian_with(stream_key, extent, scale, bound, split, heavy, kind=jnp.bfloat16):
    entries = scale * jax.random.normal(stream_key, extent, jnp.float32)
    if split:
        entries = entries * shard_levels(stream_key, extent, split, -0.22, 0.18)
    return jnp.clip(strengthened(entries, jax.random.fold_in(stream_key, 3), *heavy), -bound, bound).astype(kind)


def setup_inputs(seed: int = 0) -> dict:
    arg_keys = jax.random.split(jax.random.key(seed), 9)
    tokens = gaussian_with(arg_keys[0], (TOKENS, D), 1.0, 6.0, ((0, 32),), (0, 1, 32, 2.75))
    spike_query = set_ends((jax.random.randint(arg_keys[1], (TOKENS, HEADS), 0, 2) < 1).astype(jnp.int32), jax.random.fold_in(arg_keys[1], 1), 0, 1)
    spike_key = set_ends((jax.random.randint(arg_keys[2], (TOKENS, HEADS), 0, 2) < 1).astype(jnp.int32), jax.random.fold_in(arg_keys[2], 1), 0, 1)
    qkv_weight = gaussian(arg_keys[3], (D, 3, D), D ** -0.5, 0.09375, ((2, 4),))
    qkv_blocks = set_ends((jax.random.randint(arg_keys[4], (3, NB, NB), 0, 2) < 1).astype(jnp.int32), jax.random.fold_in(arg_keys[4], 1), 0, 1)
    out_weight = gaussian(arg_keys[5], (D, D), D ** -0.5, 0.09375, ((0, 4),))
    out_blocks = set_ends((jax.random.randint(arg_keys[6], (NB, NB), 0, 2) < 1).astype(jnp.int32), jax.random.fold_in(arg_keys[6], 1), 0, 1)
    cotangent = gaussian_with(arg_keys[7], (TOKENS, D), 1.0, 6.0, ((0, 32),), (0, 1, 32, 2.75))
    return dict(tokens=tokens, spike_query=spike_query, spike_key=spike_key, qkv_weight=qkv_weight, qkv_blocks=qkv_blocks, out_weight=out_weight, out_blocks=out_blocks, cotangent=cotangent)


EPSILON = 1e-05

def expand_blocks(blocks):
    row_blocks, col_blocks = blocks.shape
    spread = jnp.broadcast_to(blocks.astype(jnp.bfloat16)[:, None, :, None], (row_blocks, BLOCK, col_blocks, BLOCK))
    return spread.reshape(row_blocks * BLOCK, col_blocks * BLOCK)

def qkv_keep_table(qkv_blocks):
    tables = [expand_blocks(qkv_blocks[projection]) for projection in range(3)]
    return jnp.stack(tables, axis=1)

def exclusive_sum(states, backward):
    zeros_state = jnp.zeros_like(states[:1])
    if backward:
        totals = jnp.flip(jnp.cumsum(jnp.flip(states, 0), axis=0), 0)
        return jnp.concatenate([totals[1:], zeros_state], axis=0)
    totals = jnp.cumsum(states, axis=0)
    return jnp.concatenate([zeros_state, totals[:-1]], axis=0)

def widen(array):
    return array.astype(jnp.float32)

def product(form, left, right):
    return jnp.einsum(form, widen(left), widen(right), precision=lax.Precision.HIGHEST)

def reference(tokens, spike_query, spike_key, qkv_weight, qkv_blocks, out_weight, out_blocks, cotangent):
    features = HEADS * HEAD
    group_width = features // N_TP
    qkv_keep = qkv_keep_table(qkv_blocks)
    qkv_used = qkv_weight * qkv_keep
    out_keep = expand_blocks(out_blocks)
    out_used = out_weight * out_keep
    projected = jnp.dot(tokens, qkv_used.reshape(D, 3 * features), preferred_element_type=jnp.float32).astype(jnp.bfloat16)
    projected = projected.reshape(N_CTX, TOK_CTX, 3, HEADS, HEAD)
    query_spikes = spike_query.reshape(N_CTX, TOK_CTX, HEADS, 1).astype(jnp.bfloat16)
    key_spikes = spike_key.reshape(N_CTX, TOK_CTX, HEADS, 1).astype(jnp.bfloat16)
    query_spiked = projected[:, :, 0] * query_spikes
    key_spiked = projected[:, :, 1] * key_spikes
    values = projected[:, :, 2]
    local_state = product('cshd,cshe->chde', key_spiked, values)
    prior_state = exclusive_sum(local_state, False)
    positions = lax.iota(jnp.int32, TOK_CTX)
    causal_keep = positions[:, None] >= positions[None, :]

    def block_scores(query_block, key_block):
        raw_scores = product('thd,shd->hts', query_block, key_block)
        return jnp.where(causal_keep, raw_scores, 0.0).astype(jnp.bfloat16)

    def forward_block(pieces):
        query_block, key_block, value_block, prior_block = pieces
        scores = block_scores(query_block, key_block)
        return product('hts,she->the', scores, value_block) + product('thd,hde->the', query_block, prior_block)
    mixed_rows = lax.map(forward_block, (query_spiked, key_spiked, values, prior_state))
    inv_rms = lax.rsqrt(lax.optimization_barrier(jnp.mean(mixed_rows * mixed_rows, axis=-1, keepdims=True)) + EPSILON)
    normed = mixed_rows * inv_rms
    attended = normed.astype(jnp.bfloat16).reshape(TOKENS, features)
    group_ids = lax.iota(jnp.int32, N_TP)

    def out_group(running, group_index):
        head_cols = lax.dynamic_slice_in_dim(attended, group_index * group_width, group_width, 1)
        weight_rows = lax.dynamic_slice_in_dim(out_used, group_index * group_width, group_width, 0)
        partial_value = jnp.dot(head_cols, weight_rows, preferred_element_type=jnp.float32).astype(jnp.bfloat16)
        return (running + widen(lax.optimization_barrier(partial_value)), None)
    head_sum = lax.scan(out_group, jnp.zeros((TOKENS, D), jnp.float32), group_ids)[0]
    layer_out = (widen(tokens) + head_sum).astype(jnp.bfloat16)
    grad_attended = jnp.dot(cotangent, out_used.T, preferred_element_type=jnp.float32).reshape(N_CTX, TOK_CTX, HEADS, HEAD)
    inner_mean = lax.optimization_barrier(jnp.mean(grad_attended * normed, axis=-1, keepdims=True))
    grad_mixed = inv_rms * (grad_attended - normed * inner_mean)
    grad_low = grad_mixed.astype(jnp.bfloat16)
    local_adjoint = product('cthd,cthe->chde', query_spiked, grad_mixed)
    after_state = exclusive_sum(local_adjoint, True)

    def backward_block(pieces):
        query_block, key_block, value_block, grad_block, low_block, prior_block, after_block = pieces
        scores = block_scores(query_block, key_block)
        adjoint_scores = jnp.where(causal_keep, product('the,she->hts', low_block, value_block), 0.0).astype(jnp.bfloat16)
        grad_query = product('hts,shd->thd', adjoint_scores, key_block) + product('the,hde->thd', grad_block, prior_block)
        grad_key = product('hts,thd->shd', adjoint_scores, query_block) + product('she,hde->shd', value_block, after_block)
        grad_value = product('hts,the->she', scores, low_block) + product('shd,hde->she', key_block, after_block)
        return (grad_query, grad_key, grad_value)
    grad_query, grad_key, grad_value = lax.map(backward_block, (query_spiked, key_spiked, values, grad_mixed, grad_low, prior_state, after_state))
    grad_proj = jnp.stack([(grad_query * widen(query_spikes)).astype(jnp.bfloat16), (grad_key * widen(key_spikes)).astype(jnp.bfloat16), grad_value.astype(jnp.bfloat16)], axis=2)
    grad_flat = grad_proj.reshape(TOKENS, 3, features)

    def input_group(running, group_index):
        grad_cols = lax.dynamic_slice_in_dim(grad_flat, group_index * group_width, group_width, 2).reshape(TOKENS, 3 * group_width)
        weight_cols = lax.dynamic_slice_in_dim(qkv_used, group_index * group_width, group_width, 2).reshape(D, 3 * group_width)
        partial_value = jnp.dot(grad_cols, weight_cols.T, preferred_element_type=jnp.float32).astype(jnp.bfloat16)
        return (running + widen(lax.optimization_barrier(partial_value)), None)
    token_sum = lax.scan(input_group, jnp.zeros((TOKENS, D), jnp.float32), group_ids)[0]
    token_grad = (widen(cotangent) + token_sum).astype(jnp.bfloat16)
    token_blocks = tokens.reshape(N_CTX, TOK_CTX, D)
    proj_blocks = grad_proj.reshape(N_CTX, TOK_CTX, 3 * features)
    attended_blocks = attended.reshape(N_CTX, TOK_CTX, features)
    cotangent_blocks = cotangent.reshape(N_CTX, TOK_CTX, D)

    def weight_block(running, pieces):
        token_block, proj_block, attended_block, cotangent_block = pieces
        qkv_part = jnp.dot(token_block.T, proj_block, preferred_element_type=jnp.float32).astype(jnp.bfloat16)
        out_part = jnp.dot(attended_block.T, cotangent_block, preferred_element_type=jnp.float32).astype(jnp.bfloat16)
        return ((running[0] + widen(lax.optimization_barrier(qkv_part)), running[1] + widen(lax.optimization_barrier(out_part))), None)
    start_sums = (jnp.zeros((D, 3 * features), jnp.float32), jnp.zeros((features, D), jnp.float32))
    qkv_total, out_total = lax.scan(weight_block, start_sums, (token_blocks, proj_blocks, attended_blocks, cotangent_blocks))[0]
    norm_factor = 1.0 / math.sqrt(TOKENS)
    qkv_grad = qkv_total.reshape(D, 3, features) * widen(qkv_keep) * norm_factor
    out_grad = out_total * widen(out_keep) * norm_factor
    return (layer_out, token_grad, qkv_grad, out_grad)
```

```python
import math

import jax
import jax.numpy as jnp
from jax import lax
from jax.sharding import PartitionSpec as P

BLOCK = 128


EPSILON = 1e-05


def carried_in(value, axis, join, neutral):
    place = lax.axis_index(axis)
    gathered = lax.all_gather(value.astype(jnp.bfloat16), axis)
    state = jnp.zeros_like(value) + jnp.asarray(neutral, value.dtype)

    def carried_one(lap, state):
        return join(state, lax.dynamic_index_in_dim(gathered, lap, 0, False).astype(value.dtype))

    return lax.fori_loop(0, place, carried_one, state)


def entering(value, axis, join, neutral):
    count = lax.axis_size(axis)
    place = lax.axis_index(axis)
    ahead = count - 1 - place
    gathered = lax.all_gather(
        value.astype(jnp.bfloat16 if value.dtype == jnp.float32 else value.dtype), axis
    )
    state = jnp.zeros_like(value) + jnp.asarray(neutral, value.dtype)

    def entering_one(lap, state):
        source = count - 1 - lap
        return join(state, lax.dynamic_index_in_dim(gathered, source, 0, False).astype(value.dtype))

    return lax.fori_loop(0, ahead, entering_one, state)


def expand_blocks(blocks):
    row_blocks, col_blocks = blocks.shape
    spread = jnp.broadcast_to(
        blocks.astype(jnp.bfloat16)[:, None, :, None], (row_blocks, BLOCK, col_blocks, BLOCK)
    )
    return spread.reshape(row_blocks * BLOCK, col_blocks * BLOCK)


def qkv_keep_table(qkv_blocks):
    tables = [expand_blocks(qkv_blocks[projection]) for projection in range(3)]
    return jnp.stack(tables, axis=1)


def add_states(earlier, following):
    return earlier + following


def on_device(
    tokens, spike_query, spike_key, qkv_weight, qkv_blocks, out_weight, out_blocks, cotangent
):
    model_width = tokens.shape[1]
    block_rows = spike_query.shape[0]
    local_heads = spike_query.shape[1]
    features = qkv_weight.shape[2]
    head_width = features // local_heads
    row_blocks = model_width // BLOCK
    col_blocks = features // BLOCK
    highest = lax.Precision.HIGHEST
    qkv_mask = jnp.transpose(qkv_blocks, (1, 0, 2)).astype(jnp.bfloat16)
    qkv_used = (
        qkv_weight.reshape(row_blocks, BLOCK, 3, col_blocks, BLOCK)
        * qkv_mask[:, None, :, :, None]
    ).reshape(model_width, 3 * features)
    out_used = (
        out_weight.reshape(col_blocks, BLOCK, row_blocks, BLOCK)
        * out_blocks.astype(jnp.bfloat16)[:, None, :, None]
    ).reshape(features, model_width)
    gathered = lax.all_gather(tokens, "tp", axis=0, tiled=True)
    projected = jnp.dot(gathered, qkv_used, preferred_element_type=jnp.float32).astype(jnp.bfloat16)
    projected = projected.reshape(block_rows, 3, local_heads, head_width)
    query_spikes = spike_query.astype(jnp.bfloat16)[:, :, None]
    key_spikes = spike_key.astype(jnp.bfloat16)[:, :, None]
    query_spiked = projected[:, 0] * query_spikes
    key_spiked = projected[:, 1] * key_spikes
    values = projected[:, 2]
    query_wide = query_spiked.astype(jnp.float32)
    key_wide = key_spiked.astype(jnp.float32)
    local_state = jnp.einsum("shd,she->hde", key_spiked, values, preferred_element_type=jnp.float32)
    zeros_state = jnp.zeros_like(local_state)
    prior_state = carried_in(local_state, "ctx", add_states, zeros_state)
    positions = lax.iota(jnp.int32, block_rows)
    causal_keep = positions[:, None] >= positions[None, :]
    scores = jnp.einsum(
        "thd,shd->hts", query_spiked, key_spiked, preferred_element_type=jnp.float32
    )
    scores = jnp.where(causal_keep, scores, 0.0).astype(jnp.bfloat16)
    mixed_rows = jnp.einsum("hts,she->the", scores, values, preferred_element_type=jnp.float32)
    mixed_rows = mixed_rows + jnp.einsum("thd,hde->the", query_wide, prior_state, precision=highest)
    inv_rms = lax.rsqrt(jnp.mean(mixed_rows * mixed_rows, axis=-1, keepdims=True) + EPSILON)
    normed = mixed_rows * inv_rms
    attended = normed.astype(jnp.bfloat16).reshape(block_rows, features)
    head_sum = lax.psum_scatter(
        jnp.dot(attended, out_used, preferred_element_type=jnp.float32).astype(jnp.bfloat16),
        "tp",
        scatter_dimension=0,
        tiled=True,
    ).astype(jnp.float32)
    layer_out = (tokens.astype(jnp.float32) + head_sum).astype(jnp.bfloat16)
    grad_rows = lax.all_gather(cotangent, "tp", axis=0, tiled=True)
    ctx_count = lax.axis_size("ctx")
    ctx_place = lax.axis_index("ctx")
    slice_rows = model_width // ctx_count
    slice_blocks = slice_rows // BLOCK
    norm_factor = 1.0 / math.sqrt(block_rows * ctx_count)
    out_part = jnp.einsum("tm,tf->mf", grad_rows, attended, preferred_element_type=jnp.float32)
    out_sum = lax.psum_scatter(
        out_part.astype(jnp.bfloat16), "ctx", scatter_dimension=0, tiled=True
    ).astype(jnp.float32)
    out_keep = lax.dynamic_slice_in_dim(out_blocks, ctx_place * slice_blocks, slice_blocks, 1)
    out_keep = jnp.broadcast_to(
        jnp.transpose(out_keep).astype(jnp.float32)[:, None, :, None],
        (slice_blocks, BLOCK, col_blocks, BLOCK),
    ).reshape(slice_rows, features)
    out_grad = jnp.transpose(out_sum * out_keep * norm_factor)
    grad_attended = jnp.einsum("tm,fm->tf", grad_rows, out_used, preferred_element_type=jnp.float32)
    grad_attended = grad_attended.reshape(block_rows, local_heads, head_width)
    inner_mean = jnp.mean(grad_attended * normed, axis=-1, keepdims=True)
    grad_mixed = inv_rms * (grad_attended - normed * inner_mean)
    grad_low = grad_mixed.astype(jnp.bfloat16)
    local_adjoint = jnp.einsum("thd,the->hde", query_wide, grad_mixed, precision=highest)
    after_state = entering(local_adjoint, "ctx", add_states, zeros_state)
    adjoint_scores = jnp.einsum(
        "the,she->hts", grad_low, values, preferred_element_type=jnp.float32
    )
    adjoint_scores = jnp.where(causal_keep, adjoint_scores, 0.0).astype(jnp.bfloat16)
    grad_query = jnp.einsum(
        "hts,shd->thd", adjoint_scores, key_spiked, preferred_element_type=jnp.float32
    )
    grad_query = grad_query + jnp.einsum("the,hde->thd", grad_mixed, prior_state, precision=highest)
    grad_key = jnp.einsum(
        "hts,thd->shd", adjoint_scores, query_spiked, preferred_element_type=jnp.float32
    )
    grad_key = grad_key + jnp.einsum(
        "she,hde->shd", values.astype(jnp.float32), after_state, precision=highest
    )
    grad_value = jnp.einsum("hts,the->she", scores, grad_low, preferred_element_type=jnp.float32)
    grad_value = grad_value + jnp.einsum("shd,hde->she", key_wide, after_state, precision=highest)
    grad_proj = jnp.stack(
        [
            (grad_query * query_spikes.astype(jnp.float32)).astype(jnp.bfloat16),
            (grad_key * key_spikes.astype(jnp.float32)).astype(jnp.bfloat16),
            grad_value.astype(jnp.bfloat16),
        ],
        axis=1,
    ).reshape(block_rows, 3 * features)
    qkv_part = jnp.einsum("tm,tc->mc", gathered, grad_proj, preferred_element_type=jnp.float32)
    qkv_sum = lax.psum_scatter(
        qkv_part.astype(jnp.bfloat16), "ctx", scatter_dimension=0, tiled=True
    ).astype(jnp.float32)
    qkv_keep = lax.dynamic_slice_in_dim(qkv_mask, ctx_place * slice_blocks, slice_blocks, 0)
    qkv_keep = jnp.broadcast_to(
        qkv_keep.astype(jnp.float32)[:, None, :, :, None],
        (slice_blocks, BLOCK, 3, col_blocks, BLOCK),
    ).reshape(slice_rows, 3, features)
    qkv_grad = qkv_sum.reshape(slice_rows, 3, features) * qkv_keep * norm_factor
    token_sum = lax.psum_scatter(
        jnp.einsum("tc,mc->tm", grad_proj, qkv_used, preferred_element_type=jnp.float32).astype(
            jnp.bfloat16
        ),
        "tp",
        scatter_dimension=0,
        tiled=True,
    ).astype(jnp.float32)
    token_grad = (cotangent.astype(jnp.float32) + token_sum).astype(jnp.bfloat16)
    return (layer_out, token_grad, qkv_grad, out_grad)


def solution(mesh):
    placed = (
        P(("ctx", "tp"), None),
        P("ctx", "tp"),
        P("ctx", "tp"),
        P(None, None, "tp"),
        P(None, None, "tp"),
        P("tp", None),
        P("tp", None),
        P(("ctx", "tp"), None),
    )
    return jax.shard_map(
        on_device,
        mesh=mesh,
        in_specs=placed,
        out_specs=(
            P(("ctx", "tp"), None),
            P(("ctx", "tp"), None),
            P("ctx", None, "tp"),
            P("tp", "ctx"),
        ),
        check_vma=False,
    )
```

```python
import math

import jax
import jax.numpy as jnp
from jax import lax
from jax.experimental import pallas as pl
from jax.experimental.pallas import tpu as pltpu
from jax.sharding import PartitionSpec as P

BLOCK = 128


EPSILON = 1e-05

def _tile(n, choices=(1024, 512, 256, 128)):
    for c in choices:
        if n % c == 0:
            return c
    return n

def _nn_kernel(a_ref, w_ref, m_ref, o_ref, acc_ref, wm_ref):
    k = pl.program_id(1)
    @pl.when(k == 0)
    def _():
        acc_ref[...] = jnp.zeros_like(acc_ref)
    for g in range(w_ref.shape[0] // BLOCK):
        rows = slice(g * BLOCK, (g + 1) * BLOCK)
        wm_ref[rows, :] = w_ref[rows, :] * m_ref[g]
    acc_ref[...] += jnp.dot(a_ref[...], wm_ref[...], preferred_element_type=jnp.float32)
    @pl.when(k == pl.num_programs(1) - 1)
    def _():
        o_ref[...] = acc_ref[...].astype(o_ref.dtype)

def _nt_kernel(a_ref, w_ref, m_ref, o_ref, acc_ref, wm_ref):
    k = pl.program_id(1)
    @pl.when(k == 0)
    def _():
        acc_ref[...] = jnp.zeros_like(acc_ref)
    for g in range(w_ref.shape[0] // BLOCK):
        rows = slice(g * BLOCK, (g + 1) * BLOCK)
        wm_ref[rows, :] = w_ref[rows, :] * m_ref[g]
    acc_ref[...] += lax.dot_general(a_ref[...], wm_ref[...], (((1,), (1,)), ((), ())), preferred_element_type=jnp.float32)
    @pl.when(k == pl.num_programs(1) - 1)
    def _():
        o_ref[...] = acc_ref[...].astype(o_ref.dtype)

def masked_matmul(a, w, mask, out_dtype, transpose_w):
    m = a.shape[0]
    rows, cols = w.shape
    if transpose_w:
        tr, tk = _tile(rows), _tile(cols)
        grid = (rows // tr, cols // tk)
        in_specs = [
            pl.BlockSpec((m, tk), lambda i, k: (0, k)),
            pl.BlockSpec((tr, tk), lambda i, k: (i, k)),
            pl.BlockSpec((tr // BLOCK, 1, tk), lambda i, k: (i, 0, k)),
        ]
        out_spec = pl.BlockSpec((m, tr), lambda i, k: (0, i))
        out_shape = jax.ShapeDtypeStruct((m, rows), out_dtype)
        scratch = [pltpu.VMEM((m, tr), jnp.float32), pltpu.VMEM((tr, tk), w.dtype)]
        kernel = _nt_kernel
        n_out = rows
    else:
        tk, tn = _tile(rows), _tile(cols)
        grid = (cols // tn, rows // tk)
        in_specs = [
            pl.BlockSpec((m, tk), lambda j, k: (0, k)),
            pl.BlockSpec((tk, tn), lambda j, k: (k, j)),
            pl.BlockSpec((tk // BLOCK, 1, tn), lambda j, k: (k, 0, j)),
        ]
        out_spec = pl.BlockSpec((m, tn), lambda j, k: (0, j))
        out_shape = jax.ShapeDtypeStruct((m, cols), out_dtype)
        scratch = [pltpu.VMEM((m, tn), jnp.float32), pltpu.VMEM((tk, tn), w.dtype)]
        kernel = _nn_kernel
        n_out = cols
    flops = 2 * m * rows * cols
    nbytes = a.size * a.dtype.itemsize * (grid[0]) + w.size * w.dtype.itemsize + m * n_out * jnp.dtype(out_dtype).itemsize
    return pl.pallas_call(
        kernel,
        grid=grid,
        in_specs=in_specs,
        out_specs=out_spec,
        out_shape=out_shape,
        scratch_shapes=scratch,
        compiler_params=pltpu.CompilerParams(dimension_semantics=("parallel", "arbitrary"), vmem_limit_bytes=48 * 1024 * 1024),
        cost_estimate=pl.CostEstimate(flops=flops, bytes_accessed=nbytes, transcendentals=0),
    )(a, w, mask)


def carried_in(value, axis, join, neutral):
    place = lax.axis_index(axis)
    gathered = lax.all_gather(value.astype(jnp.bfloat16), axis)
    state = jnp.zeros_like(value) + jnp.asarray(neutral, value.dtype)

    def carried_one(lap, state):
        return join(state, lax.dynamic_index_in_dim(gathered, lap, 0, False).astype(value.dtype))

    return lax.fori_loop(0, place, carried_one, state)


def entering(value, axis, join, neutral):
    count = lax.axis_size(axis)
    place = lax.axis_index(axis)
    ahead = count - 1 - place
    gathered = lax.all_gather(
        value.astype(jnp.bfloat16 if value.dtype == jnp.float32 else value.dtype), axis
    )
    state = jnp.zeros_like(value) + jnp.asarray(neutral, value.dtype)

    def entering_one(lap, state):
        source = count - 1 - lap
        return join(state, lax.dynamic_index_in_dim(gathered, source, 0, False).astype(value.dtype))

    return lax.fori_loop(0, ahead, entering_one, state)


def expand_blocks(blocks):
    row_blocks, col_blocks = blocks.shape
    spread = jnp.broadcast_to(
        blocks.astype(jnp.bfloat16)[:, None, :, None], (row_blocks, BLOCK, col_blocks, BLOCK)
    )
    return spread.reshape(row_blocks * BLOCK, col_blocks * BLOCK)


def qkv_keep_table(qkv_blocks):
    tables = [expand_blocks(qkv_blocks[projection]) for projection in range(3)]
    return jnp.stack(tables, axis=1)


def add_states(earlier, following):
    return earlier + following


def on_device(
    tokens, spike_query, spike_key, qkv_weight, qkv_blocks, out_weight, out_blocks, cotangent
):
    model_width = tokens.shape[1]
    block_rows = spike_query.shape[0]
    local_heads = spike_query.shape[1]
    features = qkv_weight.shape[2]
    head_width = features // local_heads
    row_blocks = model_width // BLOCK
    col_blocks = features // BLOCK
    highest = lax.Precision.HIGHEST
    qkv_mask = jnp.transpose(qkv_blocks, (1, 0, 2)).astype(jnp.bfloat16)
    qkv_flat = qkv_weight.reshape(model_width, 3 * features)
    qkv_spread = jnp.broadcast_to(
        qkv_mask[:, :, :, None], (row_blocks, 3, col_blocks, BLOCK)
    ).reshape(row_blocks, 1, 3 * features)
    out_spread = jnp.broadcast_to(
        out_blocks.astype(jnp.bfloat16)[:, :, None], (col_blocks, row_blocks, BLOCK)
    ).reshape(col_blocks, 1, model_width)
    gathered = lax.all_gather(tokens, "tp", axis=0, tiled=True)
    projected = masked_matmul(gathered, qkv_flat, qkv_spread, jnp.bfloat16, False)
    projected = projected.reshape(block_rows, 3, local_heads, head_width)
    query_spikes = spike_query.astype(jnp.bfloat16)[:, :, None]
    key_spikes = spike_key.astype(jnp.bfloat16)[:, :, None]
    query_spiked = projected[:, 0] * query_spikes
    key_spiked = projected[:, 1] * key_spikes
    values = projected[:, 2]
    query_wide = query_spiked.astype(jnp.float32)
    key_wide = key_spiked.astype(jnp.float32)
    local_state = jnp.einsum("shd,she->hde", key_spiked, values, preferred_element_type=jnp.float32)
    zeros_state = jnp.zeros_like(local_state)
    prior_state = carried_in(local_state, "ctx", add_states, zeros_state)
    positions = lax.iota(jnp.int32, block_rows)
    causal_keep = positions[:, None] >= positions[None, :]
    scores = jnp.einsum(
        "thd,shd->hts", query_spiked, key_spiked, preferred_element_type=jnp.float32
    )
    scores = jnp.where(causal_keep, scores, 0.0).astype(jnp.bfloat16)
    mixed_rows = jnp.einsum("hts,she->the", scores, values, preferred_element_type=jnp.float32)
    mixed_rows = mixed_rows + jnp.einsum("thd,hde->the", query_wide, prior_state, precision=highest)
    inv_rms = lax.rsqrt(jnp.mean(mixed_rows * mixed_rows, axis=-1, keepdims=True) + EPSILON)
    normed = mixed_rows * inv_rms
    attended = normed.astype(jnp.bfloat16).reshape(block_rows, features)
    head_sum = lax.psum_scatter(
        masked_matmul(attended, out_weight, out_spread, jnp.bfloat16, False),
        "tp",
        scatter_dimension=0,
        tiled=True,
    ).astype(jnp.float32)
    layer_out = (tokens.astype(jnp.float32) + head_sum).astype(jnp.bfloat16)
    grad_rows = lax.all_gather(cotangent, "tp", axis=0, tiled=True)
    ctx_count = lax.axis_size("ctx")
    ctx_place = lax.axis_index("ctx")
    slice_rows = model_width // ctx_count
    slice_blocks = slice_rows // BLOCK
    norm_factor = 1.0 / math.sqrt(block_rows * ctx_count)
    out_part = jnp.einsum("tm,tf->mf", grad_rows, attended, preferred_element_type=jnp.float32)
    out_sum = lax.psum_scatter(
        out_part.astype(jnp.bfloat16), "ctx", scatter_dimension=0, tiled=True
    ).astype(jnp.float32)
    out_keep = lax.dynamic_slice_in_dim(out_blocks, ctx_place * slice_blocks, slice_blocks, 1)
    out_keep = jnp.broadcast_to(
        jnp.transpose(out_keep).astype(jnp.float32)[:, None, :, None],
        (slice_blocks, BLOCK, col_blocks, BLOCK),
    ).reshape(slice_rows, features)
    out_grad = jnp.transpose(out_sum * out_keep * norm_factor)
    grad_attended = masked_matmul(grad_rows, out_weight, out_spread, jnp.float32, True)
    grad_attended = grad_attended.reshape(block_rows, local_heads, head_width)
    inner_mean = jnp.mean(grad_attended * normed, axis=-1, keepdims=True)
    grad_mixed = inv_rms * (grad_attended - normed * inner_mean)
    grad_low = grad_mixed.astype(jnp.bfloat16)
    local_adjoint = jnp.einsum("thd,the->hde", query_wide, grad_mixed, precision=highest)
    after_state = entering(local_adjoint, "ctx", add_states, zeros_state)
    adjoint_scores = jnp.einsum(
        "the,she->hts", grad_low, values, preferred_element_type=jnp.float32
    )
    adjoint_scores = jnp.where(causal_keep, adjoint_scores, 0.0).astype(jnp.bfloat16)
    grad_query = jnp.einsum(
        "hts,shd->thd", adjoint_scores, key_spiked, preferred_element_type=jnp.float32
    )
    grad_query = grad_query + jnp.einsum("the,hde->thd", grad_mixed, prior_state, precision=highest)
    grad_key = jnp.einsum(
        "hts,thd->shd", adjoint_scores, query_spiked, preferred_element_type=jnp.float32
    )
    grad_key = grad_key + jnp.einsum(
        "she,hde->shd", values.astype(jnp.float32), after_state, precision=highest
    )
    grad_value = jnp.einsum("hts,the->she", scores, grad_low, preferred_element_type=jnp.float32)
    grad_value = grad_value + jnp.einsum("shd,hde->she", key_wide, after_state, precision=highest)
    grad_proj = jnp.stack(
        [
            (grad_query * query_spikes.astype(jnp.float32)).astype(jnp.bfloat16),
            (grad_key * key_spikes.astype(jnp.float32)).astype(jnp.bfloat16),
            grad_value.astype(jnp.bfloat16),
        ],
        axis=1,
    ).reshape(block_rows, 3 * features)
    qkv_part = jnp.einsum("tm,tc->mc", gathered, grad_proj, preferred_element_type=jnp.float32)
    qkv_sum = lax.psum_scatter(
        qkv_part.astype(jnp.bfloat16), "ctx", scatter_dimension=0, tiled=True
    ).astype(jnp.float32)
    qkv_keep = lax.dynamic_slice_in_dim(qkv_mask, ctx_place * slice_blocks, slice_blocks, 0)
    qkv_keep = jnp.broadcast_to(
        qkv_keep.astype(jnp.float32)[:, None, :, :, None],
        (slice_blocks, BLOCK, 3, col_blocks, BLOCK),
    ).reshape(slice_rows, 3, features)
    qkv_grad = qkv_sum.reshape(slice_rows, 3, features) * qkv_keep * norm_factor
    token_sum = lax.psum_scatter(
        masked_matmul(grad_proj, qkv_flat, qkv_spread, jnp.bfloat16, True),
        "tp",
        scatter_dimension=0,
        tiled=True,
    ).astype(jnp.float32)
    token_grad = (cotangent.astype(jnp.float32) + token_sum).astype(jnp.bfloat16)
    return (layer_out, token_grad, qkv_grad, out_grad)


def solution(mesh):
    placed = (
        P(("ctx", "tp"), None),
        P("ctx", "tp"),
        P("ctx", "tp"),
        P(None, None, "tp"),
        P(None, None, "tp"),
        P("tp", None),
        P("tp", None),
        P(("ctx", "tp"), None),
    )
    return jax.shard_map(
        on_device,
        mesh=mesh,
        in_specs=placed,
        out_specs=(
            P(("ctx", "tp"), None),
            P(("ctx", "tp"), None),
            P("ctx", None, "tp"),
            P("tp", "ctx"),
        ),
        check_vma=False,
    )
```

```python
import math

import jax
import jax.numpy as jnp
from jax import lax
from jax.experimental import pallas as pl
from jax.experimental.pallas import tpu as pltpu
from jax.sharding import PartitionSpec as P

BLOCK = 128


EPSILON = 1e-05

def _tile(n, choices=(1024, 512, 256, 128)):
    for c in choices:
        if n % c == 0:
            return c
    return n


def _masked_tile(w_ref, m_ref, wm_ref):
    for g in range(w_ref.shape[0] // BLOCK):
        rows = slice(g * BLOCK, (g + 1) * BLOCK)
        wm_ref[rows, :] = w_ref[rows, :] * m_ref[g]


def _nn_kernel(a_ref, w_ref, m_ref, o_ref, acc_ref, wm_ref):
    k = pl.program_id(2)

    @pl.when(k == 0)
    def _():
        acc_ref[...] = jnp.zeros_like(acc_ref)

    _masked_tile(w_ref, m_ref, wm_ref)
    acc_ref[...] += jnp.dot(a_ref[...], wm_ref[...], preferred_element_type=jnp.float32)

    @pl.when(k == pl.num_programs(2) - 1)
    def _():
        o_ref[...] = acc_ref[...].astype(o_ref.dtype)


def _nt_kernel(a_ref, w_ref, m_ref, o_ref, acc_ref, wm_ref):
    p = pl.program_id(1)
    k = pl.program_id(2)

    @pl.when((p == 0) & (k == 0))
    def _():
        acc_ref[...] = jnp.zeros_like(acc_ref)

    _masked_tile(w_ref, m_ref, wm_ref)
    acc_ref[...] += lax.dot_general(
        a_ref[...], wm_ref[...], (((1,), (1,)), ((), ())), preferred_element_type=jnp.float32
    )

    @pl.when((p == pl.num_programs(1) - 1) & (k == pl.num_programs(2) - 1))
    def _():
        o_ref[...] = acc_ref[...].astype(o_ref.dtype)


def masked_matmul_nn(a, w, mask, out_dtype):
    m = a.shape[0]
    planes, rows, cols = w.shape
    tk, tn = _tile(rows), _tile(cols)
    grid = (planes, cols // tn, rows // tk)
    return pl.pallas_call(
        _nn_kernel,
        grid=grid,
        in_specs=[
            pl.BlockSpec((m, tk), lambda p, j, k: (0, k)),
            pl.BlockSpec((None, tk, tn), lambda p, j, k: (p, k, j)),
            pl.BlockSpec((None, tk // BLOCK, 1, tn), lambda p, j, k: (p, k, 0, j)),
        ],
        out_specs=pl.BlockSpec((None, m, tn), lambda p, j, k: (p, 0, j)),
        out_shape=jax.ShapeDtypeStruct((planes, m, cols), out_dtype),
        scratch_shapes=[pltpu.VMEM((m, tn), jnp.float32), pltpu.VMEM((tk, tn), w.dtype)],
        compiler_params=pltpu.CompilerParams(
            dimension_semantics=("parallel", "parallel", "arbitrary"),
            vmem_limit_bytes=48 * 1024 * 1024,
        ),
        cost_estimate=pl.CostEstimate(
            flops=2 * m * planes * rows * cols,
            bytes_accessed=a.size * 2 * planes * (cols // tn) + w.size * 2
            + m * planes * cols * jnp.dtype(out_dtype).itemsize,
            transcendentals=0,
        ),
    )(a, w, mask)


def masked_matmul_nt(a, w, mask, out_dtype):
    planes, m, _ = a.shape
    _, rows, cols = w.shape
    tr, tk = _tile(rows), _tile(cols)
    grid = (rows // tr, planes, cols // tk)
    return pl.pallas_call(
        _nt_kernel,
        grid=grid,
        in_specs=[
            pl.BlockSpec((None, m, tk), lambda i, p, k: (p, 0, k)),
            pl.BlockSpec((None, tr, tk), lambda i, p, k: (p, i, k)),
            pl.BlockSpec((None, tr // BLOCK, 1, tk), lambda i, p, k: (p, i, 0, k)),
        ],
        out_specs=pl.BlockSpec((m, tr), lambda i, p, k: (0, i)),
        out_shape=jax.ShapeDtypeStruct((m, rows), out_dtype),
        scratch_shapes=[pltpu.VMEM((m, tr), jnp.float32), pltpu.VMEM((tr, tk), w.dtype)],
        compiler_params=pltpu.CompilerParams(
            dimension_semantics=("parallel", "arbitrary", "arbitrary"),
            vmem_limit_bytes=48 * 1024 * 1024,
        ),
        cost_estimate=pl.CostEstimate(
            flops=2 * m * planes * rows * cols,
            bytes_accessed=a.size * 2 * (rows // tr) + w.size * 2
            + m * rows * jnp.dtype(out_dtype).itemsize,
            transcendentals=0,
        ),
    )(a, w, mask)


def carried_in(value, axis, join, neutral):
    place = lax.axis_index(axis)
    gathered = lax.all_gather(value.astype(jnp.bfloat16), axis)
    state = jnp.zeros_like(value) + jnp.asarray(neutral, value.dtype)

    def carried_one(lap, state):
        return join(state, lax.dynamic_index_in_dim(gathered, lap, 0, False).astype(value.dtype))

    return lax.fori_loop(0, place, carried_one, state)


def entering(value, axis, join, neutral):
    count = lax.axis_size(axis)
    place = lax.axis_index(axis)
    ahead = count - 1 - place
    gathered = lax.all_gather(
        value.astype(jnp.bfloat16 if value.dtype == jnp.float32 else value.dtype), axis
    )
    state = jnp.zeros_like(value) + jnp.asarray(neutral, value.dtype)

    def entering_one(lap, state):
        source = count - 1 - lap
        return join(state, lax.dynamic_index_in_dim(gathered, source, 0, False).astype(value.dtype))

    return lax.fori_loop(0, ahead, entering_one, state)


def expand_blocks(blocks):
    row_blocks, col_blocks = blocks.shape
    spread = jnp.broadcast_to(
        blocks.astype(jnp.bfloat16)[:, None, :, None], (row_blocks, BLOCK, col_blocks, BLOCK)
    )
    return spread.reshape(row_blocks * BLOCK, col_blocks * BLOCK)


def qkv_keep_table(qkv_blocks):
    tables = [expand_blocks(qkv_blocks[projection]) for projection in range(3)]
    return jnp.stack(tables, axis=1)


def add_states(earlier, following):
    return earlier + following


def on_device(
    tokens, spike_query, spike_key, qkv_weight, qkv_blocks, out_weight, out_blocks, cotangent
):
    model_width = tokens.shape[1]
    block_rows = spike_query.shape[0]
    local_heads = spike_query.shape[1]
    features = qkv_weight.shape[2]
    head_width = features // local_heads
    row_blocks = model_width // BLOCK
    col_blocks = features // BLOCK
    highest = lax.Precision.HIGHEST
    qkv_planes = jnp.transpose(qkv_weight, (1, 0, 2))
    qkv_spread = jnp.broadcast_to(
        qkv_blocks.astype(jnp.bfloat16)[:, :, None, :, None],
        (3, row_blocks, 1, col_blocks, BLOCK),
    ).reshape(3, row_blocks, 1, features)
    out_planes = out_weight[None]
    out_spread = jnp.broadcast_to(
        out_blocks.astype(jnp.bfloat16)[None, :, None, :, None],
        (1, col_blocks, 1, row_blocks, BLOCK),
    ).reshape(1, col_blocks, 1, model_width)
    gathered = lax.all_gather(tokens, "tp", axis=0, tiled=True)
    projected = masked_matmul_nn(gathered, qkv_planes, qkv_spread, jnp.bfloat16)
    projected = projected.reshape(3, block_rows, local_heads, head_width)
    query_spikes = spike_query.astype(jnp.bfloat16)[:, :, None]
    key_spikes = spike_key.astype(jnp.bfloat16)[:, :, None]
    query_spiked = projected[0] * query_spikes
    key_spiked = projected[1] * key_spikes
    values = projected[2]
    query_wide = query_spiked.astype(jnp.float32)
    key_wide = key_spiked.astype(jnp.float32)
    local_state = jnp.einsum("shd,she->hde", key_spiked, values, preferred_element_type=jnp.float32)
    zeros_state = jnp.zeros_like(local_state)
    prior_state = carried_in(local_state, "ctx", add_states, zeros_state)
    positions = lax.iota(jnp.int32, block_rows)
    causal_keep = positions[:, None] >= positions[None, :]
    scores = jnp.einsum(
        "thd,shd->hts", query_spiked, key_spiked, preferred_element_type=jnp.float32
    )
    scores = jnp.where(causal_keep, scores, 0.0).astype(jnp.bfloat16)
    mixed_rows = jnp.einsum("hts,she->the", scores, values, preferred_element_type=jnp.float32)
    mixed_rows = mixed_rows + jnp.einsum("thd,hde->the", query_wide, prior_state, precision=highest)
    inv_rms = lax.rsqrt(jnp.mean(mixed_rows * mixed_rows, axis=-1, keepdims=True) + EPSILON)
    normed = mixed_rows * inv_rms
    attended = normed.astype(jnp.bfloat16).reshape(block_rows, features)
    head_sum = lax.psum_scatter(
        masked_matmul_nn(attended, out_planes, out_spread, jnp.bfloat16)[0],
        "tp",
        scatter_dimension=0,
        tiled=True,
    ).astype(jnp.float32)
    layer_out = (tokens.astype(jnp.float32) + head_sum).astype(jnp.bfloat16)
    grad_rows = lax.all_gather(cotangent, "tp", axis=0, tiled=True)
    ctx_count = lax.axis_size("ctx")
    ctx_place = lax.axis_index("ctx")
    slice_rows = model_width // ctx_count
    slice_blocks = slice_rows // BLOCK
    norm_factor = 1.0 / math.sqrt(block_rows * ctx_count)
    out_part = jnp.einsum("tm,tf->mf", grad_rows, attended, preferred_element_type=jnp.float32)
    out_sum = lax.psum_scatter(
        out_part.astype(jnp.bfloat16), "ctx", scatter_dimension=0, tiled=True
    ).astype(jnp.float32)
    out_keep = lax.dynamic_slice_in_dim(out_blocks, ctx_place * slice_blocks, slice_blocks, 1)
    out_keep = jnp.broadcast_to(
        jnp.transpose(out_keep).astype(jnp.float32)[:, None, :, None],
        (slice_blocks, BLOCK, col_blocks, BLOCK),
    ).reshape(slice_rows, features)
    out_grad = jnp.transpose(out_sum * out_keep * norm_factor)
    grad_attended = masked_matmul_nt(grad_rows[None], out_planes, out_spread, jnp.float32)
    grad_attended = grad_attended.reshape(block_rows, local_heads, head_width)
    inner_mean = jnp.mean(grad_attended * normed, axis=-1, keepdims=True)
    grad_mixed = inv_rms * (grad_attended - normed * inner_mean)
    grad_low = grad_mixed.astype(jnp.bfloat16)
    local_adjoint = jnp.einsum("thd,the->hde", query_wide, grad_mixed, precision=highest)
    after_state = entering(local_adjoint, "ctx", add_states, zeros_state)
    adjoint_scores = jnp.einsum(
        "the,she->hts", grad_low, values, preferred_element_type=jnp.float32
    )
    adjoint_scores = jnp.where(causal_keep, adjoint_scores, 0.0).astype(jnp.bfloat16)
    grad_query = jnp.einsum(
        "hts,shd->thd", adjoint_scores, key_spiked, preferred_element_type=jnp.float32
    )
    grad_query = grad_query + jnp.einsum("the,hde->thd", grad_mixed, prior_state, precision=highest)
    grad_key = jnp.einsum(
        "hts,thd->shd", adjoint_scores, query_spiked, preferred_element_type=jnp.float32
    )
    grad_key = grad_key + jnp.einsum(
        "she,hde->shd", values.astype(jnp.float32), after_state, precision=highest
    )
    grad_value = jnp.einsum("hts,the->she", scores, grad_low, preferred_element_type=jnp.float32)
    grad_value = grad_value + jnp.einsum("shd,hde->she", key_wide, after_state, precision=highest)
    grad_proj = jnp.stack(
        [
            (grad_query * query_spikes.astype(jnp.float32)).astype(jnp.bfloat16),
            (grad_key * key_spikes.astype(jnp.float32)).astype(jnp.bfloat16),
            grad_value.astype(jnp.bfloat16),
        ],
        axis=0,
    ).reshape(3, block_rows, features)
    qkv_part = jnp.einsum("tm,ptc->mpc", gathered, grad_proj, preferred_element_type=jnp.float32)
    qkv_sum = lax.psum_scatter(
        qkv_part.astype(jnp.bfloat16), "ctx", scatter_dimension=0, tiled=True
    ).astype(jnp.float32)
    qkv_keep = lax.dynamic_slice_in_dim(qkv_blocks, ctx_place * slice_blocks, slice_blocks, 1)
    qkv_keep = jnp.broadcast_to(
        jnp.transpose(qkv_keep, (1, 0, 2)).astype(jnp.float32)[:, None, :, :, None],
        (slice_blocks, BLOCK, 3, col_blocks, BLOCK),
    ).reshape(slice_rows, 3, features)
    qkv_grad = qkv_sum * qkv_keep * norm_factor
    token_sum = lax.psum_scatter(
        masked_matmul_nt(grad_proj, qkv_planes, qkv_spread, jnp.bfloat16),
        "tp",
        scatter_dimension=0,
        tiled=True,
    ).astype(jnp.float32)
    token_grad = (cotangent.astype(jnp.float32) + token_sum).astype(jnp.bfloat16)
    return (layer_out, token_grad, qkv_grad, out_grad)


def solution(mesh):
    placed = (
        P(("ctx", "tp"), None),
        P("ctx", "tp"),
        P("ctx", "tp"),
        P(None, None, "tp"),
        P(None, None, "tp"),
        P("tp", None),
        P("tp", None),
        P(("ctx", "tp"), None),
    )
    return jax.shard_map(
        on_device,
        mesh=mesh,
        in_specs=placed,
        out_specs=(
            P(("ctx", "tp"), None),
            P(("ctx", "tp"), None),
            P("ctx", None, "tp"),
            P("tp", "ctx"),
        ),
        check_vma=False,
    )
```

```python
import math

import jax
import jax.numpy as jnp
from jax import lax
from jax.experimental import pallas as pl
from jax.experimental.pallas import tpu as pltpu
from jax.sharding import PartitionSpec as P

BLOCK = 128


EPSILON = 1e-05

def _tile(n, choices=(1024, 512, 256, 128)):
    for c in choices:
        if n % c == 0:
            return c
    return n


def _masked_tile(w_ref, m_ref, wm_ref):
    for g in range(w_ref.shape[0] // BLOCK):
        rows = slice(g * BLOCK, (g + 1) * BLOCK)
        wm_ref[rows, :] = w_ref[rows, :] * m_ref[g]


def _nn_kernel(a_ref, w_ref, m_ref, o_ref, acc_ref, wm_ref):
    k = pl.program_id(2)

    @pl.when(k == 0)
    def _():
        acc_ref[...] = jnp.zeros_like(acc_ref)

    _masked_tile(w_ref, m_ref, wm_ref)
    acc_ref[...] += jnp.dot(a_ref[...], wm_ref[...], preferred_element_type=jnp.float32)

    @pl.when(k == pl.num_programs(2) - 1)
    def _():
        o_ref[...] = acc_ref[...].astype(o_ref.dtype)


def _nt_kernel(a_ref, w_ref, m_ref, o_ref, acc_ref, wm_ref):
    p = pl.program_id(1)
    k = pl.program_id(2)

    @pl.when((p == 0) & (k == 0))
    def _():
        acc_ref[...] = jnp.zeros_like(acc_ref)

    _masked_tile(w_ref, m_ref, wm_ref)
    acc_ref[...] += lax.dot_general(
        a_ref[...], wm_ref[...], (((1,), (1,)), ((), ())), preferred_element_type=jnp.float32
    )

    @pl.when((p == pl.num_programs(1) - 1) & (k == pl.num_programs(2) - 1))
    def _():
        o_ref[...] = acc_ref[...].astype(o_ref.dtype)


def masked_matmul_nn(a, w, mask, out_dtype):
    m = a.shape[0]
    planes, rows, cols = w.shape
    tk, tn = _tile(rows), _tile(cols)
    grid = (planes, cols // tn, rows // tk)
    return pl.pallas_call(
        _nn_kernel,
        grid=grid,
        in_specs=[
            pl.BlockSpec((m, tk), lambda p, j, k: (0, k)),
            pl.BlockSpec((None, tk, tn), lambda p, j, k: (p, k, j)),
            pl.BlockSpec((None, tk // BLOCK, 1, tn), lambda p, j, k: (p, k, 0, j)),
        ],
        out_specs=pl.BlockSpec((None, m, tn), lambda p, j, k: (p, 0, j)),
        out_shape=jax.ShapeDtypeStruct((planes, m, cols), out_dtype),
        scratch_shapes=[pltpu.VMEM((m, tn), jnp.float32), pltpu.VMEM((tk, tn), w.dtype)],
        compiler_params=pltpu.CompilerParams(
            dimension_semantics=("parallel", "parallel", "arbitrary"),
            vmem_limit_bytes=48 * 1024 * 1024,
        ),
        cost_estimate=pl.CostEstimate(
            flops=2 * m * planes * rows * cols,
            bytes_accessed=a.size * 2 * planes * (cols // tn) + w.size * 2
            + m * planes * cols * jnp.dtype(out_dtype).itemsize,
            transcendentals=0,
        ),
    )(a, w, mask)


def masked_matmul_nt(a, w, mask, out_dtype):
    planes, m, _ = a.shape
    _, rows, cols = w.shape
    tr, tk = _tile(rows), _tile(cols)
    grid = (rows // tr, planes, cols // tk)
    return pl.pallas_call(
        _nt_kernel,
        grid=grid,
        in_specs=[
            pl.BlockSpec((None, m, tk), lambda i, p, k: (p, 0, k)),
            pl.BlockSpec((None, tr, tk), lambda i, p, k: (p, i, k)),
            pl.BlockSpec((None, tr // BLOCK, 1, tk), lambda i, p, k: (p, i, 0, k)),
        ],
        out_specs=pl.BlockSpec((m, tr), lambda i, p, k: (0, i)),
        out_shape=jax.ShapeDtypeStruct((m, rows), out_dtype),
        scratch_shapes=[pltpu.VMEM((m, tr), jnp.float32), pltpu.VMEM((tr, tk), w.dtype)],
        compiler_params=pltpu.CompilerParams(
            dimension_semantics=("parallel", "arbitrary", "arbitrary"),
            vmem_limit_bytes=48 * 1024 * 1024,
        ),
        cost_estimate=pl.CostEstimate(
            flops=2 * m * planes * rows * cols,
            bytes_accessed=a.size * 2 * (rows // tr) + w.size * 2
            + m * rows * jnp.dtype(out_dtype).itemsize,
            transcendentals=0,
        ),
    )(a, w, mask)


def ring_gather(value, axis):
    count = lax.axis_size(axis)
    place = lax.axis_index(axis)
    step = [(index, (index + 1) % count) for index in range(count)]
    pieces = [value]
    moving = value
    for _ in range(1, count):
        moving = lax.ppermute(moving, axis, step)
        pieces.append(moving)
    stacked = jnp.stack(pieces)
    order = (place - jnp.arange(count)) % count
    ordered = jnp.take(stacked, order, axis=0)
    return ordered.reshape((count * value.shape[0],) + value.shape[1:])


def ring_scatter(value, axis):
    count = lax.axis_size(axis)
    place = lax.axis_index(axis)
    step = [(index, (index + 1) % count) for index in range(count)]
    rows = value.shape[0] // count
    pieces = value.reshape((count, rows) + value.shape[1:])

    def piece(index):
        return lax.dynamic_index_in_dim(pieces, index % count, 0, False).astype(jnp.float32)

    running = piece(place + count - 1)
    for lap in range(1, count):
        arrived = lax.ppermute(running.astype(jnp.bfloat16), axis, step)
        running = arrived.astype(jnp.float32) + piece(place + 2 * count - 1 - lap)
    return running


def carried_in(value, axis, join, neutral):
    place = lax.axis_index(axis)
    gathered = lax.all_gather(value.astype(jnp.bfloat16), axis)
    state = jnp.zeros_like(value) + jnp.asarray(neutral, value.dtype)

    def carried_one(lap, state):
        return join(state, lax.dynamic_index_in_dim(gathered, lap, 0, False).astype(value.dtype))

    return lax.fori_loop(0, place, carried_one, state)


def entering(value, axis, join, neutral):
    count = lax.axis_size(axis)
    place = lax.axis_index(axis)
    ahead = count - 1 - place
    gathered = lax.all_gather(
        value.astype(jnp.bfloat16 if value.dtype == jnp.float32 else value.dtype), axis
    )
    state = jnp.zeros_like(value) + jnp.asarray(neutral, value.dtype)

    def entering_one(lap, state):
        source = count - 1 - lap
        return join(state, lax.dynamic_index_in_dim(gathered, source, 0, False).astype(value.dtype))

    return lax.fori_loop(0, ahead, entering_one, state)


def expand_blocks(blocks):
    row_blocks, col_blocks = blocks.shape
    spread = jnp.broadcast_to(
        blocks.astype(jnp.bfloat16)[:, None, :, None], (row_blocks, BLOCK, col_blocks, BLOCK)
    )
    return spread.reshape(row_blocks * BLOCK, col_blocks * BLOCK)


def qkv_keep_table(qkv_blocks):
    tables = [expand_blocks(qkv_blocks[projection]) for projection in range(3)]
    return jnp.stack(tables, axis=1)


def add_states(earlier, following):
    return earlier + following


def on_device(
    tokens, spike_query, spike_key, qkv_weight, qkv_blocks, out_weight, out_blocks, cotangent
):
    model_width = tokens.shape[1]
    block_rows = spike_query.shape[0]
    local_heads = spike_query.shape[1]
    features = qkv_weight.shape[2]
    head_width = features // local_heads
    row_blocks = model_width // BLOCK
    col_blocks = features // BLOCK
    highest = lax.Precision.HIGHEST
    qkv_planes = jnp.transpose(qkv_weight, (1, 0, 2))
    qkv_spread = jnp.broadcast_to(
        qkv_blocks.astype(jnp.bfloat16)[:, :, None, :, None],
        (3, row_blocks, 1, col_blocks, BLOCK),
    ).reshape(3, row_blocks, 1, features)
    out_planes = out_weight[None]
    out_spread = jnp.broadcast_to(
        out_blocks.astype(jnp.bfloat16)[None, :, None, :, None],
        (1, col_blocks, 1, row_blocks, BLOCK),
    ).reshape(1, col_blocks, 1, model_width)
    gathered = ring_gather(tokens, "tp")
    projected = masked_matmul_nn(gathered, qkv_planes, qkv_spread, jnp.bfloat16)
    projected, cotangent_late = lax.optimization_barrier((projected, cotangent))
    projected = projected.reshape(3, block_rows, local_heads, head_width)
    query_spikes = spike_query.astype(jnp.bfloat16)[:, :, None]
    key_spikes = spike_key.astype(jnp.bfloat16)[:, :, None]
    query_spiked = projected[0] * query_spikes
    key_spiked = projected[1] * key_spikes
    values = projected[2]
    query_wide = query_spiked.astype(jnp.float32)
    key_wide = key_spiked.astype(jnp.float32)
    local_state = jnp.einsum("shd,she->hde", key_spiked, values, preferred_element_type=jnp.float32)
    zeros_state = jnp.zeros_like(local_state)
    prior_state = carried_in(local_state, "ctx", add_states, zeros_state)
    positions = lax.iota(jnp.int32, block_rows)
    causal_keep = positions[:, None] >= positions[None, :]
    scores = jnp.einsum(
        "thd,shd->hts", query_spiked, key_spiked, preferred_element_type=jnp.float32
    )
    scores = jnp.where(causal_keep, scores, 0.0).astype(jnp.bfloat16)
    mixed_rows = jnp.einsum("hts,she->the", scores, values, preferred_element_type=jnp.float32)
    mixed_rows = mixed_rows + jnp.einsum("thd,hde->the", query_wide, prior_state, precision=highest)
    inv_rms = lax.rsqrt(jnp.mean(mixed_rows * mixed_rows, axis=-1, keepdims=True) + EPSILON)
    normed = mixed_rows * inv_rms
    attended = normed.astype(jnp.bfloat16).reshape(block_rows, features)
    head_part = masked_matmul_nn(attended, out_planes, out_spread, jnp.bfloat16)[0]
    grad_rows = ring_gather(cotangent_late, "tp")
    head_part, grad_rows = lax.optimization_barrier((head_part, grad_rows))
    head_sum = ring_scatter(head_part, "tp")
    ctx_count = lax.axis_size("ctx")
    ctx_place = lax.axis_index("ctx")
    slice_rows = model_width // ctx_count
    slice_blocks = slice_rows // BLOCK
    norm_factor = 1.0 / math.sqrt(block_rows * ctx_count)
    out_part = jnp.einsum("tm,tf->mf", grad_rows, attended, preferred_element_type=jnp.float32)
    out_sum = lax.psum_scatter(
        out_part.astype(jnp.bfloat16), "ctx", scatter_dimension=0, tiled=True
    ).astype(jnp.float32)
    out_keep = lax.dynamic_slice_in_dim(out_blocks, ctx_place * slice_blocks, slice_blocks, 1)
    out_keep = jnp.broadcast_to(
        jnp.transpose(out_keep).astype(jnp.float32)[:, None, :, None],
        (slice_blocks, BLOCK, col_blocks, BLOCK),
    ).reshape(slice_rows, features)
    out_grad = jnp.transpose(out_sum * out_keep * norm_factor)
    grad_attended = masked_matmul_nt(grad_rows[None], out_planes, out_spread, jnp.float32)
    grad_attended = grad_attended.reshape(block_rows, local_heads, head_width)
    inner_mean = jnp.mean(grad_attended * normed, axis=-1, keepdims=True)
    grad_mixed = inv_rms * (grad_attended - normed * inner_mean)
    grad_low = grad_mixed.astype(jnp.bfloat16)
    local_adjoint = jnp.einsum("thd,the->hde", query_wide, grad_mixed, precision=highest)
    after_state = entering(local_adjoint, "ctx", add_states, zeros_state)
    adjoint_scores = jnp.einsum(
        "the,she->hts", grad_low, values, preferred_element_type=jnp.float32
    )
    adjoint_scores = jnp.where(causal_keep, adjoint_scores, 0.0).astype(jnp.bfloat16)
    grad_query = jnp.einsum(
        "hts,shd->thd", adjoint_scores, key_spiked, preferred_element_type=jnp.float32
    )
    grad_query = grad_query + jnp.einsum("the,hde->thd", grad_mixed, prior_state, precision=highest)
    grad_key = jnp.einsum(
        "hts,thd->shd", adjoint_scores, query_spiked, preferred_element_type=jnp.float32
    )
    grad_key = grad_key + jnp.einsum(
        "she,hde->shd", values.astype(jnp.float32), after_state, precision=highest
    )
    grad_value = jnp.einsum("hts,the->she", scores, grad_low, preferred_element_type=jnp.float32)
    grad_value = grad_value + jnp.einsum("shd,hde->she", key_wide, after_state, precision=highest)
    grad_proj = jnp.stack(
        [
            (grad_query * query_spikes.astype(jnp.float32)).astype(jnp.bfloat16),
            (grad_key * key_spikes.astype(jnp.float32)).astype(jnp.bfloat16),
            grad_value.astype(jnp.bfloat16),
        ],
        axis=0,
    ).reshape(3, block_rows, features)
    qkv_part = jnp.einsum("tm,ptc->mpc", gathered, grad_proj, preferred_element_type=jnp.float32)
    qkv_sum = lax.psum_scatter(
        qkv_part.astype(jnp.bfloat16), "ctx", scatter_dimension=0, tiled=True
    ).astype(jnp.float32)
    qkv_keep = lax.dynamic_slice_in_dim(qkv_blocks, ctx_place * slice_blocks, slice_blocks, 1)
    qkv_keep = jnp.broadcast_to(
        jnp.transpose(qkv_keep, (1, 0, 2)).astype(jnp.float32)[:, None, :, :, None],
        (slice_blocks, BLOCK, 3, col_blocks, BLOCK),
    ).reshape(slice_rows, 3, features)
    qkv_grad = qkv_sum * qkv_keep * norm_factor
    grad_proj_late, head_sum = lax.optimization_barrier((grad_proj, head_sum))
    token_sum = ring_scatter(
        masked_matmul_nt(grad_proj_late, qkv_planes, qkv_spread, jnp.bfloat16), "tp"
    )
    layer_out = (tokens.astype(jnp.float32) + head_sum).astype(jnp.bfloat16)
    token_grad = (cotangent.astype(jnp.float32) + token_sum).astype(jnp.bfloat16)
    return (layer_out, token_grad, qkv_grad, out_grad)


def solution(mesh):
    placed = (
        P(("ctx", "tp"), None),
        P("ctx", "tp"),
        P("ctx", "tp"),
        P(None, None, "tp"),
        P(None, None, "tp"),
        P("tp", None),
        P("tp", None),
        P(("ctx", "tp"), None),
    )
    return jax.shard_map(
        on_device,
        mesh=mesh,
        in_specs=placed,
        out_specs=(
            P(("ctx", "tp"), None),
            P(("ctx", "tp"), None),
            P("ctx", None, "tp"),
            P("tp", "ctx"),
        ),
        check_vma=False,
    )
```

```python
import math

import jax
import jax.numpy as jnp
from jax import lax
from jax.experimental import pallas as pl
from jax.experimental.pallas import tpu as pltpu
from jax.sharding import PartitionSpec as P

BLOCK = 128


EPSILON = 1e-05

def _tile(n, choices=(1024, 512, 256, 128)):
    for c in choices:
        if n % c == 0:
            return c
    return n


def _masked_tile(w_ref, m_ref, wm_ref):
    for g in range(w_ref.shape[0] // BLOCK):
        rows = slice(g * BLOCK, (g + 1) * BLOCK)
        wm_ref[rows, :] = w_ref[rows, :] * m_ref[g]


def _nn_kernel(a_ref, w_ref, m_ref, o_ref, acc_ref, wm_ref):
    k = pl.program_id(2)

    @pl.when(k == 0)
    def _():
        acc_ref[...] = jnp.zeros_like(acc_ref)

    _masked_tile(w_ref, m_ref, wm_ref)
    acc_ref[...] += jnp.dot(a_ref[...], wm_ref[...], preferred_element_type=jnp.float32)

    @pl.when(k == pl.num_programs(2) - 1)
    def _():
        o_ref[...] = acc_ref[...].astype(o_ref.dtype)


def _nt_kernel(a_ref, w_ref, m_ref, o_ref, acc_ref, wm_ref):
    p = pl.program_id(1)
    k = pl.program_id(2)

    @pl.when((p == 0) & (k == 0))
    def _():
        acc_ref[...] = jnp.zeros_like(acc_ref)

    _masked_tile(w_ref, m_ref, wm_ref)
    acc_ref[...] += lax.dot_general(
        a_ref[...], wm_ref[...], (((1,), (1,)), ((), ())), preferred_element_type=jnp.float32
    )

    @pl.when((p == pl.num_programs(1) - 1) & (k == pl.num_programs(2) - 1))
    def _():
        o_ref[...] = acc_ref[...].astype(o_ref.dtype)


def masked_matmul_nn(a, w, mask, out_dtype):
    m = a.shape[0]
    planes, rows, cols = w.shape
    tk, tn = _tile(rows), _tile(cols)
    grid = (planes, cols // tn, rows // tk)
    return pl.pallas_call(
        _nn_kernel,
        grid=grid,
        in_specs=[
            pl.BlockSpec((m, tk), lambda p, j, k: (0, k)),
            pl.BlockSpec((None, tk, tn), lambda p, j, k: (p, k, j)),
            pl.BlockSpec((None, tk // BLOCK, 1, tn), lambda p, j, k: (p, k, 0, j)),
        ],
        out_specs=pl.BlockSpec((None, m, tn), lambda p, j, k: (p, 0, j)),
        out_shape=jax.ShapeDtypeStruct((planes, m, cols), out_dtype),
        scratch_shapes=[pltpu.VMEM((m, tn), jnp.float32), pltpu.VMEM((tk, tn), w.dtype)],
        compiler_params=pltpu.CompilerParams(
            dimension_semantics=("parallel", "parallel", "arbitrary"),
            vmem_limit_bytes=48 * 1024 * 1024,
        ),
        cost_estimate=pl.CostEstimate(
            flops=2 * m * planes * rows * cols,
            bytes_accessed=a.size * 2 * planes * (cols // tn) + w.size * 2
            + m * planes * cols * jnp.dtype(out_dtype).itemsize,
            transcendentals=0,
        ),
    )(a, w, mask)


def masked_matmul_nt(a, w, mask, out_dtype):
    planes, m, _ = a.shape
    _, rows, cols = w.shape
    tr, tk = _tile(rows), _tile(cols)
    grid = (rows // tr, planes, cols // tk)
    return pl.pallas_call(
        _nt_kernel,
        grid=grid,
        in_specs=[
            pl.BlockSpec((None, m, tk), lambda i, p, k: (p, 0, k)),
            pl.BlockSpec((None, tr, tk), lambda i, p, k: (p, i, k)),
            pl.BlockSpec((None, tr // BLOCK, 1, tk), lambda i, p, k: (p, i, 0, k)),
        ],
        out_specs=pl.BlockSpec((m, tr), lambda i, p, k: (0, i)),
        out_shape=jax.ShapeDtypeStruct((m, rows), out_dtype),
        scratch_shapes=[pltpu.VMEM((m, tr), jnp.float32), pltpu.VMEM((tr, tk), w.dtype)],
        compiler_params=pltpu.CompilerParams(
            dimension_semantics=("parallel", "arbitrary", "arbitrary"),
            vmem_limit_bytes=48 * 1024 * 1024,
        ),
        cost_estimate=pl.CostEstimate(
            flops=2 * m * planes * rows * cols,
            bytes_accessed=a.size * 2 * (rows // tr) + w.size * 2
            + m * rows * jnp.dtype(out_dtype).itemsize,
            transcendentals=0,
        ),
    )(a, w, mask)


def ring_gather(value, axis, work=None):
    count = lax.axis_size(axis)
    place = lax.axis_index(axis)
    step = [(index, (index + 1) % count) for index in range(count)]
    moving = value
    placed = jnp.zeros((count,) + value.shape, value.dtype)
    placed = lax.dynamic_update_index_in_dim(placed, value, place, 0)
    results = None
    if work is not None:
        done = work(value)
        results = jnp.zeros((done.shape[0], count) + done.shape[1:], done.dtype)
        results = lax.dynamic_update_index_in_dim(results, done, place, 1)
    for lap in range(1, count):
        moving = lax.ppermute(moving, axis, step)
        source = (place + count - lap) % count
        placed = lax.dynamic_update_index_in_dim(placed, moving, source, 0)
        if work is not None:
            results = lax.dynamic_update_index_in_dim(results, work(moving), source, 1)
    return placed, results


def ring_scatter(value, axis):
    count = lax.axis_size(axis)
    place = lax.axis_index(axis)
    step = [(index, (index + 1) % count) for index in range(count)]
    rows = value.shape[0] // count
    pieces = value.reshape((count, rows) + value.shape[1:])

    def piece(index):
        return lax.dynamic_index_in_dim(pieces, index % count, 0, False).astype(jnp.float32)

    running = piece(place + count - 1)
    for lap in range(1, count):
        arrived = lax.ppermute(running.astype(jnp.bfloat16), axis, step)
        running = arrived.astype(jnp.float32) + piece(place + 2 * count - 1 - lap)
    return running


def carried_in(value, axis, join, neutral):
    place = lax.axis_index(axis)
    gathered = lax.all_gather(value.astype(jnp.bfloat16), axis)
    state = jnp.zeros_like(value) + jnp.asarray(neutral, value.dtype)

    def carried_one(lap, state):
        return join(state, lax.dynamic_index_in_dim(gathered, lap, 0, False).astype(value.dtype))

    return lax.fori_loop(0, place, carried_one, state)


def entering(value, axis, join, neutral):
    count = lax.axis_size(axis)
    place = lax.axis_index(axis)
    ahead = count - 1 - place
    gathered = lax.all_gather(
        value.astype(jnp.bfloat16 if value.dtype == jnp.float32 else value.dtype), axis
    )
    state = jnp.zeros_like(value) + jnp.asarray(neutral, value.dtype)

    def entering_one(lap, state):
        source = count - 1 - lap
        return join(state, lax.dynamic_index_in_dim(gathered, source, 0, False).astype(value.dtype))

    return lax.fori_loop(0, ahead, entering_one, state)


def expand_blocks(blocks):
    row_blocks, col_blocks = blocks.shape
    spread = jnp.broadcast_to(
        blocks.astype(jnp.bfloat16)[:, None, :, None], (row_blocks, BLOCK, col_blocks, BLOCK)
    )
    return spread.reshape(row_blocks * BLOCK, col_blocks * BLOCK)


def qkv_keep_table(qkv_blocks):
    tables = [expand_blocks(qkv_blocks[projection]) for projection in range(3)]
    return jnp.stack(tables, axis=1)


def add_states(earlier, following):
    return earlier + following


def on_device(
    tokens, spike_query, spike_key, qkv_weight, qkv_blocks, out_weight, out_blocks, cotangent
):
    model_width = tokens.shape[1]
    block_rows = spike_query.shape[0]
    local_heads = spike_query.shape[1]
    features = qkv_weight.shape[2]
    head_width = features // local_heads
    row_blocks = model_width // BLOCK
    col_blocks = features // BLOCK
    highest = lax.Precision.HIGHEST
    qkv_planes = jnp.transpose(qkv_weight, (1, 0, 2))
    qkv_spread = jnp.broadcast_to(
        qkv_blocks.astype(jnp.bfloat16)[:, :, None, :, None],
        (3, row_blocks, 1, col_blocks, BLOCK),
    ).reshape(3, row_blocks, 1, features)
    out_planes = out_weight[None]
    out_spread = jnp.broadcast_to(
        out_blocks.astype(jnp.bfloat16)[None, :, None, :, None],
        (1, col_blocks, 1, row_blocks, BLOCK),
    ).reshape(1, col_blocks, 1, model_width)
    gathered, projected = ring_gather(
        tokens, "tp", lambda piece: masked_matmul_nn(piece, qkv_planes, qkv_spread, jnp.bfloat16)
    )
    gathered = gathered.reshape(block_rows, model_width)
    projected = projected.reshape(3, block_rows, features)
    projected, cotangent_late = lax.optimization_barrier((projected, cotangent))
    projected = projected.reshape(3, block_rows, local_heads, head_width)
    query_spikes = spike_query.astype(jnp.bfloat16)[:, :, None]
    key_spikes = spike_key.astype(jnp.bfloat16)[:, :, None]
    query_spiked = projected[0] * query_spikes
    key_spiked = projected[1] * key_spikes
    values = projected[2]
    query_wide = query_spiked.astype(jnp.float32)
    key_wide = key_spiked.astype(jnp.float32)
    local_state = jnp.einsum("shd,she->hde", key_spiked, values, preferred_element_type=jnp.float32)
    zeros_state = jnp.zeros_like(local_state)
    prior_state = carried_in(local_state, "ctx", add_states, zeros_state)
    positions = lax.iota(jnp.int32, block_rows)
    causal_keep = positions[:, None] >= positions[None, :]
    scores = jnp.einsum(
        "thd,shd->hts", query_spiked, key_spiked, preferred_element_type=jnp.float32
    )
    scores = jnp.where(causal_keep, scores, 0.0).astype(jnp.bfloat16)
    mixed_rows = jnp.einsum("hts,she->the", scores, values, preferred_element_type=jnp.float32)
    mixed_rows = mixed_rows + jnp.einsum("thd,hde->the", query_wide, prior_state, precision=highest)
    inv_rms = lax.rsqrt(jnp.mean(mixed_rows * mixed_rows, axis=-1, keepdims=True) + EPSILON)
    normed = mixed_rows * inv_rms
    attended = normed.astype(jnp.bfloat16).reshape(block_rows, features)
    head_part = masked_matmul_nn(attended, out_planes, out_spread, jnp.bfloat16)[0]
    grad_rows = ring_gather(cotangent_late, "tp")[0].reshape(block_rows, model_width)
    head_part, grad_rows = lax.optimization_barrier((head_part, grad_rows))
    head_sum = ring_scatter(head_part, "tp")
    ctx_count = lax.axis_size("ctx")
    ctx_place = lax.axis_index("ctx")
    slice_rows = model_width // ctx_count
    slice_blocks = slice_rows // BLOCK
    norm_factor = 1.0 / math.sqrt(block_rows * ctx_count)
    out_part = jnp.einsum("tm,tf->mf", grad_rows, attended, preferred_element_type=jnp.float32)
    out_sum = lax.psum_scatter(
        out_part.astype(jnp.bfloat16), "ctx", scatter_dimension=0, tiled=True
    ).astype(jnp.float32)
    out_keep = lax.dynamic_slice_in_dim(out_blocks, ctx_place * slice_blocks, slice_blocks, 1)
    out_keep = jnp.broadcast_to(
        jnp.transpose(out_keep).astype(jnp.float32)[:, None, :, None],
        (slice_blocks, BLOCK, col_blocks, BLOCK),
    ).reshape(slice_rows, features)
    out_grad = jnp.transpose(out_sum * out_keep * norm_factor)
    grad_attended = masked_matmul_nt(grad_rows[None], out_planes, out_spread, jnp.float32)
    grad_attended = grad_attended.reshape(block_rows, local_heads, head_width)
    inner_mean = jnp.mean(grad_attended * normed, axis=-1, keepdims=True)
    grad_mixed = inv_rms * (grad_attended - normed * inner_mean)
    grad_low = grad_mixed.astype(jnp.bfloat16)
    local_adjoint = jnp.einsum("thd,the->hde", query_wide, grad_mixed, precision=highest)
    after_state = entering(local_adjoint, "ctx", add_states, zeros_state)
    adjoint_scores = jnp.einsum(
        "the,she->hts", grad_low, values, preferred_element_type=jnp.float32
    )
    adjoint_scores = jnp.where(causal_keep, adjoint_scores, 0.0).astype(jnp.bfloat16)
    grad_query = jnp.einsum(
        "hts,shd->thd", adjoint_scores, key_spiked, preferred_element_type=jnp.float32
    )
    grad_query = grad_query + jnp.einsum("the,hde->thd", grad_mixed, prior_state, precision=highest)
    grad_key = jnp.einsum(
        "hts,thd->shd", adjoint_scores, query_spiked, preferred_element_type=jnp.float32
    )
    grad_key = grad_key + jnp.einsum(
        "she,hde->shd", values.astype(jnp.float32), after_state, precision=highest
    )
    grad_value = jnp.einsum("hts,the->she", scores, grad_low, preferred_element_type=jnp.float32)
    grad_value = grad_value + jnp.einsum("shd,hde->she", key_wide, after_state, precision=highest)
    grad_proj = jnp.stack(
        [
            (grad_query * query_spikes.astype(jnp.float32)).astype(jnp.bfloat16),
            (grad_key * key_spikes.astype(jnp.float32)).astype(jnp.bfloat16),
            grad_value.astype(jnp.bfloat16),
        ],
        axis=0,
    ).reshape(3, block_rows, features)
    qkv_part = jnp.einsum("tm,ptc->mpc", gathered, grad_proj, preferred_element_type=jnp.float32)
    qkv_sum = lax.psum_scatter(
        qkv_part.astype(jnp.bfloat16), "ctx", scatter_dimension=0, tiled=True
    ).astype(jnp.float32)
    qkv_keep = lax.dynamic_slice_in_dim(qkv_blocks, ctx_place * slice_blocks, slice_blocks, 1)
    qkv_keep = jnp.broadcast_to(
        jnp.transpose(qkv_keep, (1, 0, 2)).astype(jnp.float32)[:, None, :, :, None],
        (slice_blocks, BLOCK, 3, col_blocks, BLOCK),
    ).reshape(slice_rows, 3, features)
    qkv_grad = qkv_sum * qkv_keep * norm_factor
    grad_proj_late, head_sum = lax.optimization_barrier((grad_proj, head_sum))
    token_sum = ring_scatter(
        masked_matmul_nt(grad_proj_late, qkv_planes, qkv_spread, jnp.bfloat16), "tp"
    )
    layer_out = (tokens.astype(jnp.float32) + head_sum).astype(jnp.bfloat16)
    token_grad = (cotangent.astype(jnp.float32) + token_sum).astype(jnp.bfloat16)
    return (layer_out, token_grad, qkv_grad, out_grad)


def solution(mesh):
    placed = (
        P(("ctx", "tp"), None),
        P("ctx", "tp"),
        P("ctx", "tp"),
        P(None, None, "tp"),
        P(None, None, "tp"),
        P("tp", None),
        P("tp", None),
        P(("ctx", "tp"), None),
    )
    return jax.shard_map(
        on_device,
        mesh=mesh,
        in_specs=placed,
        out_specs=(
            P(("ctx", "tp"), None),
            P(("ctx", "tp"), None),
            P("ctx", None, "tp"),
            P("tp", "ctx"),
        ),
        check_vma=False,
    )
```

```python
import math

import jax
import jax.numpy as jnp
from jax import lax
from jax.experimental import pallas as pl
from jax.experimental.pallas import tpu as pltpu
from jax.sharding import PartitionSpec as P

BLOCK = 128


EPSILON = 1e-05

def _tile(n, choices=(1024, 512, 256, 128)):
    for c in choices:
        if n % c == 0:
            return c
    return n


def _masked_tile(w_ref, m_ref, wm_ref):
    for g in range(w_ref.shape[0] // BLOCK):
        rows = slice(g * BLOCK, (g + 1) * BLOCK)
        wm_ref[rows, :] = w_ref[rows, :] * m_ref[g]


def _nn_kernel(a_ref, w_ref, m_ref, o_ref, acc_ref, wm_ref):
    k = pl.program_id(2)

    @pl.when(k == 0)
    def _():
        acc_ref[...] = jnp.zeros_like(acc_ref)

    _masked_tile(w_ref, m_ref, wm_ref)
    acc_ref[...] += jnp.dot(a_ref[...], wm_ref[...], preferred_element_type=jnp.float32)

    @pl.when(k == pl.num_programs(2) - 1)
    def _():
        o_ref[...] = acc_ref[...].astype(o_ref.dtype)


def _nt_kernel(a_ref, w_ref, m_ref, o_ref, acc_ref, wm_ref):
    p = pl.program_id(1)
    k = pl.program_id(2)

    @pl.when((p == 0) & (k == 0))
    def _():
        acc_ref[...] = jnp.zeros_like(acc_ref)

    _masked_tile(w_ref, m_ref, wm_ref)
    acc_ref[...] += lax.dot_general(
        a_ref[...], wm_ref[...], (((1,), (1,)), ((), ())), preferred_element_type=jnp.float32
    )

    @pl.when((p == pl.num_programs(1) - 1) & (k == pl.num_programs(2) - 1))
    def _():
        o_ref[...] = acc_ref[...].astype(o_ref.dtype)


def masked_matmul_nn(a, w, mask, out_dtype):
    m = a.shape[0]
    planes, rows, cols = w.shape
    tk, tn = _tile(rows), _tile(cols)
    grid = (planes, cols // tn, rows // tk)
    return pl.pallas_call(
        _nn_kernel,
        grid=grid,
        in_specs=[
            pl.BlockSpec((m, tk), lambda p, j, k: (0, k)),
            pl.BlockSpec((None, tk, tn), lambda p, j, k: (p, k, j)),
            pl.BlockSpec((None, tk // BLOCK, 1, tn), lambda p, j, k: (p, k, 0, j)),
        ],
        out_specs=pl.BlockSpec((None, m, tn), lambda p, j, k: (p, 0, j)),
        out_shape=jax.ShapeDtypeStruct((planes, m, cols), out_dtype),
        scratch_shapes=[pltpu.VMEM((m, tn), jnp.float32), pltpu.VMEM((tk, tn), w.dtype)],
        compiler_params=pltpu.CompilerParams(
            dimension_semantics=("parallel", "parallel", "arbitrary"),
            vmem_limit_bytes=48 * 1024 * 1024,
        ),
        cost_estimate=pl.CostEstimate(
            flops=2 * m * planes * rows * cols,
            bytes_accessed=a.size * 2 * planes * (cols // tn) + w.size * 2
            + m * planes * cols * jnp.dtype(out_dtype).itemsize,
            transcendentals=0,
        ),
    )(a, w, mask)


def masked_matmul_nt(a, w, mask, out_dtype):
    planes, m, _ = a.shape
    _, rows, cols = w.shape
    tr, tk = _tile(rows), _tile(cols)
    grid = (rows // tr, planes, cols // tk)
    return pl.pallas_call(
        _nt_kernel,
        grid=grid,
        in_specs=[
            pl.BlockSpec((None, m, tk), lambda i, p, k: (p, 0, k)),
            pl.BlockSpec((None, tr, tk), lambda i, p, k: (p, i, k)),
            pl.BlockSpec((None, tr // BLOCK, 1, tk), lambda i, p, k: (p, i, 0, k)),
        ],
        out_specs=pl.BlockSpec((m, tr), lambda i, p, k: (0, i)),
        out_shape=jax.ShapeDtypeStruct((m, rows), out_dtype),
        scratch_shapes=[pltpu.VMEM((m, tr), jnp.float32), pltpu.VMEM((tr, tk), w.dtype)],
        compiler_params=pltpu.CompilerParams(
            dimension_semantics=("parallel", "arbitrary", "arbitrary"),
            vmem_limit_bytes=48 * 1024 * 1024,
        ),
        cost_estimate=pl.CostEstimate(
            flops=2 * m * planes * rows * cols,
            bytes_accessed=a.size * 2 * (rows // tr) + w.size * 2
            + m * rows * jnp.dtype(out_dtype).itemsize,
            transcendentals=0,
        ),
    )(a, w, mask)


def ring_gather(value, axis, work=None):
    count = lax.axis_size(axis)
    place = lax.axis_index(axis)
    step = [(index, (index + 1) % count) for index in range(count)]
    moving = value
    placed = jnp.zeros((count,) + value.shape, value.dtype)
    placed = lax.dynamic_update_index_in_dim(placed, value, place, 0)
    results = None
    if work is not None:
        done = work(value)
        results = jnp.zeros((done.shape[0], count) + done.shape[1:], done.dtype)
        results = lax.dynamic_update_index_in_dim(results, done, place, 1)
    for lap in range(1, count):
        moving = lax.ppermute(moving, axis, step)
        source = (place + count - lap) % count
        placed = lax.dynamic_update_index_in_dim(placed, moving, source, 0)
        if work is not None:
            results = lax.dynamic_update_index_in_dim(results, work(moving), source, 1)
    return placed, results


def ring_scatter(value, axis):
    count = lax.axis_size(axis)
    place = lax.axis_index(axis)
    step = [(index, (index + 1) % count) for index in range(count)]
    rows = value.shape[0] // count
    pieces = value.reshape((count, rows) + value.shape[1:])

    def piece(index):
        return lax.dynamic_index_in_dim(pieces, index % count, 0, False).astype(jnp.float32)

    running = piece(place + count - 1)
    for lap in range(1, count):
        arrived = lax.ppermute(running.astype(jnp.bfloat16), axis, step)
        running = arrived.astype(jnp.float32) + piece(place + 2 * count - 1 - lap)
    return running


class GatherRing:
    def __init__(self, value, axis):
        self.axis = axis
        self.count = lax.axis_size(axis)
        self.place = lax.axis_index(axis)
        self.step = [(index, (index + 1) % self.count) for index in range(self.count)]
        self.moving = value
        placed = jnp.zeros((self.count,) + value.shape, value.dtype)
        self.placed = lax.dynamic_update_index_in_dim(placed, value, self.place, 0)
        self.lap = 1

    def advance(self, tie=None):
        if self.lap >= self.count:
            return tie
        moved = lax.ppermute(self.moving, self.axis, self.step)
        if tie is not None:
            moved, tie = lax.optimization_barrier((moved, tie))
        source = (self.place + self.count - self.lap) % self.count
        self.placed = lax.dynamic_update_index_in_dim(self.placed, moved, source, 0)
        self.moving = moved
        self.lap += 1
        return tie

    def finish(self):
        while self.lap < self.count:
            self.advance()
        return self.placed


class ScatterRing:
    def __init__(self, value, axis):
        self.axis = axis
        self.count = lax.axis_size(axis)
        self.place = lax.axis_index(axis)
        self.step = [(index, (index + 1) % self.count) for index in range(self.count)]
        rows = value.shape[0] // self.count
        self.pieces = value.reshape((self.count, rows) + value.shape[1:])
        self.running = self.piece(self.place + self.count - 1)
        self.lap = 1

    def piece(self, index):
        return lax.dynamic_index_in_dim(
            self.pieces, index % self.count, 0, False
        ).astype(jnp.float32)

    def advance(self, tie=None):
        if self.lap >= self.count:
            return tie
        arrived = lax.ppermute(self.running.astype(jnp.bfloat16), self.axis, self.step)
        if tie is not None:
            arrived, tie = lax.optimization_barrier((arrived, tie))
        self.running = arrived.astype(jnp.float32) + self.piece(
            self.place + 2 * self.count - 1 - self.lap
        )
        self.lap += 1
        return tie

    def finish(self):
        while self.lap < self.count:
            self.advance()
        return self.running


def carried_in(value, axis, join, neutral):
    place = lax.axis_index(axis)
    gathered = lax.all_gather(value.astype(jnp.bfloat16), axis)
    state = jnp.zeros_like(value) + jnp.asarray(neutral, value.dtype)

    def carried_one(lap, state):
        return join(state, lax.dynamic_index_in_dim(gathered, lap, 0, False).astype(value.dtype))

    return lax.fori_loop(0, place, carried_one, state)


def entering(value, axis, join, neutral):
    count = lax.axis_size(axis)
    place = lax.axis_index(axis)
    ahead = count - 1 - place
    gathered = lax.all_gather(
        value.astype(jnp.bfloat16 if value.dtype == jnp.float32 else value.dtype), axis
    )
    state = jnp.zeros_like(value) + jnp.asarray(neutral, value.dtype)

    def entering_one(lap, state):
        source = count - 1 - lap
        return join(state, lax.dynamic_index_in_dim(gathered, source, 0, False).astype(value.dtype))

    return lax.fori_loop(0, ahead, entering_one, state)


def expand_blocks(blocks):
    row_blocks, col_blocks = blocks.shape
    spread = jnp.broadcast_to(
        blocks.astype(jnp.bfloat16)[:, None, :, None], (row_blocks, BLOCK, col_blocks, BLOCK)
    )
    return spread.reshape(row_blocks * BLOCK, col_blocks * BLOCK)


def qkv_keep_table(qkv_blocks):
    tables = [expand_blocks(qkv_blocks[projection]) for projection in range(3)]
    return jnp.stack(tables, axis=1)


def add_states(earlier, following):
    return earlier + following


def on_device(
    tokens, spike_query, spike_key, qkv_weight, qkv_blocks, out_weight, out_blocks, cotangent
):
    model_width = tokens.shape[1]
    block_rows = spike_query.shape[0]
    local_heads = spike_query.shape[1]
    features = qkv_weight.shape[2]
    head_width = features // local_heads
    row_blocks = model_width // BLOCK
    col_blocks = features // BLOCK
    highest = lax.Precision.HIGHEST
    qkv_planes = jnp.transpose(qkv_weight, (1, 0, 2))
    qkv_spread = jnp.broadcast_to(
        qkv_blocks.astype(jnp.bfloat16)[:, :, None, :, None],
        (3, row_blocks, 1, col_blocks, BLOCK),
    ).reshape(3, row_blocks, 1, features)
    out_planes = out_weight[None]
    out_spread = jnp.broadcast_to(
        out_blocks.astype(jnp.bfloat16)[None, :, None, :, None],
        (1, col_blocks, 1, row_blocks, BLOCK),
    ).reshape(1, col_blocks, 1, model_width)
    gathered, projected = ring_gather(
        tokens, "tp", lambda piece: masked_matmul_nn(piece, qkv_planes, qkv_spread, jnp.bfloat16)
    )
    gathered = gathered.reshape(block_rows, model_width)
    projected = projected.reshape(3, block_rows, features)
    projected, cotangent_late = lax.optimization_barrier((projected, cotangent))
    projected = projected.reshape(3, block_rows, local_heads, head_width)
    query_spikes = spike_query.astype(jnp.bfloat16)[:, :, None]
    key_spikes = spike_key.astype(jnp.bfloat16)[:, :, None]
    query_spiked = projected[0] * query_spikes
    key_spiked = projected[1] * key_spikes
    values = projected[2]
    query_wide = query_spiked.astype(jnp.float32)
    key_wide = key_spiked.astype(jnp.float32)
    local_state = jnp.einsum("shd,she->hde", key_spiked, values, preferred_element_type=jnp.float32)
    zeros_state = jnp.zeros_like(local_state)
    prior_state = carried_in(local_state, "ctx", add_states, zeros_state)
    positions = lax.iota(jnp.int32, block_rows)
    causal_keep = positions[:, None] >= positions[None, :]
    scores = jnp.einsum(
        "thd,shd->hts", query_spiked, key_spiked, preferred_element_type=jnp.float32
    )
    scores = jnp.where(causal_keep, scores, 0.0).astype(jnp.bfloat16)
    cotangent_ring = GatherRing(cotangent_late, "tp")
    scores = cotangent_ring.advance(scores)
    mixed_rows = jnp.einsum("hts,she->the", scores, values, preferred_element_type=jnp.float32)
    mixed_rows = mixed_rows + jnp.einsum("thd,hde->the", query_wide, prior_state, precision=highest)
    mixed_rows = cotangent_ring.advance(mixed_rows)
    inv_rms = lax.rsqrt(jnp.mean(mixed_rows * mixed_rows, axis=-1, keepdims=True) + EPSILON)
    normed = mixed_rows * inv_rms
    attended = normed.astype(jnp.bfloat16).reshape(block_rows, features)
    head_part = masked_matmul_nn(attended, out_planes, out_spread, jnp.bfloat16)[0]
    head_part = cotangent_ring.advance(head_part)
    grad_rows = cotangent_ring.finish().reshape(block_rows, model_width)
    head_part, grad_rows = lax.optimization_barrier((head_part, grad_rows))
    head_ring = ScatterRing(head_part, "tp")
    ctx_count = lax.axis_size("ctx")
    ctx_place = lax.axis_index("ctx")
    slice_rows = model_width // ctx_count
    slice_blocks = slice_rows // BLOCK
    norm_factor = 1.0 / math.sqrt(block_rows * ctx_count)
    out_part = jnp.einsum("tm,tf->mf", grad_rows, attended, preferred_element_type=jnp.float32)
    out_sum = lax.psum_scatter(
        out_part.astype(jnp.bfloat16), "ctx", scatter_dimension=0, tiled=True
    ).astype(jnp.float32)
    out_keep = lax.dynamic_slice_in_dim(out_blocks, ctx_place * slice_blocks, slice_blocks, 1)
    out_keep = jnp.broadcast_to(
        jnp.transpose(out_keep).astype(jnp.float32)[:, None, :, None],
        (slice_blocks, BLOCK, col_blocks, BLOCK),
    ).reshape(slice_rows, features)
    out_grad = jnp.transpose(out_sum * out_keep * norm_factor)
    grad_attended = masked_matmul_nt(grad_rows[None], out_planes, out_spread, jnp.float32)
    grad_attended = head_ring.advance(grad_attended)
    grad_attended = grad_attended.reshape(block_rows, local_heads, head_width)
    inner_mean = jnp.mean(grad_attended * normed, axis=-1, keepdims=True)
    grad_mixed = inv_rms * (grad_attended - normed * inner_mean)
    grad_low = grad_mixed.astype(jnp.bfloat16)
    local_adjoint = jnp.einsum("thd,the->hde", query_wide, grad_mixed, precision=highest)
    after_state = entering(local_adjoint, "ctx", add_states, zeros_state)
    adjoint_scores = jnp.einsum(
        "the,she->hts", grad_low, values, preferred_element_type=jnp.float32
    )
    adjoint_scores = jnp.where(causal_keep, adjoint_scores, 0.0).astype(jnp.bfloat16)
    adjoint_scores = head_ring.advance(adjoint_scores)
    grad_query = jnp.einsum(
        "hts,shd->thd", adjoint_scores, key_spiked, preferred_element_type=jnp.float32
    )
    grad_query = grad_query + jnp.einsum("the,hde->thd", grad_mixed, prior_state, precision=highest)
    grad_key = jnp.einsum(
        "hts,thd->shd", adjoint_scores, query_spiked, preferred_element_type=jnp.float32
    )
    grad_key = grad_key + jnp.einsum(
        "she,hde->shd", values.astype(jnp.float32), after_state, precision=highest
    )
    grad_value = jnp.einsum("hts,the->she", scores, grad_low, preferred_element_type=jnp.float32)
    grad_value = grad_value + jnp.einsum("shd,hde->she", key_wide, after_state, precision=highest)
    grad_proj = jnp.stack(
        [
            (grad_query * query_spikes.astype(jnp.float32)).astype(jnp.bfloat16),
            (grad_key * key_spikes.astype(jnp.float32)).astype(jnp.bfloat16),
            grad_value.astype(jnp.bfloat16),
        ],
        axis=0,
    ).reshape(3, block_rows, features)
    qkv_part = jnp.einsum("tm,ptc->mpc", gathered, grad_proj, preferred_element_type=jnp.float32)
    qkv_sum = lax.psum_scatter(
        qkv_part.astype(jnp.bfloat16), "ctx", scatter_dimension=0, tiled=True
    ).astype(jnp.float32)
    qkv_keep = lax.dynamic_slice_in_dim(qkv_blocks, ctx_place * slice_blocks, slice_blocks, 1)
    qkv_keep = jnp.broadcast_to(
        jnp.transpose(qkv_keep, (1, 0, 2)).astype(jnp.float32)[:, None, :, :, None],
        (slice_blocks, BLOCK, 3, col_blocks, BLOCK),
    ).reshape(slice_rows, 3, features)
    qkv_grad = qkv_sum * qkv_keep * norm_factor
    grad_proj = head_ring.advance(grad_proj)
    head_sum = head_ring.finish()
    grad_proj_late, head_sum = lax.optimization_barrier((grad_proj, head_sum))
    token_sum = ring_scatter(
        masked_matmul_nt(grad_proj_late, qkv_planes, qkv_spread, jnp.bfloat16), "tp"
    )
    layer_out = (tokens.astype(jnp.float32) + head_sum).astype(jnp.bfloat16)
    token_grad = (cotangent.astype(jnp.float32) + token_sum).astype(jnp.bfloat16)
    return (layer_out, token_grad, qkv_grad, out_grad)


def solution(mesh):
    placed = (
        P(("ctx", "tp"), None),
        P("ctx", "tp"),
        P("ctx", "tp"),
        P(None, None, "tp"),
        P(None, None, "tp"),
        P("tp", None),
        P("tp", None),
        P(("ctx", "tp"), None),
    )
    return jax.shard_map(
        on_device,
        mesh=mesh,
        in_specs=placed,
        out_specs=(
            P(("ctx", "tp"), None),
            P(("ctx", "tp"), None),
            P("ctx", None, "tp"),
            P("tp", "ctx"),
        ),
        check_vma=False,
    )
```

```python
import math

import jax
import jax.numpy as jnp
from jax import lax
from jax.experimental import pallas as pl
from jax.experimental.pallas import tpu as pltpu
from jax.sharding import PartitionSpec as P

BLOCK = 128


EPSILON = 1e-05
CTX = ("chip", "core")

def _tile(n, choices=(1024, 512, 256, 128)):
    for c in choices:
        if n % c == 0:
            return c
    return n


def _masked_tile(w_ref, m_ref, wm_ref):
    for g in range(w_ref.shape[0] // BLOCK):
        rows = slice(g * BLOCK, (g + 1) * BLOCK)
        wm_ref[rows, :] = w_ref[rows, :] * m_ref[g]


def _nn_kernel(a_ref, w_ref, m_ref, o_ref, acc_ref, wm_ref):
    k = pl.program_id(2)

    @pl.when(k == 0)
    def _():
        acc_ref[...] = jnp.zeros_like(acc_ref)

    _masked_tile(w_ref, m_ref, wm_ref)
    acc_ref[...] += jnp.dot(a_ref[...], wm_ref[...], preferred_element_type=jnp.float32)

    @pl.when(k == pl.num_programs(2) - 1)
    def _():
        o_ref[...] = acc_ref[...].astype(o_ref.dtype)


def _nt_kernel(a_ref, w_ref, m_ref, o_ref, acc_ref, wm_ref):
    p = pl.program_id(1)
    k = pl.program_id(2)

    @pl.when((p == 0) & (k == 0))
    def _():
        acc_ref[...] = jnp.zeros_like(acc_ref)

    _masked_tile(w_ref, m_ref, wm_ref)
    acc_ref[...] += lax.dot_general(
        a_ref[...], wm_ref[...], (((1,), (1,)), ((), ())), preferred_element_type=jnp.float32
    )

    @pl.when((p == pl.num_programs(1) - 1) & (k == pl.num_programs(2) - 1))
    def _():
        o_ref[...] = acc_ref[...].astype(o_ref.dtype)


def masked_matmul_nn(a, w, mask, out_dtype):
    m = a.shape[0]
    planes, rows, cols = w.shape
    tk, tn = _tile(rows), _tile(cols)
    grid = (planes, cols // tn, rows // tk)
    return pl.pallas_call(
        _nn_kernel,
        grid=grid,
        in_specs=[
            pl.BlockSpec((m, tk), lambda p, j, k: (0, k)),
            pl.BlockSpec((None, tk, tn), lambda p, j, k: (p, k, j)),
            pl.BlockSpec((None, tk // BLOCK, 1, tn), lambda p, j, k: (p, k, 0, j)),
        ],
        out_specs=pl.BlockSpec((None, m, tn), lambda p, j, k: (p, 0, j)),
        out_shape=jax.ShapeDtypeStruct((planes, m, cols), out_dtype),
        scratch_shapes=[pltpu.VMEM((m, tn), jnp.float32), pltpu.VMEM((tk, tn), w.dtype)],
        compiler_params=pltpu.CompilerParams(
            dimension_semantics=("parallel", "parallel", "arbitrary"),
            vmem_limit_bytes=48 * 1024 * 1024,
        ),
        cost_estimate=pl.CostEstimate(
            flops=2 * m * planes * rows * cols,
            bytes_accessed=a.size * 2 * planes * (cols // tn) + w.size * 2
            + m * planes * cols * jnp.dtype(out_dtype).itemsize,
            transcendentals=0,
        ),
    )(a, w, mask)


def masked_matmul_nt(a, w, mask, out_dtype):
    planes, m, _ = a.shape
    _, rows, cols = w.shape
    tr, tk = _tile(rows), _tile(cols)
    grid = (rows // tr, planes, cols // tk)
    return pl.pallas_call(
        _nt_kernel,
        grid=grid,
        in_specs=[
            pl.BlockSpec((None, m, tk), lambda i, p, k: (p, 0, k)),
            pl.BlockSpec((None, tr, tk), lambda i, p, k: (p, i, k)),
            pl.BlockSpec((None, tr // BLOCK, 1, tk), lambda i, p, k: (p, i, 0, k)),
        ],
        out_specs=pl.BlockSpec((m, tr), lambda i, p, k: (0, i)),
        out_shape=jax.ShapeDtypeStruct((m, rows), out_dtype),
        scratch_shapes=[pltpu.VMEM((m, tr), jnp.float32), pltpu.VMEM((tr, tk), w.dtype)],
        compiler_params=pltpu.CompilerParams(
            dimension_semantics=("parallel", "arbitrary", "arbitrary"),
            vmem_limit_bytes=48 * 1024 * 1024,
        ),
        cost_estimate=pl.CostEstimate(
            flops=2 * m * planes * rows * cols,
            bytes_accessed=a.size * 2 * (rows // tr) + w.size * 2
            + m * rows * jnp.dtype(out_dtype).itemsize,
            transcendentals=0,
        ),
    )(a, w, mask)


def ring_gather(value, axis, work=None):
    count = lax.axis_size(axis)
    place = lax.axis_index(axis)
    step = [(index, (index + 1) % count) for index in range(count)]
    moving = value
    placed = jnp.zeros((count,) + value.shape, value.dtype)
    placed = lax.dynamic_update_index_in_dim(placed, value, place, 0)
    results = None
    if work is not None:
        done = work(value)
        results = jnp.zeros((done.shape[0], count) + done.shape[1:], done.dtype)
        results = lax.dynamic_update_index_in_dim(results, done, place, 1)
    for lap in range(1, count):
        moving = lax.ppermute(moving, axis, step)
        source = (place + count - lap) % count
        placed = lax.dynamic_update_index_in_dim(placed, moving, source, 0)
        if work is not None:
            results = lax.dynamic_update_index_in_dim(results, work(moving), source, 1)
    return placed, results


def ring_scatter(value, axis):
    count = lax.axis_size(axis)
    place = lax.axis_index(axis)
    step = [(index, (index + 1) % count) for index in range(count)]
    rows = value.shape[0] // count
    pieces = value.reshape((count, rows) + value.shape[1:])

    def piece(index):
        return lax.dynamic_index_in_dim(pieces, index % count, 0, False).astype(jnp.float32)

    running = piece(place + count - 1)
    for lap in range(1, count):
        arrived = lax.ppermute(running.astype(jnp.bfloat16), axis, step)
        running = arrived.astype(jnp.float32) + piece(place + 2 * count - 1 - lap)
    return running


class GatherRing:
    def __init__(self, value, axis):
        self.axis = axis
        self.count = lax.axis_size(axis)
        self.place = lax.axis_index(axis)
        self.step = [(index, (index + 1) % self.count) for index in range(self.count)]
        self.moving = value
        placed = jnp.zeros((self.count,) + value.shape, value.dtype)
        self.placed = lax.dynamic_update_index_in_dim(placed, value, self.place, 0)
        self.lap = 1

    def advance(self, tie=None):
        if self.lap >= self.count:
            return tie
        moved = lax.ppermute(self.moving, self.axis, self.step)
        if tie is not None:
            moved, tie = lax.optimization_barrier((moved, tie))
        source = (self.place + self.count - self.lap) % self.count
        self.placed = lax.dynamic_update_index_in_dim(self.placed, moved, source, 0)
        self.moving = moved
        self.lap += 1
        return tie

    def finish(self):
        while self.lap < self.count:
            self.advance()
        return self.placed


class ScatterRing:
    def __init__(self, value, axis):
        self.axis = axis
        self.count = lax.axis_size(axis)
        self.place = lax.axis_index(axis)
        self.step = [(index, (index + 1) % self.count) for index in range(self.count)]
        rows = value.shape[0] // self.count
        self.pieces = value.reshape((self.count, rows) + value.shape[1:])
        self.running = self.piece(self.place + self.count - 1)
        self.lap = 1

    def piece(self, index):
        return lax.dynamic_index_in_dim(
            self.pieces, index % self.count, 0, False
        ).astype(jnp.float32)

    def advance(self, tie=None):
        if self.lap >= self.count:
            return tie
        arrived = lax.ppermute(self.running.astype(jnp.bfloat16), self.axis, self.step)
        if tie is not None:
            arrived, tie = lax.optimization_barrier((arrived, tie))
        self.running = arrived.astype(jnp.float32) + self.piece(
            self.place + 2 * self.count - 1 - self.lap
        )
        self.lap += 1
        return tie

    def finish(self):
        while self.lap < self.count:
            self.advance()
        return self.running


def chip_scatter(value):
    chips = lax.axis_size("chip")
    core = lax.axis_index("core")
    halves = value.reshape((chips, 2, value.shape[0] // (2 * chips)) + value.shape[1:])
    kept = lax.dynamic_index_in_dim(halves, core, 1, False)
    given = lax.dynamic_index_in_dim(halves, 1 - core, 1, False)
    swap = [(0, 1), (1, 0)]
    arrived = lax.ppermute(given.astype(jnp.bfloat16), "core", swap)
    joined = (kept.astype(jnp.float32) + arrived.astype(jnp.float32)).astype(jnp.bfloat16)
    joined = joined.reshape((chips * joined.shape[1],) + joined.shape[2:])
    return lax.psum_scatter(joined, "chip", scatter_dimension=0, tiled=True).astype(jnp.float32)


def carried_in(value, axis, join, neutral):
    place = lax.axis_index(axis)
    gathered = lax.all_gather(value.astype(jnp.bfloat16), axis)
    state = jnp.zeros_like(value) + jnp.asarray(neutral, value.dtype)

    def carried_one(lap, state):
        return join(state, lax.dynamic_index_in_dim(gathered, lap, 0, False).astype(value.dtype))

    return lax.fori_loop(0, place, carried_one, state)


def entering(value, axis, join, neutral):
    count = lax.axis_size(axis)
    place = lax.axis_index(axis)
    ahead = count - 1 - place
    gathered = lax.all_gather(
        value.astype(jnp.bfloat16 if value.dtype == jnp.float32 else value.dtype), axis
    )
    state = jnp.zeros_like(value) + jnp.asarray(neutral, value.dtype)

    def entering_one(lap, state):
        source = count - 1 - lap
        return join(state, lax.dynamic_index_in_dim(gathered, source, 0, False).astype(value.dtype))

    return lax.fori_loop(0, ahead, entering_one, state)


def expand_blocks(blocks):
    row_blocks, col_blocks = blocks.shape
    spread = jnp.broadcast_to(
        blocks.astype(jnp.bfloat16)[:, None, :, None], (row_blocks, BLOCK, col_blocks, BLOCK)
    )
    return spread.reshape(row_blocks * BLOCK, col_blocks * BLOCK)


def qkv_keep_table(qkv_blocks):
    tables = [expand_blocks(qkv_blocks[projection]) for projection in range(3)]
    return jnp.stack(tables, axis=1)


def add_states(earlier, following):
    return earlier + following


def on_device(
    tokens, spike_query, spike_key, qkv_weight, qkv_blocks, out_weight, out_blocks, cotangent
):
    model_width = tokens.shape[1]
    block_rows = spike_query.shape[0]
    local_heads = spike_query.shape[1]
    features = qkv_weight.shape[2]
    head_width = features // local_heads
    row_blocks = model_width // BLOCK
    col_blocks = features // BLOCK
    highest = lax.Precision.HIGHEST
    qkv_planes = jnp.transpose(qkv_weight, (1, 0, 2))
    qkv_spread = jnp.broadcast_to(
        qkv_blocks.astype(jnp.bfloat16)[:, :, None, :, None],
        (3, row_blocks, 1, col_blocks, BLOCK),
    ).reshape(3, row_blocks, 1, features)
    out_planes = out_weight[None]
    out_spread = jnp.broadcast_to(
        out_blocks.astype(jnp.bfloat16)[None, :, None, :, None],
        (1, col_blocks, 1, row_blocks, BLOCK),
    ).reshape(1, col_blocks, 1, model_width)
    gathered, projected = ring_gather(
        tokens, "tp", lambda piece: masked_matmul_nn(piece, qkv_planes, qkv_spread, jnp.bfloat16)
    )
    gathered = gathered.reshape(block_rows, model_width)
    projected = projected.reshape(3, block_rows, features)
    projected, cotangent_late = lax.optimization_barrier((projected, cotangent))
    projected = projected.reshape(3, block_rows, local_heads, head_width)
    query_spikes = spike_query.astype(jnp.bfloat16)[:, :, None]
    key_spikes = spike_key.astype(jnp.bfloat16)[:, :, None]
    query_spiked = projected[0] * query_spikes
    key_spiked = projected[1] * key_spikes
    values = projected[2]
    query_wide = query_spiked.astype(jnp.float32)
    key_wide = key_spiked.astype(jnp.float32)
    local_state = jnp.einsum("shd,she->hde", key_spiked, values, preferred_element_type=jnp.float32)
    zeros_state = jnp.zeros_like(local_state)
    prior_state = carried_in(local_state, CTX, add_states, zeros_state)
    positions = lax.iota(jnp.int32, block_rows)
    causal_keep = positions[:, None] >= positions[None, :]
    scores = jnp.einsum(
        "thd,shd->hts", query_spiked, key_spiked, preferred_element_type=jnp.float32
    )
    scores = jnp.where(causal_keep, scores, 0.0).astype(jnp.bfloat16)
    cotangent_ring = GatherRing(cotangent_late, "tp")
    scores = cotangent_ring.advance(scores)
    mixed_rows = jnp.einsum("hts,she->the", scores, values, preferred_element_type=jnp.float32)
    mixed_rows = mixed_rows + jnp.einsum("thd,hde->the", query_wide, prior_state, precision=highest)
    mixed_rows = cotangent_ring.advance(mixed_rows)
    inv_rms = lax.rsqrt(jnp.mean(mixed_rows * mixed_rows, axis=-1, keepdims=True) + EPSILON)
    normed = mixed_rows * inv_rms
    attended = normed.astype(jnp.bfloat16).reshape(block_rows, features)
    head_part = masked_matmul_nn(attended, out_planes, out_spread, jnp.bfloat16)[0]
    head_part = cotangent_ring.advance(head_part)
    grad_rows = cotangent_ring.finish().reshape(block_rows, model_width)
    head_part, grad_rows = lax.optimization_barrier((head_part, grad_rows))
    head_ring = ScatterRing(head_part, "tp")
    ctx_count = lax.axis_size(CTX)
    ctx_place = lax.axis_index(CTX)
    slice_rows = model_width // ctx_count
    slice_blocks = slice_rows // BLOCK
    norm_factor = 1.0 / math.sqrt(block_rows * ctx_count)
    out_part = jnp.einsum("tm,tf->mf", grad_rows, attended, preferred_element_type=jnp.float32)
    out_sum = chip_scatter(out_part)
    out_keep = lax.dynamic_slice_in_dim(out_blocks, ctx_place * slice_blocks, slice_blocks, 1)
    out_keep = jnp.broadcast_to(
        jnp.transpose(out_keep).astype(jnp.float32)[:, None, :, None],
        (slice_blocks, BLOCK, col_blocks, BLOCK),
    ).reshape(slice_rows, features)
    out_grad = jnp.transpose(out_sum * out_keep * norm_factor)
    grad_attended = masked_matmul_nt(grad_rows[None], out_planes, out_spread, jnp.float32)
    grad_attended = head_ring.advance(grad_attended)
    grad_attended = grad_attended.reshape(block_rows, local_heads, head_width)
    inner_mean = jnp.mean(grad_attended * normed, axis=-1, keepdims=True)
    grad_mixed = inv_rms * (grad_attended - normed * inner_mean)
    grad_low = grad_mixed.astype(jnp.bfloat16)
    local_adjoint = jnp.einsum("thd,the->hde", query_wide, grad_mixed, precision=highest)
    after_state = entering(local_adjoint, CTX, add_states, zeros_state)
    adjoint_scores = jnp.einsum(
        "the,she->hts", grad_low, values, preferred_element_type=jnp.float32
    )
    adjoint_scores = jnp.where(causal_keep, adjoint_scores, 0.0).astype(jnp.bfloat16)
    adjoint_scores = head_ring.advance(adjoint_scores)
    grad_query = jnp.einsum(
        "hts,shd->thd", adjoint_scores, key_spiked, preferred_element_type=jnp.float32
    )
    grad_query = grad_query + jnp.einsum("the,hde->thd", grad_mixed, prior_state, precision=highest)
    grad_key = jnp.einsum(
        "hts,thd->shd", adjoint_scores, query_spiked, preferred_element_type=jnp.float32
    )
    grad_key = grad_key + jnp.einsum(
        "she,hde->shd", values.astype(jnp.float32), after_state, precision=highest
    )
    grad_value = jnp.einsum("hts,the->she", scores, grad_low, preferred_element_type=jnp.float32)
    grad_value = grad_value + jnp.einsum("shd,hde->she", key_wide, after_state, precision=highest)
    grad_proj = jnp.stack(
        [
            (grad_query * query_spikes.astype(jnp.float32)).astype(jnp.bfloat16),
            (grad_key * key_spikes.astype(jnp.float32)).astype(jnp.bfloat16),
            grad_value.astype(jnp.bfloat16),
        ],
        axis=0,
    ).reshape(3, block_rows, features)
    qkv_part = jnp.einsum("tm,ptc->mpc", gathered, grad_proj, preferred_element_type=jnp.float32)
    qkv_sum = chip_scatter(qkv_part)
    qkv_keep = lax.dynamic_slice_in_dim(qkv_blocks, ctx_place * slice_blocks, slice_blocks, 1)
    qkv_keep = jnp.broadcast_to(
        jnp.transpose(qkv_keep, (1, 0, 2)).astype(jnp.float32)[:, None, :, :, None],
        (slice_blocks, BLOCK, 3, col_blocks, BLOCK),
    ).reshape(slice_rows, 3, features)
    qkv_grad = qkv_sum * qkv_keep * norm_factor
    grad_proj = head_ring.advance(grad_proj)
    head_sum = head_ring.finish()
    grad_proj_late, head_sum = lax.optimization_barrier((grad_proj, head_sum))
    token_sum = ring_scatter(
        masked_matmul_nt(grad_proj_late, qkv_planes, qkv_spread, jnp.bfloat16), "tp"
    )
    layer_out = (tokens.astype(jnp.float32) + head_sum).astype(jnp.bfloat16)
    token_grad = (cotangent.astype(jnp.float32) + token_sum).astype(jnp.bfloat16)
    return (layer_out, token_grad, qkv_grad, out_grad)


def solution(mesh):
    ctx_count, tp_count = mesh.devices.shape
    split = jax.sharding.Mesh(
        mesh.devices.reshape(ctx_count // 2, 2, tp_count), ("chip", "core", "tp")
    )
    placed = (
        P((*CTX, "tp"), None),
        P(CTX, "tp"),
        P(CTX, "tp"),
        P(None, None, "tp"),
        P(None, None, "tp"),
        P("tp", None),
        P("tp", None),
        P((*CTX, "tp"), None),
    )
    return jax.shard_map(
        on_device,
        mesh=split,
        in_specs=placed,
        out_specs=(
            P((*CTX, "tp"), None),
            P((*CTX, "tp"), None),
            P(CTX, None, "tp"),
            P("tp", CTX),
        ),
        check_vma=False,
    )
```

```python
import math

import jax
import jax.numpy as jnp
from jax import lax
from jax.experimental import pallas as pl
from jax.experimental.pallas import tpu as pltpu
from jax.sharding import PartitionSpec as P

BLOCK = 128


EPSILON = 1e-05

def _tile(n, choices=(1024, 512, 256, 128)):
    for c in choices:
        if n % c == 0:
            return c
    return n


def _masked_tile(w_ref, m_ref, wm_ref):
    for g in range(w_ref.shape[0] // BLOCK):
        rows = slice(g * BLOCK, (g + 1) * BLOCK)
        wm_ref[rows, :] = w_ref[rows, :] * m_ref[g]


def _nn_kernel(a_ref, w_ref, m_ref, o_ref, acc_ref, wm_ref):
    k = pl.program_id(2)

    @pl.when(k == 0)
    def _():
        acc_ref[...] = jnp.zeros_like(acc_ref)

    _masked_tile(w_ref, m_ref, wm_ref)
    acc_ref[...] += jnp.dot(a_ref[...], wm_ref[...], preferred_element_type=jnp.float32)

    @pl.when(k == pl.num_programs(2) - 1)
    def _():
        o_ref[...] = acc_ref[...].astype(o_ref.dtype)


def _nt_kernel(a_ref, w_ref, m_ref, o_ref, acc_ref, wm_ref):
    p = pl.program_id(1)
    k = pl.program_id(2)

    @pl.when((p == 0) & (k == 0))
    def _():
        acc_ref[...] = jnp.zeros_like(acc_ref)

    _masked_tile(w_ref, m_ref, wm_ref)
    acc_ref[...] += lax.dot_general(
        a_ref[...], wm_ref[...], (((1,), (1,)), ((), ())), preferred_element_type=jnp.float32
    )

    @pl.when((p == pl.num_programs(1) - 1) & (k == pl.num_programs(2) - 1))
    def _():
        o_ref[...] = acc_ref[...].astype(o_ref.dtype)


def masked_matmul_nn(a, w, mask, out_dtype):
    m = a.shape[0]
    planes, rows, cols = w.shape
    tk, tn = _tile(rows), _tile(cols)
    grid = (planes, cols // tn, rows // tk)
    return pl.pallas_call(
        _nn_kernel,
        grid=grid,
        in_specs=[
            pl.BlockSpec((m, tk), lambda p, j, k: (0, k)),
            pl.BlockSpec((None, tk, tn), lambda p, j, k: (p, k, j)),
            pl.BlockSpec((None, tk // BLOCK, 1, tn), lambda p, j, k: (p, k, 0, j)),
        ],
        out_specs=pl.BlockSpec((None, m, tn), lambda p, j, k: (p, 0, j)),
        out_shape=jax.ShapeDtypeStruct((planes, m, cols), out_dtype),
        scratch_shapes=[pltpu.VMEM((m, tn), jnp.float32), pltpu.VMEM((tk, tn), w.dtype)],
        compiler_params=pltpu.CompilerParams(
            dimension_semantics=("parallel", "parallel", "arbitrary"),
            vmem_limit_bytes=48 * 1024 * 1024,
        ),
        cost_estimate=pl.CostEstimate(
            flops=2 * m * planes * rows * cols,
            bytes_accessed=a.size * 2 * planes * (cols // tn) + w.size * 2
            + m * planes * cols * jnp.dtype(out_dtype).itemsize,
            transcendentals=0,
        ),
    )(a, w, mask)


def masked_matmul_nt(a, w, mask, out_dtype):
    planes, m, _ = a.shape
    _, rows, cols = w.shape
    tr, tk = _tile(rows), _tile(cols)
    grid = (rows // tr, planes, cols // tk)
    return pl.pallas_call(
        _nt_kernel,
        grid=grid,
        in_specs=[
            pl.BlockSpec((None, m, tk), lambda i, p, k: (p, 0, k)),
            pl.BlockSpec((None, tr, tk), lambda i, p, k: (p, i, k)),
            pl.BlockSpec((None, tr // BLOCK, 1, tk), lambda i, p, k: (p, i, 0, k)),
        ],
        out_specs=pl.BlockSpec((m, tr), lambda i, p, k: (0, i)),
        out_shape=jax.ShapeDtypeStruct((m, rows), out_dtype),
        scratch_shapes=[pltpu.VMEM((m, tr), jnp.float32), pltpu.VMEM((tr, tk), w.dtype)],
        compiler_params=pltpu.CompilerParams(
            dimension_semantics=("parallel", "arbitrary", "arbitrary"),
            vmem_limit_bytes=48 * 1024 * 1024,
        ),
        cost_estimate=pl.CostEstimate(
            flops=2 * m * planes * rows * cols,
            bytes_accessed=a.size * 2 * (rows // tr) + w.size * 2
            + m * rows * jnp.dtype(out_dtype).itemsize,
            transcendentals=0,
        ),
    )(a, w, mask)


def ring_gather(value, axis, work=None):
    count = lax.axis_size(axis)
    place = lax.axis_index(axis)
    step = [(index, (index + 1) % count) for index in range(count)]
    moving = value
    placed = jnp.zeros((count,) + value.shape, value.dtype)
    placed = lax.dynamic_update_index_in_dim(placed, value, place, 0)
    results = None
    if work is not None:
        done = work(value)
        results = jnp.zeros((done.shape[0], count) + done.shape[1:], done.dtype)
        results = lax.dynamic_update_index_in_dim(results, done, place, 1)
    for lap in range(1, count):
        moving = lax.ppermute(moving, axis, step)
        source = (place + count - lap) % count
        placed = lax.dynamic_update_index_in_dim(placed, moving, source, 0)
        if work is not None:
            results = lax.dynamic_update_index_in_dim(results, work(moving), source, 1)
    return placed, results


def ring_scatter(value, axis):
    count = lax.axis_size(axis)
    place = lax.axis_index(axis)
    step = [(index, (index + 1) % count) for index in range(count)]
    rows = value.shape[0] // count
    pieces = value.reshape((count, rows) + value.shape[1:])

    def piece(index):
        return lax.dynamic_index_in_dim(pieces, index % count, 0, False).astype(jnp.float32)

    running = piece(place + count - 1)
    for lap in range(1, count):
        arrived = lax.ppermute(running.astype(jnp.bfloat16), axis, step)
        running = arrived.astype(jnp.float32) + piece(place + 2 * count - 1 - lap)
    return running


class GatherRing:
    def __init__(self, value, axis):
        self.axis = axis
        self.count = lax.axis_size(axis)
        self.place = lax.axis_index(axis)
        self.step = [(index, (index + 1) % self.count) for index in range(self.count)]
        self.moving = value
        placed = jnp.zeros((self.count,) + value.shape, value.dtype)
        self.placed = lax.dynamic_update_index_in_dim(placed, value, self.place, 0)
        self.lap = 1

    def advance(self, tie=None):
        if self.lap >= self.count:
            return tie
        moved = lax.ppermute(self.moving, self.axis, self.step)
        if tie is not None:
            moved, tie = lax.optimization_barrier((moved, tie))
        source = (self.place + self.count - self.lap) % self.count
        self.placed = lax.dynamic_update_index_in_dim(self.placed, moved, source, 0)
        self.moving = moved
        self.lap += 1
        return tie

    def finish(self):
        while self.lap < self.count:
            self.advance()
        return self.placed


class ScatterRing:
    def __init__(self, value, axis):
        self.axis = axis
        self.count = lax.axis_size(axis)
        self.place = lax.axis_index(axis)
        self.step = [(index, (index + 1) % self.count) for index in range(self.count)]
        rows = value.shape[0] // self.count
        self.pieces = value.reshape((self.count, rows) + value.shape[1:])
        self.running = self.piece(self.place + self.count - 1)
        self.lap = 1

    def piece(self, index):
        return lax.dynamic_index_in_dim(
            self.pieces, index % self.count, 0, False
        ).astype(jnp.float32)

    def advance(self, tie=None):
        if self.lap >= self.count:
            return tie
        arrived = lax.ppermute(self.running.astype(jnp.bfloat16), self.axis, self.step)
        if tie is not None:
            arrived, tie = lax.optimization_barrier((arrived, tie))
        self.running = arrived.astype(jnp.float32) + self.piece(
            self.place + 2 * self.count - 1 - self.lap
        )
        self.lap += 1
        return tie

    def finish(self):
        while self.lap < self.count:
            self.advance()
        return self.running


def carried_in(value, axis, join, neutral):
    place = lax.axis_index(axis)
    gathered = lax.all_gather(value.astype(jnp.bfloat16), axis)
    state = jnp.zeros_like(value) + jnp.asarray(neutral, value.dtype)

    def carried_one(lap, state):
        return join(state, lax.dynamic_index_in_dim(gathered, lap, 0, False).astype(value.dtype))

    return lax.fori_loop(0, place, carried_one, state)


def entering(value, axis, join, neutral):
    count = lax.axis_size(axis)
    place = lax.axis_index(axis)
    ahead = count - 1 - place
    gathered = lax.all_gather(
        value.astype(jnp.bfloat16 if value.dtype == jnp.float32 else value.dtype), axis
    )
    state = jnp.zeros_like(value) + jnp.asarray(neutral, value.dtype)

    def entering_one(lap, state):
        source = count - 1 - lap
        return join(state, lax.dynamic_index_in_dim(gathered, source, 0, False).astype(value.dtype))

    return lax.fori_loop(0, ahead, entering_one, state)


def expand_blocks(blocks):
    row_blocks, col_blocks = blocks.shape
    spread = jnp.broadcast_to(
        blocks.astype(jnp.bfloat16)[:, None, :, None], (row_blocks, BLOCK, col_blocks, BLOCK)
    )
    return spread.reshape(row_blocks * BLOCK, col_blocks * BLOCK)


def qkv_keep_table(qkv_blocks):
    tables = [expand_blocks(qkv_blocks[projection]) for projection in range(3)]
    return jnp.stack(tables, axis=1)


def add_states(earlier, following):
    return earlier + following


def on_device(
    tokens, spike_query, spike_key, qkv_weight, qkv_blocks, out_weight, out_blocks, cotangent
):
    model_width = tokens.shape[1]
    block_rows = spike_query.shape[0]
    local_heads = spike_query.shape[1]
    features = qkv_weight.shape[2]
    head_width = features // local_heads
    row_blocks = model_width // BLOCK
    col_blocks = features // BLOCK
    highest = lax.Precision.HIGHEST
    qkv_planes = jnp.transpose(qkv_weight, (1, 0, 2))
    qkv_spread = jnp.broadcast_to(
        qkv_blocks.astype(jnp.bfloat16)[:, :, None, :, None],
        (3, row_blocks, 1, col_blocks, BLOCK),
    ).reshape(3, row_blocks, 1, features)
    out_planes = out_weight[None]
    out_spread = jnp.broadcast_to(
        out_blocks.astype(jnp.bfloat16)[None, :, None, :, None],
        (1, col_blocks, 1, row_blocks, BLOCK),
    ).reshape(1, col_blocks, 1, model_width)
    gathered, projected = ring_gather(
        tokens, "tp", lambda piece: masked_matmul_nn(piece, qkv_planes, qkv_spread, jnp.bfloat16)
    )
    gathered = gathered.reshape(block_rows, model_width)
    projected = projected.reshape(3, block_rows, features)
    projected, cotangent_late = lax.optimization_barrier((projected, cotangent))
    projected = projected.reshape(3, block_rows, local_heads, head_width)
    query_spikes = spike_query.astype(jnp.bfloat16)[:, :, None]
    key_spikes = spike_key.astype(jnp.bfloat16)[:, :, None]
    query_spiked = projected[0] * query_spikes
    key_spiked = projected[1] * key_spikes
    values = projected[2]
    query_wide = query_spiked.astype(jnp.float32)
    key_wide = key_spiked.astype(jnp.float32)
    local_state = jnp.einsum("shd,she->hde", key_spiked, values, preferred_element_type=jnp.float32)
    zeros_state = jnp.zeros_like(local_state)
    prior_state = carried_in(local_state, "ctx", add_states, zeros_state)
    positions = lax.iota(jnp.int32, block_rows)
    causal_keep = positions[:, None] >= positions[None, :]
    scores = jnp.einsum(
        "thd,shd->hts", query_spiked, key_spiked, preferred_element_type=jnp.float32
    )
    scores = jnp.where(causal_keep, scores, 0.0).astype(jnp.bfloat16)
    cotangent_ring = GatherRing(cotangent_late, "tp")
    scores = cotangent_ring.advance(scores)
    mixed_rows = jnp.einsum("hts,she->the", scores, values, preferred_element_type=jnp.float32)
    mixed_rows = mixed_rows + jnp.einsum("thd,hde->the", query_wide, prior_state, precision=highest)
    mixed_rows = cotangent_ring.advance(mixed_rows)
    inv_rms = lax.rsqrt(jnp.mean(mixed_rows * mixed_rows, axis=-1, keepdims=True) + EPSILON)
    normed = mixed_rows * inv_rms
    attended = normed.astype(jnp.bfloat16).reshape(block_rows, features)
    head_part = masked_matmul_nn(attended, out_planes, out_spread, jnp.bfloat16)[0]
    head_part = cotangent_ring.advance(head_part)
    grad_rows = cotangent_ring.finish().reshape(block_rows, model_width)
    head_part, grad_rows = lax.optimization_barrier((head_part, grad_rows))
    head_ring = ScatterRing(head_part, "tp")
    ctx_count = lax.axis_size("ctx")
    ctx_place = lax.axis_index("ctx")
    slice_rows = model_width // ctx_count
    slice_blocks = slice_rows // BLOCK
    norm_factor = 1.0 / math.sqrt(block_rows * ctx_count)
    out_part = jnp.einsum("tm,tf->mf", grad_rows, attended, preferred_element_type=jnp.float32)
    out_sum = lax.psum_scatter(
        out_part.astype(jnp.bfloat16), "ctx", scatter_dimension=0, tiled=True
    ).astype(jnp.float32)
    out_keep = lax.dynamic_slice_in_dim(out_blocks, ctx_place * slice_blocks, slice_blocks, 1)
    out_keep = jnp.broadcast_to(
        jnp.transpose(out_keep).astype(jnp.float32)[:, None, :, None],
        (slice_blocks, BLOCK, col_blocks, BLOCK),
    ).reshape(slice_rows, features)
    out_grad = jnp.transpose(out_sum * out_keep * norm_factor)
    grad_attended = masked_matmul_nt(grad_rows[None], out_planes, out_spread, jnp.float32)
    grad_attended = grad_attended.reshape(block_rows, local_heads, head_width)
    inner_mean = jnp.mean(grad_attended * normed, axis=-1, keepdims=True)
    grad_mixed = inv_rms * (grad_attended - normed * inner_mean)
    grad_low = grad_mixed.astype(jnp.bfloat16)
    local_adjoint = jnp.einsum("thd,the->hde", query_wide, grad_mixed, precision=highest)
    after_state = entering(local_adjoint, "ctx", add_states, zeros_state)
    adjoint_scores = jnp.einsum(
        "the,she->hts", grad_low, values, preferred_element_type=jnp.float32
    )
    adjoint_scores = jnp.where(causal_keep, adjoint_scores, 0.0).astype(jnp.bfloat16)
    adjoint_scores = head_ring.advance(adjoint_scores)
    grad_query = jnp.einsum(
        "hts,shd->thd", adjoint_scores, key_spiked, preferred_element_type=jnp.float32
    )
    grad_query = grad_query + jnp.einsum("the,hde->thd", grad_mixed, prior_state, precision=highest)
    grad_key = jnp.einsum(
        "hts,thd->shd", adjoint_scores, query_spiked, preferred_element_type=jnp.float32
    )
    grad_key = grad_key + jnp.einsum(
        "she,hde->shd", values.astype(jnp.float32), after_state, precision=highest
    )
    grad_value = jnp.einsum("hts,the->she", scores, grad_low, preferred_element_type=jnp.float32)
    grad_value = grad_value + jnp.einsum("shd,hde->she", key_wide, after_state, precision=highest)
    grad_proj = jnp.stack(
        [
            (grad_query * query_spikes.astype(jnp.float32)).astype(jnp.bfloat16),
            (grad_key * key_spikes.astype(jnp.float32)).astype(jnp.bfloat16),
            grad_value.astype(jnp.bfloat16),
        ],
        axis=0,
    ).reshape(3, block_rows, features)
    qkv_part = jnp.einsum("tm,ptc->mpc", gathered, grad_proj, preferred_element_type=jnp.float32)
    qkv_sum = lax.psum_scatter(
        qkv_part.astype(jnp.bfloat16), "ctx", scatter_dimension=0, tiled=True
    ).astype(jnp.float32)
    qkv_keep = lax.dynamic_slice_in_dim(qkv_blocks, ctx_place * slice_blocks, slice_blocks, 1)
    qkv_keep = jnp.broadcast_to(
        jnp.transpose(qkv_keep, (1, 0, 2)).astype(jnp.float32)[:, None, :, :, None],
        (slice_blocks, BLOCK, 3, col_blocks, BLOCK),
    ).reshape(slice_rows, 3, features)
    qkv_grad = qkv_sum * qkv_keep * norm_factor
    grad_proj = head_ring.advance(grad_proj)
    grad_proj_late = grad_proj
    token_sum = ring_scatter(
        masked_matmul_nt(grad_proj_late, qkv_planes, qkv_spread, jnp.bfloat16), "tp"
    )
    head_sum = head_ring.finish()
    layer_out = (tokens.astype(jnp.float32) + head_sum).astype(jnp.bfloat16)
    token_grad = (cotangent.astype(jnp.float32) + token_sum).astype(jnp.bfloat16)
    return (layer_out, token_grad, qkv_grad, out_grad)


def solution(mesh):
    placed = (
        P(("ctx", "tp"), None),
        P("ctx", "tp"),
        P("ctx", "tp"),
        P(None, None, "tp"),
        P(None, None, "tp"),
        P("tp", None),
        P("tp", None),
        P(("ctx", "tp"), None),
    )
    return jax.shard_map(
        on_device,
        mesh=mesh,
        in_specs=placed,
        out_specs=(
            P(("ctx", "tp"), None),
            P(("ctx", "tp"), None),
            P("ctx", None, "tp"),
            P("tp", "ctx"),
        ),
        check_vma=False,
    )
```

```python
import math

import jax
import jax.numpy as jnp
from jax import lax
from jax.experimental import pallas as pl
from jax.experimental.pallas import tpu as pltpu
from jax.sharding import PartitionSpec as P

BLOCK = 128


EPSILON = 1e-05

def _tile(n, choices=(1024, 512, 256, 128)):
    for c in choices:
        if n % c == 0:
            return c
    return n


def _masked_tile(w_ref, m_ref, wm_ref):
    for g in range(w_ref.shape[0] // BLOCK):
        rows = slice(g * BLOCK, (g + 1) * BLOCK)
        wm_ref[rows, :] = w_ref[rows, :] * m_ref[g]


def _nn_kernel(a_ref, w_ref, m_ref, o_ref, acc_ref, wm_ref):
    k = pl.program_id(2)

    @pl.when(k == 0)
    def _():
        acc_ref[...] = jnp.zeros_like(acc_ref)

    _masked_tile(w_ref, m_ref, wm_ref)
    acc_ref[...] += jnp.dot(a_ref[...], wm_ref[...], preferred_element_type=jnp.float32)

    @pl.when(k == pl.num_programs(2) - 1)
    def _():
        o_ref[...] = acc_ref[...].astype(o_ref.dtype)


def _nt_kernel(a_ref, w_ref, m_ref, o_ref, acc_ref, wm_ref):
    p = pl.program_id(1)
    k = pl.program_id(2)

    @pl.when((p == 0) & (k == 0))
    def _():
        acc_ref[...] = jnp.zeros_like(acc_ref)

    _masked_tile(w_ref, m_ref, wm_ref)
    acc_ref[...] += lax.dot_general(
        a_ref[...], wm_ref[...], (((1,), (1,)), ((), ())), preferred_element_type=jnp.float32
    )

    @pl.when((p == pl.num_programs(1) - 1) & (k == pl.num_programs(2) - 1))
    def _():
        o_ref[...] = acc_ref[...].astype(o_ref.dtype)


def masked_matmul_nn(a, w, mask, out_dtype):
    m = a.shape[0]
    planes, rows, cols = w.shape
    tk, tn = _tile(rows), _tile(cols)
    grid = (planes, cols // tn, rows // tk)
    return pl.pallas_call(
        _nn_kernel,
        grid=grid,
        in_specs=[
            pl.BlockSpec((m, tk), lambda p, j, k: (0, k)),
            pl.BlockSpec((None, tk, tn), lambda p, j, k: (p, k, j)),
            pl.BlockSpec((None, tk // BLOCK, 1, tn), lambda p, j, k: (p, k, 0, j)),
        ],
        out_specs=pl.BlockSpec((None, m, tn), lambda p, j, k: (p, 0, j)),
        out_shape=jax.ShapeDtypeStruct((planes, m, cols), out_dtype),
        scratch_shapes=[pltpu.VMEM((m, tn), jnp.float32), pltpu.VMEM((tk, tn), w.dtype)],
        compiler_params=pltpu.CompilerParams(
            dimension_semantics=("parallel", "parallel", "arbitrary"),
            vmem_limit_bytes=48 * 1024 * 1024,
        ),
        cost_estimate=pl.CostEstimate(
            flops=2 * m * planes * rows * cols,
            bytes_accessed=a.size * 2 * planes * (cols // tn) + w.size * 2
            + m * planes * cols * jnp.dtype(out_dtype).itemsize,
            transcendentals=0,
        ),
    )(a, w, mask)


def masked_matmul_nt(a, w, mask, out_dtype):
    planes, m, _ = a.shape
    _, rows, cols = w.shape
    tr, tk = _tile(rows), _tile(cols)
    grid = (rows // tr, planes, cols // tk)
    return pl.pallas_call(
        _nt_kernel,
        grid=grid,
        in_specs=[
            pl.BlockSpec((None, m, tk), lambda i, p, k: (p, 0, k)),
            pl.BlockSpec((None, tr, tk), lambda i, p, k: (p, i, k)),
            pl.BlockSpec((None, tr // BLOCK, 1, tk), lambda i, p, k: (p, i, 0, k)),
        ],
        out_specs=pl.BlockSpec((m, tr), lambda i, p, k: (0, i)),
        out_shape=jax.ShapeDtypeStruct((m, rows), out_dtype),
        scratch_shapes=[pltpu.VMEM((m, tr), jnp.float32), pltpu.VMEM((tr, tk), w.dtype)],
        compiler_params=pltpu.CompilerParams(
            dimension_semantics=("parallel", "arbitrary", "arbitrary"),
            vmem_limit_bytes=48 * 1024 * 1024,
        ),
        cost_estimate=pl.CostEstimate(
            flops=2 * m * planes * rows * cols,
            bytes_accessed=a.size * 2 * (rows // tr) + w.size * 2
            + m * rows * jnp.dtype(out_dtype).itemsize,
            transcendentals=0,
        ),
    )(a, w, mask)


def ring_gather(value, axis, work=None):
    count = lax.axis_size(axis)
    place = lax.axis_index(axis)
    step = [(index, (index + 1) % count) for index in range(count)]
    moving = value
    placed = jnp.zeros((count,) + value.shape, value.dtype)
    placed = lax.dynamic_update_index_in_dim(placed, value, place, 0)
    results = None
    if work is not None:
        done = work(value)
        results = jnp.zeros((done.shape[0], count) + done.shape[1:], done.dtype)
        results = lax.dynamic_update_index_in_dim(results, done, place, 1)
    for lap in range(1, count):
        moving = lax.ppermute(moving, axis, step)
        source = (place + count - lap) % count
        placed = lax.dynamic_update_index_in_dim(placed, moving, source, 0)
        if work is not None:
            results = lax.dynamic_update_index_in_dim(results, work(moving), source, 1)
    return placed, results


def ring_scatter(value, axis):
    count = lax.axis_size(axis)
    place = lax.axis_index(axis)
    step = [(index, (index + 1) % count) for index in range(count)]
    rows = value.shape[0] // count
    pieces = value.reshape((count, rows) + value.shape[1:])

    def piece(index):
        return lax.dynamic_index_in_dim(pieces, index % count, 0, False).astype(jnp.float32)

    running = piece(place + count - 1)
    for lap in range(1, count):
        arrived = lax.ppermute(running.astype(jnp.bfloat16), axis, step)
        running = arrived.astype(jnp.float32) + piece(place + 2 * count - 1 - lap)
    return running


class GatherRing:
    def __init__(self, value, axis):
        self.axis = axis
        self.count = lax.axis_size(axis)
        self.place = lax.axis_index(axis)
        self.step = [(index, (index + 1) % self.count) for index in range(self.count)]
        self.moving = value
        placed = jnp.zeros((self.count,) + value.shape, value.dtype)
        self.placed = lax.dynamic_update_index_in_dim(placed, value, self.place, 0)
        self.lap = 1

    def advance(self, tie=None):
        if self.lap >= self.count:
            return tie
        moved = lax.ppermute(self.moving, self.axis, self.step)
        if tie is not None:
            moved, tie = lax.optimization_barrier((moved, tie))
        source = (self.place + self.count - self.lap) % self.count
        self.placed = lax.dynamic_update_index_in_dim(self.placed, moved, source, 0)
        self.moving = moved
        self.lap += 1
        return tie

    def finish(self):
        while self.lap < self.count:
            self.advance()
        return self.placed


class ScatterRing:
    def __init__(self, value, axis):
        self.axis = axis
        self.count = lax.axis_size(axis)
        self.place = lax.axis_index(axis)
        self.step = [(index, (index + 1) % self.count) for index in range(self.count)]
        rows = value.shape[0] // self.count
        self.pieces = value.reshape((self.count, rows) + value.shape[1:])
        self.running = self.piece(self.place + self.count - 1)
        self.lap = 1

    def piece(self, index):
        return lax.dynamic_index_in_dim(
            self.pieces, index % self.count, 0, False
        ).astype(jnp.float32)

    def advance(self, tie=None):
        if self.lap >= self.count:
            return tie
        arrived = lax.ppermute(self.running.astype(jnp.bfloat16), self.axis, self.step)
        if tie is not None:
            arrived, tie = lax.optimization_barrier((arrived, tie))
        self.running = arrived.astype(jnp.float32) + self.piece(
            self.place + 2 * self.count - 1 - self.lap
        )
        self.lap += 1
        return tie

    def finish(self):
        while self.lap < self.count:
            self.advance()
        return self.running


def carried_in(value, axis, join, neutral):
    place = lax.axis_index(axis)
    gathered = lax.all_gather(value.astype(jnp.bfloat16), axis)
    state = jnp.zeros_like(value) + jnp.asarray(neutral, value.dtype)

    def carried_one(lap, state):
        return join(state, lax.dynamic_index_in_dim(gathered, lap, 0, False).astype(value.dtype))

    return lax.fori_loop(0, place, carried_one, state)


def entering(value, axis, join, neutral):
    count = lax.axis_size(axis)
    place = lax.axis_index(axis)
    ahead = count - 1 - place
    gathered = lax.all_gather(
        value.astype(jnp.bfloat16 if value.dtype == jnp.float32 else value.dtype), axis
    )
    state = jnp.zeros_like(value) + jnp.asarray(neutral, value.dtype)

    def entering_one(lap, state):
        source = count - 1 - lap
        return join(state, lax.dynamic_index_in_dim(gathered, source, 0, False).astype(value.dtype))

    return lax.fori_loop(0, ahead, entering_one, state)


def expand_blocks(blocks):
    row_blocks, col_blocks = blocks.shape
    spread = jnp.broadcast_to(
        blocks.astype(jnp.bfloat16)[:, None, :, None], (row_blocks, BLOCK, col_blocks, BLOCK)
    )
    return spread.reshape(row_blocks * BLOCK, col_blocks * BLOCK)


def qkv_keep_table(qkv_blocks):
    tables = [expand_blocks(qkv_blocks[projection]) for projection in range(3)]
    return jnp.stack(tables, axis=1)


def add_states(earlier, following):
    return earlier + following


def on_device(
    tokens, spike_query, spike_key, qkv_weight, qkv_blocks, out_weight, out_blocks, cotangent
):
    model_width = tokens.shape[1]
    block_rows = spike_query.shape[0]
    local_heads = spike_query.shape[1]
    features = qkv_weight.shape[2]
    head_width = features // local_heads
    row_blocks = model_width // BLOCK
    col_blocks = features // BLOCK
    highest = lax.Precision.HIGHEST
    qkv_planes = jnp.transpose(qkv_weight, (1, 0, 2))
    qkv_spread = jnp.broadcast_to(
        qkv_blocks.astype(jnp.bfloat16)[:, :, None, :, None],
        (3, row_blocks, 1, col_blocks, BLOCK),
    ).reshape(3, row_blocks, 1, features)
    out_planes = out_weight[None]
    out_spread = jnp.broadcast_to(
        out_blocks.astype(jnp.bfloat16)[None, :, None, :, None],
        (1, col_blocks, 1, row_blocks, BLOCK),
    ).reshape(1, col_blocks, 1, model_width)
    gathered, projected = ring_gather(
        tokens, "tp", lambda piece: masked_matmul_nn(piece, qkv_planes, qkv_spread, jnp.bfloat16)
    )
    gathered = gathered.reshape(block_rows, model_width)
    projected = projected.reshape(3, block_rows, features)
    projected, cotangent_late = lax.optimization_barrier((projected, cotangent))
    projected = projected.reshape(3, block_rows, local_heads, head_width)
    query_spikes = spike_query.astype(jnp.bfloat16)[:, :, None]
    key_spikes = spike_key.astype(jnp.bfloat16)[:, :, None]
    query_spiked = projected[0] * query_spikes
    key_spiked = projected[1] * key_spikes
    values = projected[2]
    query_wide = query_spiked.astype(jnp.float32)
    key_wide = key_spiked.astype(jnp.float32)
    local_state = jnp.einsum("shd,she->hde", key_spiked, values, preferred_element_type=jnp.float32)
    zeros_state = jnp.zeros_like(local_state)
    prior_state = carried_in(local_state, "ctx", add_states, zeros_state)
    positions = lax.iota(jnp.int32, block_rows)
    causal_keep = positions[:, None] >= positions[None, :]
    scores = jnp.einsum(
        "thd,shd->hts", query_spiked, key_spiked, preferred_element_type=jnp.float32
    )
    scores = jnp.where(causal_keep, scores, 0.0).astype(jnp.bfloat16)
    cotangent_ring = GatherRing(cotangent_late, "tp")
    scores = cotangent_ring.advance(scores)
    mixed_rows = jnp.einsum("hts,she->the", scores, values, preferred_element_type=jnp.float32)
    mixed_rows = mixed_rows + jnp.einsum("thd,hde->the", query_wide, prior_state, precision=highest)
    mixed_rows = cotangent_ring.advance(mixed_rows)
    inv_rms = lax.rsqrt(jnp.mean(mixed_rows * mixed_rows, axis=-1, keepdims=True) + EPSILON)
    normed = mixed_rows * inv_rms
    attended = normed.astype(jnp.bfloat16).reshape(block_rows, features)
    head_part = masked_matmul_nn(attended, out_planes, out_spread, jnp.bfloat16)[0]
    head_part = cotangent_ring.advance(head_part)
    grad_rows = cotangent_ring.finish().reshape(block_rows, model_width)
    head_part, grad_rows = lax.optimization_barrier((head_part, grad_rows))
    head_ring = ScatterRing(head_part, "tp")
    ctx_count = lax.axis_size("ctx")
    ctx_place = lax.axis_index("ctx")
    slice_rows = model_width // ctx_count
    slice_blocks = slice_rows // BLOCK
    norm_factor = 1.0 / math.sqrt(block_rows * ctx_count)
    out_part = jnp.einsum("tm,tf->mf", grad_rows, attended, preferred_element_type=jnp.float32)
    out_sum = lax.psum_scatter(
        out_part.astype(jnp.bfloat16), "ctx", scatter_dimension=0, tiled=True
    ).astype(jnp.float32)
    out_keep = lax.dynamic_slice_in_dim(out_blocks, ctx_place * slice_blocks, slice_blocks, 1)
    out_keep = jnp.broadcast_to(
        jnp.transpose(out_keep).astype(jnp.float32)[:, None, :, None],
        (slice_blocks, BLOCK, col_blocks, BLOCK),
    ).reshape(slice_rows, features)
    out_grad = jnp.transpose(out_sum * out_keep * norm_factor)
    grad_attended = masked_matmul_nt(grad_rows[None], out_planes, out_spread, jnp.float32)
    grad_attended = grad_attended.reshape(block_rows, local_heads, head_width)
    inner_mean = jnp.mean(grad_attended * normed, axis=-1, keepdims=True)
    grad_mixed = inv_rms * (grad_attended - normed * inner_mean)
    grad_low = grad_mixed.astype(jnp.bfloat16)
    local_adjoint = jnp.einsum("thd,the->hde", query_wide, grad_mixed, precision=highest)
    after_state = entering(local_adjoint, "ctx", add_states, zeros_state)
    adjoint_scores = jnp.einsum(
        "the,she->hts", grad_low, values, preferred_element_type=jnp.float32
    )
    adjoint_scores = jnp.where(causal_keep, adjoint_scores, 0.0).astype(jnp.bfloat16)
    grad_query = jnp.einsum(
        "hts,shd->thd", adjoint_scores, key_spiked, preferred_element_type=jnp.float32
    )
    grad_query = grad_query + jnp.einsum("the,hde->thd", grad_mixed, prior_state, precision=highest)
    grad_key = jnp.einsum(
        "hts,thd->shd", adjoint_scores, query_spiked, preferred_element_type=jnp.float32
    )
    grad_key = grad_key + jnp.einsum(
        "she,hde->shd", values.astype(jnp.float32), after_state, precision=highest
    )
    grad_value = jnp.einsum("hts,the->she", scores, grad_low, preferred_element_type=jnp.float32)
    grad_value = grad_value + jnp.einsum("shd,hde->she", key_wide, after_state, precision=highest)
    grad_proj = jnp.stack(
        [
            (grad_query * query_spikes.astype(jnp.float32)).astype(jnp.bfloat16),
            (grad_key * key_spikes.astype(jnp.float32)).astype(jnp.bfloat16),
            grad_value.astype(jnp.bfloat16),
        ],
        axis=0,
    ).reshape(3, block_rows, features)
    qkv_part = jnp.einsum("tm,ptc->mpc", gathered, grad_proj, preferred_element_type=jnp.float32)
    qkv_sum = lax.psum_scatter(
        qkv_part.astype(jnp.bfloat16), "ctx", scatter_dimension=0, tiled=True
    ).astype(jnp.float32)
    qkv_keep = lax.dynamic_slice_in_dim(qkv_blocks, ctx_place * slice_blocks, slice_blocks, 1)
    qkv_keep = jnp.broadcast_to(
        jnp.transpose(qkv_keep, (1, 0, 2)).astype(jnp.float32)[:, None, :, :, None],
        (slice_blocks, BLOCK, 3, col_blocks, BLOCK),
    ).reshape(slice_rows, 3, features)
    qkv_grad = qkv_sum * qkv_keep * norm_factor
    grad_proj_late = grad_proj
    token_sum = ring_scatter(
        masked_matmul_nt(grad_proj_late, qkv_planes, qkv_spread, jnp.bfloat16), "tp"
    )
    head_sum = head_ring.finish()
    layer_out = (tokens.astype(jnp.float32) + head_sum).astype(jnp.bfloat16)
    token_grad = (cotangent.astype(jnp.float32) + token_sum).astype(jnp.bfloat16)
    return (layer_out, token_grad, qkv_grad, out_grad)


def solution(mesh):
    placed = (
        P(("ctx", "tp"), None),
        P("ctx", "tp"),
        P("ctx", "tp"),
        P(None, None, "tp"),
        P(None, None, "tp"),
        P("tp", None),
        P("tp", None),
        P(("ctx", "tp"), None),
    )
    return jax.shard_map(
        on_device,
        mesh=mesh,
        in_specs=placed,
        out_specs=(
            P(("ctx", "tp"), None),
            P(("ctx", "tp"), None),
            P("ctx", None, "tp"),
            P("tp", "ctx"),
        ),
        check_vma=False,
    )
```

```python
import math

import jax
import jax.numpy as jnp
from jax import lax
from jax.experimental import pallas as pl
from jax.experimental.pallas import tpu as pltpu
from jax.sharding import PartitionSpec as P

BLOCK = 128


EPSILON = 1e-05

def _tile(n, choices=(1024, 512, 256, 128)):
    for c in choices:
        if n % c == 0:
            return c
    return n


def _masked_tile(w_ref, m_ref, wm_ref):
    for g in range(w_ref.shape[0] // BLOCK):
        rows = slice(g * BLOCK, (g + 1) * BLOCK)
        wm_ref[rows, :] = w_ref[rows, :] * m_ref[g]


def _nn_kernel(a_ref, w_ref, m_ref, o_ref, acc_ref, wm_ref):
    k = pl.program_id(2)

    @pl.when(k == 0)
    def _():
        acc_ref[...] = jnp.zeros_like(acc_ref)

    _masked_tile(w_ref, m_ref, wm_ref)
    acc_ref[...] += jnp.dot(a_ref[...], wm_ref[...], preferred_element_type=jnp.float32)

    @pl.when(k == pl.num_programs(2) - 1)
    def _():
        o_ref[...] = acc_ref[...].astype(o_ref.dtype)


def _nt_kernel(a_ref, w_ref, m_ref, o_ref, acc_ref, wm_ref):
    p = pl.program_id(1)
    k = pl.program_id(2)

    @pl.when((p == 0) & (k == 0))
    def _():
        acc_ref[...] = jnp.zeros_like(acc_ref)

    _masked_tile(w_ref, m_ref, wm_ref)
    acc_ref[...] += lax.dot_general(
        a_ref[...], wm_ref[...], (((1,), (1,)), ((), ())), preferred_element_type=jnp.float32
    )

    @pl.when((p == pl.num_programs(1) - 1) & (k == pl.num_programs(2) - 1))
    def _():
        o_ref[...] = acc_ref[...].astype(o_ref.dtype)


def masked_matmul_nn(a, w, mask, out_dtype):
    m = a.shape[0]
    planes, rows, cols = w.shape
    tk, tn = _tile(rows), _tile(cols)
    grid = (planes, cols // tn, rows // tk)
    return pl.pallas_call(
        _nn_kernel,
        grid=grid,
        in_specs=[
            pl.BlockSpec((m, tk), lambda p, j, k: (0, k)),
            pl.BlockSpec((None, tk, tn), lambda p, j, k: (p, k, j)),
            pl.BlockSpec((None, tk // BLOCK, 1, tn), lambda p, j, k: (p, k, 0, j)),
        ],
        out_specs=pl.BlockSpec((None, m, tn), lambda p, j, k: (p, 0, j)),
        out_shape=jax.ShapeDtypeStruct((planes, m, cols), out_dtype),
        scratch_shapes=[pltpu.VMEM((m, tn), jnp.float32), pltpu.VMEM((tk, tn), w.dtype)],
        compiler_params=pltpu.CompilerParams(
            dimension_semantics=("parallel", "parallel", "arbitrary"),
            vmem_limit_bytes=48 * 1024 * 1024,
        ),
        cost_estimate=pl.CostEstimate(
            flops=2 * m * planes * rows * cols,
            bytes_accessed=a.size * 2 * planes * (cols // tn) + w.size * 2
            + m * planes * cols * jnp.dtype(out_dtype).itemsize,
            transcendentals=0,
        ),
    )(a, w, mask)


def masked_matmul_nt(a, w, mask, out_dtype):
    planes, m, _ = a.shape
    _, rows, cols = w.shape
    tr, tk = _tile(rows), _tile(cols)
    grid = (rows // tr, planes, cols // tk)
    return pl.pallas_call(
        _nt_kernel,
        grid=grid,
        in_specs=[
            pl.BlockSpec((None, m, tk), lambda i, p, k: (p, 0, k)),
            pl.BlockSpec((None, tr, tk), lambda i, p, k: (p, i, k)),
            pl.BlockSpec((None, tr // BLOCK, 1, tk), lambda i, p, k: (p, i, 0, k)),
        ],
        out_specs=pl.BlockSpec((m, tr), lambda i, p, k: (0, i)),
        out_shape=jax.ShapeDtypeStruct((m, rows), out_dtype),
        scratch_shapes=[pltpu.VMEM((m, tr), jnp.float32), pltpu.VMEM((tr, tk), w.dtype)],
        compiler_params=pltpu.CompilerParams(
            dimension_semantics=("parallel", "arbitrary", "arbitrary"),
            vmem_limit_bytes=48 * 1024 * 1024,
        ),
        cost_estimate=pl.CostEstimate(
            flops=2 * m * planes * rows * cols,
            bytes_accessed=a.size * 2 * (rows // tr) + w.size * 2
            + m * rows * jnp.dtype(out_dtype).itemsize,
            transcendentals=0,
        ),
    )(a, w, mask)


def ring_gather(value, axis, work=None):
    count = lax.axis_size(axis)
    place = lax.axis_index(axis)
    step = [(index, (index + 1) % count) for index in range(count)]
    moving = value
    placed = jnp.zeros((count,) + value.shape, value.dtype)
    placed = lax.dynamic_update_index_in_dim(placed, value, place, 0)
    results = None
    if work is not None:
        done = work(value)
        results = jnp.zeros((done.shape[0], count) + done.shape[1:], done.dtype)
        results = lax.dynamic_update_index_in_dim(results, done, place, 1)
    for lap in range(1, count):
        moving = lax.ppermute(moving, axis, step)
        source = (place + count - lap) % count
        placed = lax.dynamic_update_index_in_dim(placed, moving, source, 0)
        if work is not None:
            results = lax.dynamic_update_index_in_dim(results, work(moving), source, 1)
    return placed, results


def ring_scatter(value, axis):
    count = lax.axis_size(axis)
    place = lax.axis_index(axis)
    step = [(index, (index + 1) % count) for index in range(count)]
    rows = value.shape[0] // count
    pieces = value.reshape((count, rows) + value.shape[1:])

    def piece(index):
        return lax.dynamic_index_in_dim(pieces, index % count, 0, False).astype(jnp.float32)

    running = piece(place + count - 1)
    for lap in range(1, count):
        arrived = lax.ppermute(running.astype(jnp.bfloat16), axis, step)
        running = arrived.astype(jnp.float32) + piece(place + 2 * count - 1 - lap)
    return running


class GatherRing:
    def __init__(self, value, axis):
        self.axis = axis
        self.count = lax.axis_size(axis)
        self.place = lax.axis_index(axis)
        self.step = [(index, (index + 1) % self.count) for index in range(self.count)]
        self.moving = value
        placed = jnp.zeros((self.count,) + value.shape, value.dtype)
        self.placed = lax.dynamic_update_index_in_dim(placed, value, self.place, 0)
        self.lap = 1

    def advance(self, tie=None):
        if self.lap >= self.count:
            return tie
        moved = lax.ppermute(self.moving, self.axis, self.step)
        if tie is not None:
            moved, tie = lax.optimization_barrier((moved, tie))
        source = (self.place + self.count - self.lap) % self.count
        self.placed = lax.dynamic_update_index_in_dim(self.placed, moved, source, 0)
        self.moving = moved
        self.lap += 1
        return tie

    def finish(self):
        while self.lap < self.count:
            self.advance()
        return self.placed


class ScatterRing:
    def __init__(self, value, axis):
        self.axis = axis
        self.count = lax.axis_size(axis)
        self.place = lax.axis_index(axis)
        self.step = [(index, (index + 1) % self.count) for index in range(self.count)]
        rows = value.shape[0] // self.count
        self.pieces = value.reshape((self.count, rows) + value.shape[1:])
        self.running = self.piece(self.place + self.count - 1)
        self.lap = 1

    def piece(self, index):
        return lax.dynamic_index_in_dim(
            self.pieces, index % self.count, 0, False
        ).astype(jnp.float32)

    def advance(self, tie=None):
        if self.lap >= self.count:
            return tie
        arrived = lax.ppermute(self.running.astype(jnp.bfloat16), self.axis, self.step)
        if tie is not None:
            arrived, tie = lax.optimization_barrier((arrived, tie))
        self.running = arrived.astype(jnp.float32) + self.piece(
            self.place + 2 * self.count - 1 - self.lap
        )
        self.lap += 1
        return tie

    def finish(self):
        while self.lap < self.count:
            self.advance()
        return self.running


def carried_in(value, axis, join, neutral):
    place = lax.axis_index(axis)
    gathered = lax.all_gather(value.astype(jnp.bfloat16), axis)
    state = jnp.zeros_like(value) + jnp.asarray(neutral, value.dtype)

    def carried_one(lap, state):
        return join(state, lax.dynamic_index_in_dim(gathered, lap, 0, False).astype(value.dtype))

    return lax.fori_loop(0, place, carried_one, state)


def entering(value, axis, join, neutral):
    count = lax.axis_size(axis)
    place = lax.axis_index(axis)
    ahead = count - 1 - place
    gathered = lax.all_gather(
        value.astype(jnp.bfloat16 if value.dtype == jnp.float32 else value.dtype), axis
    )
    state = jnp.zeros_like(value) + jnp.asarray(neutral, value.dtype)

    def entering_one(lap, state):
        source = count - 1 - lap
        return join(state, lax.dynamic_index_in_dim(gathered, source, 0, False).astype(value.dtype))

    return lax.fori_loop(0, ahead, entering_one, state)


def expand_blocks(blocks):
    row_blocks, col_blocks = blocks.shape
    spread = jnp.broadcast_to(
        blocks.astype(jnp.bfloat16)[:, None, :, None], (row_blocks, BLOCK, col_blocks, BLOCK)
    )
    return spread.reshape(row_blocks * BLOCK, col_blocks * BLOCK)


def qkv_keep_table(qkv_blocks):
    tables = [expand_blocks(qkv_blocks[projection]) for projection in range(3)]
    return jnp.stack(tables, axis=1)


def add_states(earlier, following):
    return earlier + following


def on_device(
    tokens, spike_query, spike_key, qkv_weight, qkv_blocks, out_weight, out_blocks, cotangent
):
    model_width = tokens.shape[1]
    block_rows = spike_query.shape[0]
    local_heads = spike_query.shape[1]
    features = qkv_weight.shape[2]
    head_width = features // local_heads
    row_blocks = model_width // BLOCK
    col_blocks = features // BLOCK
    highest = lax.Precision.HIGHEST
    qkv_planes = jnp.transpose(qkv_weight, (1, 0, 2))
    qkv_spread = jnp.broadcast_to(
        qkv_blocks.astype(jnp.bfloat16)[:, :, None, :, None],
        (3, row_blocks, 1, col_blocks, BLOCK),
    ).reshape(3, row_blocks, 1, features)
    out_planes = out_weight[None]
    out_spread = jnp.broadcast_to(
        out_blocks.astype(jnp.bfloat16)[None, :, None, :, None],
        (1, col_blocks, 1, row_blocks, BLOCK),
    ).reshape(1, col_blocks, 1, model_width)
    gathered, projected = ring_gather(
        tokens, "tp", lambda piece: masked_matmul_nn(piece, qkv_planes, qkv_spread, jnp.bfloat16)
    )
    gathered = gathered.reshape(block_rows, model_width)
    projected = projected.reshape(3, block_rows, features)
    projected, cotangent_late = lax.optimization_barrier((projected, cotangent))
    projected = projected.reshape(3, block_rows, local_heads, head_width)
    query_spikes = spike_query.astype(jnp.bfloat16)[:, :, None]
    key_spikes = spike_key.astype(jnp.bfloat16)[:, :, None]
    query_spiked = projected[0] * query_spikes
    key_spiked = projected[1] * key_spikes
    values = projected[2]
    query_wide = query_spiked.astype(jnp.float32)
    key_wide = key_spiked.astype(jnp.float32)
    local_state = jnp.einsum("shd,she->hde", key_spiked, values, preferred_element_type=jnp.float32)
    zeros_state = jnp.zeros_like(local_state)
    prior_state = carried_in(local_state, "ctx", add_states, zeros_state)
    positions = lax.iota(jnp.int32, block_rows)
    causal_keep = positions[:, None] >= positions[None, :]
    scores = jnp.einsum(
        "thd,shd->hts", query_spiked, key_spiked, preferred_element_type=jnp.float32
    )
    scores = jnp.where(causal_keep, scores, 0.0).astype(jnp.bfloat16)
    cotangent_ring = GatherRing(cotangent_late, "tp")
    scores = cotangent_ring.advance(scores)
    mixed_rows = jnp.einsum("hts,she->the", scores, values, preferred_element_type=jnp.float32)
    mixed_rows = mixed_rows + jnp.einsum("thd,hde->the", query_wide, prior_state, precision=highest)
    mixed_rows = cotangent_ring.advance(mixed_rows)
    inv_rms = lax.rsqrt(jnp.mean(mixed_rows * mixed_rows, axis=-1, keepdims=True) + EPSILON)
    normed = mixed_rows * inv_rms
    attended = normed.astype(jnp.bfloat16).reshape(block_rows, features)
    head_part = masked_matmul_nn(attended, out_planes, out_spread, jnp.bfloat16)[0]
    head_part = cotangent_ring.advance(head_part)
    grad_rows = cotangent_ring.finish().reshape(block_rows, model_width)
    head_part, grad_rows = lax.optimization_barrier((head_part, grad_rows))
    head_ring = ScatterRing(head_part, "tp")
    ctx_count = lax.axis_size("ctx")
    ctx_place = lax.axis_index("ctx")
    slice_rows = model_width // ctx_count
    slice_blocks = slice_rows // BLOCK
    norm_factor = 1.0 / math.sqrt(block_rows * ctx_count)
    out_part = jnp.einsum("tm,tf->mf", grad_rows, attended, preferred_element_type=jnp.float32)
    out_sum = lax.psum_scatter(
        out_part.astype(jnp.bfloat16), "ctx", scatter_dimension=0, tiled=True
    ).astype(jnp.float32)
    out_keep = lax.dynamic_slice_in_dim(out_blocks, ctx_place * slice_blocks, slice_blocks, 1)
    out_keep = jnp.broadcast_to(
        jnp.transpose(out_keep).astype(jnp.float32)[:, None, :, None],
        (slice_blocks, BLOCK, col_blocks, BLOCK),
    ).reshape(slice_rows, features)
    out_grad = jnp.transpose(out_sum * out_keep * norm_factor)
    grad_attended = masked_matmul_nt(grad_rows[None], out_planes, out_spread, jnp.float32)
    grad_attended = grad_attended.reshape(block_rows, local_heads, head_width)
    inner_mean = jnp.mean(grad_attended * normed, axis=-1, keepdims=True)
    grad_mixed = inv_rms * (grad_attended - normed * inner_mean)
    grad_low = grad_mixed.astype(jnp.bfloat16)
    local_adjoint = jnp.einsum("thd,the->hde", query_wide, grad_mixed, precision=highest)
    after_state = entering(local_adjoint, "ctx", add_states, zeros_state)
    adjoint_scores = jnp.einsum(
        "the,she->hts", grad_low, values, preferred_element_type=jnp.float32
    )
    adjoint_scores = jnp.where(causal_keep, adjoint_scores, 0.0).astype(jnp.bfloat16)
    grad_query = jnp.einsum(
        "hts,shd->thd", adjoint_scores, key_spiked, preferred_element_type=jnp.float32
    )
    grad_query = grad_query + jnp.einsum("the,hde->thd", grad_mixed, prior_state, precision=highest)
    grad_key = jnp.einsum(
        "hts,thd->shd", adjoint_scores, query_spiked, preferred_element_type=jnp.float32
    )
    grad_key = grad_key + jnp.einsum(
        "she,hde->shd", values.astype(jnp.float32), after_state, precision=highest
    )
    grad_value = jnp.einsum("hts,the->she", scores, grad_low, preferred_element_type=jnp.float32)
    grad_value = grad_value + jnp.einsum("shd,hde->she", key_wide, after_state, precision=highest)
    grad_proj = jnp.stack(
        [
            (grad_query * query_spikes.astype(jnp.float32)).astype(jnp.bfloat16),
            (grad_key * key_spikes.astype(jnp.float32)).astype(jnp.bfloat16),
            grad_value.astype(jnp.bfloat16),
        ],
        axis=0,
    ).reshape(3, block_rows, features)
    plane_sums = {}
    for plane in (2, 1, 0):
        plane_part = jnp.dot(
            gathered.T, grad_proj[plane], preferred_element_type=jnp.float32
        ).astype(jnp.bfloat16)
        plane_sums[plane] = lax.psum_scatter(plane_part, "ctx", scatter_dimension=0, tiled=True)
    qkv_sum = jnp.stack([plane_sums[plane] for plane in range(3)], axis=1).astype(jnp.float32)
    qkv_keep = lax.dynamic_slice_in_dim(qkv_blocks, ctx_place * slice_blocks, slice_blocks, 1)
    qkv_keep = jnp.broadcast_to(
        jnp.transpose(qkv_keep, (1, 0, 2)).astype(jnp.float32)[:, None, :, :, None],
        (slice_blocks, BLOCK, 3, col_blocks, BLOCK),
    ).reshape(slice_rows, 3, features)
    qkv_grad = qkv_sum * qkv_keep * norm_factor
    grad_proj_late = grad_proj
    token_sum = ring_scatter(
        masked_matmul_nt(grad_proj_late, qkv_planes, qkv_spread, jnp.bfloat16), "tp"
    )
    head_sum = head_ring.finish()
    layer_out = (tokens.astype(jnp.float32) + head_sum).astype(jnp.bfloat16)
    token_grad = (cotangent.astype(jnp.float32) + token_sum).astype(jnp.bfloat16)
    return (layer_out, token_grad, qkv_grad, out_grad)


def solution(mesh):
    placed = (
        P(("ctx", "tp"), None),
        P("ctx", "tp"),
        P("ctx", "tp"),
        P(None, None, "tp"),
        P(None, None, "tp"),
        P("tp", None),
        P("tp", None),
        P(("ctx", "tp"), None),
    )
    return jax.shard_map(
        on_device,
        mesh=mesh,
        in_specs=placed,
        out_specs=(
            P(("ctx", "tp"), None),
            P(("ctx", "tp"), None),
            P("ctx", None, "tp"),
            P("tp", "ctx"),
        ),
        check_vma=False,
    )
```

```python
import math

import jax
import jax.numpy as jnp
from jax import lax
from jax.experimental import pallas as pl
from jax.experimental.pallas import tpu as pltpu
from jax.sharding import PartitionSpec as P

BLOCK = 128


EPSILON = 1e-05

def _tile(n, choices=(1024, 512, 256, 128)):
    for c in choices:
        if n % c == 0:
            return c
    return n


def _masked_tile(w_ref, m_ref, wm_ref):
    for g in range(w_ref.shape[0] // BLOCK):
        rows = slice(g * BLOCK, (g + 1) * BLOCK)
        wm_ref[rows, :] = w_ref[rows, :] * m_ref[g]


def _nn_kernel(a_ref, w_ref, m_ref, o_ref, acc_ref, wm_ref):
    k = pl.program_id(2)

    @pl.when(k == 0)
    def _():
        acc_ref[...] = jnp.zeros_like(acc_ref)

    _masked_tile(w_ref, m_ref, wm_ref)
    acc_ref[...] += jnp.dot(a_ref[...], wm_ref[...], preferred_element_type=jnp.float32)

    @pl.when(k == pl.num_programs(2) - 1)
    def _():
        o_ref[...] = acc_ref[...].astype(o_ref.dtype)


def _nt_kernel(a_ref, w_ref, m_ref, o_ref, acc_ref, wm_ref):
    p = pl.program_id(1)
    k = pl.program_id(2)

    @pl.when((p == 0) & (k == 0))
    def _():
        acc_ref[...] = jnp.zeros_like(acc_ref)

    _masked_tile(w_ref, m_ref, wm_ref)
    acc_ref[...] += lax.dot_general(
        a_ref[...], wm_ref[...], (((1,), (1,)), ((), ())), preferred_element_type=jnp.float32
    )

    @pl.when((p == pl.num_programs(1) - 1) & (k == pl.num_programs(2) - 1))
    def _():
        o_ref[...] = acc_ref[...].astype(o_ref.dtype)


def masked_matmul_nn(a, w, mask, out_dtype):
    m = a.shape[0]
    planes, rows, cols = w.shape
    tk, tn = _tile(rows), _tile(cols)
    grid = (planes, cols // tn, rows // tk)
    return pl.pallas_call(
        _nn_kernel,
        grid=grid,
        in_specs=[
            pl.BlockSpec((m, tk), lambda p, j, k: (0, k)),
            pl.BlockSpec((None, tk, tn), lambda p, j, k: (p, k, j)),
            pl.BlockSpec((None, tk // BLOCK, 1, tn), lambda p, j, k: (p, k, 0, j)),
        ],
        out_specs=pl.BlockSpec((None, m, tn), lambda p, j, k: (p, 0, j)),
        out_shape=jax.ShapeDtypeStruct((planes, m, cols), out_dtype),
        scratch_shapes=[pltpu.VMEM((m, tn), jnp.float32), pltpu.VMEM((tk, tn), w.dtype)],
        compiler_params=pltpu.CompilerParams(
            dimension_semantics=("parallel", "parallel", "arbitrary"),
            vmem_limit_bytes=48 * 1024 * 1024,
        ),
        cost_estimate=pl.CostEstimate(
            flops=2 * m * planes * rows * cols,
            bytes_accessed=a.size * 2 * planes * (cols // tn) + w.size * 2
            + m * planes * cols * jnp.dtype(out_dtype).itemsize,
            transcendentals=0,
        ),
    )(a, w, mask)


def masked_matmul_nt(a, w, mask, out_dtype):
    planes, m, _ = a.shape
    _, rows, cols = w.shape
    tr, tk = _tile(rows), _tile(cols)
    grid = (rows // tr, planes, cols // tk)
    return pl.pallas_call(
        _nt_kernel,
        grid=grid,
        in_specs=[
            pl.BlockSpec((None, m, tk), lambda i, p, k: (p, 0, k)),
            pl.BlockSpec((None, tr, tk), lambda i, p, k: (p, i, k)),
            pl.BlockSpec((None, tr // BLOCK, 1, tk), lambda i, p, k: (p, i, 0, k)),
        ],
        out_specs=pl.BlockSpec((m, tr), lambda i, p, k: (0, i)),
        out_shape=jax.ShapeDtypeStruct((m, rows), out_dtype),
        scratch_shapes=[pltpu.VMEM((m, tr), jnp.float32), pltpu.VMEM((tr, tk), w.dtype)],
        compiler_params=pltpu.CompilerParams(
            dimension_semantics=("parallel", "arbitrary", "arbitrary"),
            vmem_limit_bytes=48 * 1024 * 1024,
        ),
        cost_estimate=pl.CostEstimate(
            flops=2 * m * planes * rows * cols,
            bytes_accessed=a.size * 2 * (rows // tr) + w.size * 2
            + m * rows * jnp.dtype(out_dtype).itemsize,
            transcendentals=0,
        ),
    )(a, w, mask)


def ring_gather(value, axis, work=None):
    count = lax.axis_size(axis)
    place = lax.axis_index(axis)
    step = [(index, (index + 1) % count) for index in range(count)]
    moving = value
    placed = jnp.zeros((count,) + value.shape, value.dtype)
    placed = lax.dynamic_update_index_in_dim(placed, value, place, 0)
    results = None
    if work is not None:
        done = work(value)
        results = jnp.zeros((done.shape[0], count) + done.shape[1:], done.dtype)
        results = lax.dynamic_update_index_in_dim(results, done, place, 1)
    for lap in range(1, count):
        moving = lax.ppermute(moving, axis, step)
        source = (place + count - lap) % count
        placed = lax.dynamic_update_index_in_dim(placed, moving, source, 0)
        if work is not None:
            results = lax.dynamic_update_index_in_dim(results, work(moving), source, 1)
    return placed, results


def ring_scatter(value, axis):
    count = lax.axis_size(axis)
    place = lax.axis_index(axis)
    step = [(index, (index + 1) % count) for index in range(count)]
    rows = value.shape[0] // count
    pieces = value.reshape((count, rows) + value.shape[1:])

    def piece(index):
        return lax.dynamic_index_in_dim(pieces, index % count, 0, False).astype(jnp.float32)

    running = piece(place + count - 1)
    for lap in range(1, count):
        arrived = lax.ppermute(running.astype(jnp.bfloat16), axis, step)
        running = arrived.astype(jnp.float32) + piece(place + 2 * count - 1 - lap)
    return running


class GatherRing:
    def __init__(self, value, axis):
        self.axis = axis
        self.count = lax.axis_size(axis)
        self.place = lax.axis_index(axis)
        self.step = [(index, (index + 1) % self.count) for index in range(self.count)]
        self.moving = value
        placed = jnp.zeros((self.count,) + value.shape, value.dtype)
        self.placed = lax.dynamic_update_index_in_dim(placed, value, self.place, 0)
        self.lap = 1

    def advance(self, tie=None):
        if self.lap >= self.count:
            return tie
        moved = lax.ppermute(self.moving, self.axis, self.step)
        if tie is not None:
            moved, tie = lax.optimization_barrier((moved, tie))
        source = (self.place + self.count - self.lap) % self.count
        self.placed = lax.dynamic_update_index_in_dim(self.placed, moved, source, 0)
        self.moving = moved
        self.lap += 1
        return tie

    def finish(self):
        while self.lap < self.count:
            self.advance()
        return self.placed


class ScatterRing:
    def __init__(self, value, axis):
        self.axis = axis
        self.count = lax.axis_size(axis)
        self.place = lax.axis_index(axis)
        self.step = [(index, (index + 1) % self.count) for index in range(self.count)]
        rows = value.shape[0] // self.count
        self.pieces = value.reshape((self.count, rows) + value.shape[1:])
        self.running = self.piece(self.place + self.count - 1)
        self.lap = 1

    def piece(self, index):
        return lax.dynamic_index_in_dim(
            self.pieces, index % self.count, 0, False
        ).astype(jnp.float32)

    def advance(self, tie=None):
        if self.lap >= self.count:
            return tie
        arrived = lax.ppermute(self.running.astype(jnp.bfloat16), self.axis, self.step)
        if tie is not None:
            arrived, tie = lax.optimization_barrier((arrived, tie))
        self.running = arrived.astype(jnp.float32) + self.piece(
            self.place + 2 * self.count - 1 - self.lap
        )
        self.lap += 1
        return tie

    def finish(self):
        while self.lap < self.count:
            self.advance()
        return self.running


def carried_in(value, axis, join, neutral):
    place = lax.axis_index(axis)
    gathered = lax.all_gather(value.astype(jnp.bfloat16), axis)
    state = jnp.zeros_like(value) + jnp.asarray(neutral, value.dtype)

    def carried_one(lap, state):
        return join(state, lax.dynamic_index_in_dim(gathered, lap, 0, False).astype(value.dtype))

    return lax.fori_loop(0, place, carried_one, state)


def entering(value, axis, join, neutral):
    count = lax.axis_size(axis)
    place = lax.axis_index(axis)
    ahead = count - 1 - place
    gathered = lax.all_gather(
        value.astype(jnp.bfloat16 if value.dtype == jnp.float32 else value.dtype), axis
    )
    state = jnp.zeros_like(value) + jnp.asarray(neutral, value.dtype)

    def entering_one(lap, state):
        source = count - 1 - lap
        return join(state, lax.dynamic_index_in_dim(gathered, source, 0, False).astype(value.dtype))

    return lax.fori_loop(0, ahead, entering_one, state)


def expand_blocks(blocks):
    row_blocks, col_blocks = blocks.shape
    spread = jnp.broadcast_to(
        blocks.astype(jnp.bfloat16)[:, None, :, None], (row_blocks, BLOCK, col_blocks, BLOCK)
    )
    return spread.reshape(row_blocks * BLOCK, col_blocks * BLOCK)


def qkv_keep_table(qkv_blocks):
    tables = [expand_blocks(qkv_blocks[projection]) for projection in range(3)]
    return jnp.stack(tables, axis=1)


def add_states(earlier, following):
    return earlier + following


def on_device(
    tokens, spike_query, spike_key, qkv_weight, qkv_blocks, out_weight, out_blocks, cotangent
):
    model_width = tokens.shape[1]
    block_rows = spike_query.shape[0]
    local_heads = spike_query.shape[1]
    features = qkv_weight.shape[2]
    head_width = features // local_heads
    row_blocks = model_width // BLOCK
    col_blocks = features // BLOCK
    highest = lax.Precision.HIGHEST
    qkv_planes = jnp.transpose(qkv_weight, (1, 0, 2))
    qkv_spread = jnp.broadcast_to(
        qkv_blocks.astype(jnp.bfloat16)[:, :, None, :, None],
        (3, row_blocks, 1, col_blocks, BLOCK),
    ).reshape(3, row_blocks, 1, features)
    out_planes = out_weight[None]
    out_spread = jnp.broadcast_to(
        out_blocks.astype(jnp.bfloat16)[None, :, None, :, None],
        (1, col_blocks, 1, row_blocks, BLOCK),
    ).reshape(1, col_blocks, 1, model_width)
    gathered, projected = ring_gather(
        tokens, "tp", lambda piece: masked_matmul_nn(piece, qkv_planes, qkv_spread, jnp.bfloat16)
    )
    gathered = gathered.reshape(block_rows, model_width)
    projected = projected.reshape(3, block_rows, features)
    projected, cotangent_late = lax.optimization_barrier((projected, cotangent))
    projected = projected.reshape(3, block_rows, local_heads, head_width)
    query_spikes = spike_query.astype(jnp.bfloat16)[:, :, None]
    key_spikes = spike_key.astype(jnp.bfloat16)[:, :, None]
    query_spiked = projected[0] * query_spikes
    key_spiked = projected[1] * key_spikes
    values = projected[2]
    query_wide = query_spiked.astype(jnp.float32)
    key_wide = key_spiked.astype(jnp.float32)
    local_state = jnp.einsum("shd,she->hde", key_spiked, values, preferred_element_type=jnp.float32)
    zeros_state = jnp.zeros_like(local_state)
    prior_state = carried_in(local_state, "ctx", add_states, zeros_state)
    positions = lax.iota(jnp.int32, block_rows)
    causal_keep = positions[:, None] >= positions[None, :]
    scores = jnp.einsum(
        "thd,shd->hts", query_spiked, key_spiked, preferred_element_type=jnp.float32
    )
    scores = jnp.where(causal_keep, scores, 0.0).astype(jnp.bfloat16)
    cotangent_ring = GatherRing(cotangent_late, "tp")
    scores = cotangent_ring.advance(scores)
    mixed_rows = jnp.einsum("hts,she->the", scores, values, preferred_element_type=jnp.float32)
    mixed_rows = mixed_rows + jnp.einsum("thd,hde->the", query_wide, prior_state, precision=highest)
    mixed_rows = cotangent_ring.advance(mixed_rows)
    inv_rms = lax.rsqrt(jnp.mean(mixed_rows * mixed_rows, axis=-1, keepdims=True) + EPSILON)
    normed = mixed_rows * inv_rms
    attended = normed.astype(jnp.bfloat16).reshape(block_rows, features)
    head_part = masked_matmul_nn(attended, out_planes, out_spread, jnp.bfloat16)[0]
    head_part = cotangent_ring.advance(head_part)
    grad_rows = cotangent_ring.finish().reshape(block_rows, model_width)
    head_part, grad_rows = lax.optimization_barrier((head_part, grad_rows))
    head_ring = ScatterRing(head_part, "tp")
    ctx_count = lax.axis_size("ctx")
    ctx_place = lax.axis_index("ctx")
    slice_rows = model_width // ctx_count
    slice_blocks = slice_rows // BLOCK
    norm_factor = 1.0 / math.sqrt(block_rows * ctx_count)
    out_part = jnp.einsum("tm,tf->mf", grad_rows, attended, preferred_element_type=jnp.float32)
    out_sum = lax.psum_scatter(
        out_part.astype(jnp.bfloat16), "ctx", scatter_dimension=0, tiled=True
    ).astype(jnp.float32)
    out_keep = lax.dynamic_slice_in_dim(out_blocks, ctx_place * slice_blocks, slice_blocks, 1)
    out_keep = jnp.broadcast_to(
        jnp.transpose(out_keep).astype(jnp.float32)[:, None, :, None],
        (slice_blocks, BLOCK, col_blocks, BLOCK),
    ).reshape(slice_rows, features)
    out_grad = jnp.transpose(out_sum * out_keep * norm_factor)
    grad_attended = masked_matmul_nt(grad_rows[None], out_planes, out_spread, jnp.float32)
    grad_attended = grad_attended.reshape(block_rows, local_heads, head_width)
    inner_mean = jnp.mean(grad_attended * normed, axis=-1, keepdims=True)
    grad_mixed = inv_rms * (grad_attended - normed * inner_mean)
    grad_low = grad_mixed.astype(jnp.bfloat16)
    local_adjoint = jnp.einsum("thd,the->hde", query_wide, grad_mixed, precision=highest)
    after_state = entering(local_adjoint, "ctx", add_states, zeros_state)
    adjoint_scores = jnp.einsum(
        "the,she->hts", grad_low, values, preferred_element_type=jnp.float32
    )
    adjoint_scores = jnp.where(causal_keep, adjoint_scores, 0.0).astype(jnp.bfloat16)
    adjoint_scores = head_ring.advance(adjoint_scores)
    grad_query = jnp.einsum(
        "hts,shd->thd", adjoint_scores, key_spiked, preferred_element_type=jnp.float32
    )
    grad_query = grad_query + jnp.einsum("the,hde->thd", grad_mixed, prior_state, precision=highest)
    grad_key = jnp.einsum(
        "hts,thd->shd", adjoint_scores, query_spiked, preferred_element_type=jnp.float32
    )
    grad_key = grad_key + jnp.einsum(
        "she,hde->shd", values.astype(jnp.float32), after_state, precision=highest
    )
    grad_value = jnp.einsum("hts,the->she", scores, grad_low, preferred_element_type=jnp.float32)
    grad_value = grad_value + jnp.einsum("shd,hde->she", key_wide, after_state, precision=highest)
    grad_proj = jnp.stack(
        [
            (grad_query * query_spikes.astype(jnp.float32)).astype(jnp.bfloat16),
            (grad_key * key_spikes.astype(jnp.float32)).astype(jnp.bfloat16),
            grad_value.astype(jnp.bfloat16),
        ],
        axis=0,
    ).reshape(3, block_rows, features)
    qkv_part = jnp.einsum("tm,ptc->mpc", gathered, grad_proj, preferred_element_type=jnp.float32)
    qkv_full_keep = jnp.broadcast_to(
        jnp.transpose(qkv_blocks, (1, 0, 2)).astype(jnp.bfloat16)[:, None, :, :, None],
        (row_blocks, BLOCK, 3, col_blocks, BLOCK),
    ).reshape(model_width, 3, features)
    qkv_sum = lax.psum_scatter(
        (qkv_part * qkv_full_keep).astype(jnp.bfloat16), "ctx", scatter_dimension=0, tiled=True
    ).astype(jnp.float32)
    qkv_grad = qkv_sum * norm_factor
    grad_proj = head_ring.advance(grad_proj)
    grad_proj_late = grad_proj
    token_sum = ring_scatter(
        masked_matmul_nt(grad_proj_late, qkv_planes, qkv_spread, jnp.bfloat16), "tp"
    )
    head_sum = head_ring.finish()
    layer_out = (tokens.astype(jnp.float32) + head_sum).astype(jnp.bfloat16)
    token_grad = (cotangent.astype(jnp.float32) + token_sum).astype(jnp.bfloat16)
    return (layer_out, token_grad, qkv_grad, out_grad)


def solution(mesh):
    placed = (
        P(("ctx", "tp"), None),
        P("ctx", "tp"),
        P("ctx", "tp"),
        P(None, None, "tp"),
        P(None, None, "tp"),
        P("tp", None),
        P("tp", None),
        P(("ctx", "tp"), None),
    )
    return jax.shard_map(
        on_device,
        mesh=mesh,
        in_specs=placed,
        out_specs=(
            P(("ctx", "tp"), None),
            P(("ctx", "tp"), None),
            P("ctx", None, "tp"),
            P("tp", "ctx"),
        ),
        check_vma=False,
    )
```

```python
import math

import jax
import jax.numpy as jnp
from jax import lax
from jax.experimental import pallas as pl
from jax.experimental.pallas import tpu as pltpu
from jax.sharding import PartitionSpec as P

BLOCK = 128


EPSILON = 1e-05

def _tile(n, choices=(1024, 512, 256, 128)):
    for c in choices:
        if n % c == 0:
            return c
    return n


def _masked_tile(w_ref, m_ref, wm_ref):
    for g in range(w_ref.shape[0] // BLOCK):
        rows = slice(g * BLOCK, (g + 1) * BLOCK)
        wm_ref[rows, :] = w_ref[rows, :] * m_ref[g]


def _nn_kernel(a_ref, w_ref, m_ref, o_ref, acc_ref, wm_ref):
    k = pl.program_id(2)

    @pl.when(k == 0)
    def _():
        acc_ref[...] = jnp.zeros_like(acc_ref)

    _masked_tile(w_ref, m_ref, wm_ref)
    acc_ref[...] += jnp.dot(a_ref[...], wm_ref[...], preferred_element_type=jnp.float32)

    @pl.when(k == pl.num_programs(2) - 1)
    def _():
        o_ref[...] = acc_ref[...].astype(o_ref.dtype)


def _nt_kernel(a_ref, w_ref, m_ref, o_ref, acc_ref, wm_ref):
    p = pl.program_id(1)
    k = pl.program_id(2)

    @pl.when((p == 0) & (k == 0))
    def _():
        acc_ref[...] = jnp.zeros_like(acc_ref)

    _masked_tile(w_ref, m_ref, wm_ref)
    acc_ref[...] += lax.dot_general(
        a_ref[...], wm_ref[...], (((1,), (1,)), ((), ())), preferred_element_type=jnp.float32
    )

    @pl.when((p == pl.num_programs(1) - 1) & (k == pl.num_programs(2) - 1))
    def _():
        o_ref[...] = acc_ref[...].astype(o_ref.dtype)


def masked_matmul_nn(a, w, mask, out_dtype):
    m = a.shape[0]
    planes, rows, cols = w.shape
    tk, tn = _tile(rows), _tile(cols)
    grid = (planes, cols // tn, rows // tk)
    return pl.pallas_call(
        _nn_kernel,
        grid=grid,
        in_specs=[
            pl.BlockSpec((m, tk), lambda p, j, k: (0, k)),
            pl.BlockSpec((None, tk, tn), lambda p, j, k: (p, k, j)),
            pl.BlockSpec((None, tk // BLOCK, 1, tn), lambda p, j, k: (p, k, 0, j)),
        ],
        out_specs=pl.BlockSpec((None, m, tn), lambda p, j, k: (p, 0, j)),
        out_shape=jax.ShapeDtypeStruct((planes, m, cols), out_dtype),
        scratch_shapes=[pltpu.VMEM((m, tn), jnp.float32), pltpu.VMEM((tk, tn), w.dtype)],
        compiler_params=pltpu.CompilerParams(
            dimension_semantics=("parallel", "parallel", "arbitrary"),
            vmem_limit_bytes=48 * 1024 * 1024,
        ),
        cost_estimate=pl.CostEstimate(
            flops=2 * m * planes * rows * cols,
            bytes_accessed=a.size * 2 * planes * (cols // tn) + w.size * 2
            + m * planes * cols * jnp.dtype(out_dtype).itemsize,
            transcendentals=0,
        ),
    )(a, w, mask)


def masked_matmul_nt(a, w, mask, out_dtype):
    planes, m, _ = a.shape
    _, rows, cols = w.shape
    tr, tk = _tile(rows), _tile(cols)
    grid = (rows // tr, planes, cols // tk)
    return pl.pallas_call(
        _nt_kernel,
        grid=grid,
        in_specs=[
            pl.BlockSpec((None, m, tk), lambda i, p, k: (p, 0, k)),
            pl.BlockSpec((None, tr, tk), lambda i, p, k: (p, i, k)),
            pl.BlockSpec((None, tr // BLOCK, 1, tk), lambda i, p, k: (p, i, 0, k)),
        ],
        out_specs=pl.BlockSpec((m, tr), lambda i, p, k: (0, i)),
        out_shape=jax.ShapeDtypeStruct((m, rows), out_dtype),
        scratch_shapes=[pltpu.VMEM((m, tr), jnp.float32), pltpu.VMEM((tr, tk), w.dtype)],
        compiler_params=pltpu.CompilerParams(
            dimension_semantics=("parallel", "arbitrary", "arbitrary"),
            vmem_limit_bytes=48 * 1024 * 1024,
        ),
        cost_estimate=pl.CostEstimate(
            flops=2 * m * planes * rows * cols,
            bytes_accessed=a.size * 2 * (rows // tr) + w.size * 2
            + m * rows * jnp.dtype(out_dtype).itemsize,
            transcendentals=0,
        ),
    )(a, w, mask)


def ring_gather(value, axis, work=None):
    count = lax.axis_size(axis)
    place = lax.axis_index(axis)
    step = [(index, (index + 1) % count) for index in range(count)]
    moving = value
    placed = jnp.zeros((count,) + value.shape, value.dtype)
    placed = lax.dynamic_update_index_in_dim(placed, value, place, 0)
    results = None
    if work is not None:
        done = work(value)
        results = jnp.zeros((done.shape[0], count) + done.shape[1:], done.dtype)
        results = lax.dynamic_update_index_in_dim(results, done, place, 1)
    for lap in range(1, count):
        moving = lax.ppermute(moving, axis, step)
        source = (place + count - lap) % count
        placed = lax.dynamic_update_index_in_dim(placed, moving, source, 0)
        if work is not None:
            results = lax.dynamic_update_index_in_dim(results, work(moving), source, 1)
    return placed, results


def ring_scatter(value, axis):
    count = lax.axis_size(axis)
    place = lax.axis_index(axis)
    step = [(index, (index + 1) % count) for index in range(count)]
    rows = value.shape[0] // count
    pieces = value.reshape((count, rows) + value.shape[1:])

    def piece(index):
        return lax.dynamic_index_in_dim(pieces, index % count, 0, False).astype(jnp.float32)

    running = piece(place + count - 1)
    for lap in range(1, count):
        arrived = lax.ppermute(running.astype(jnp.bfloat16), axis, step)
        running = arrived.astype(jnp.float32) + piece(place + 2 * count - 1 - lap)
    return running


class GatherRing:
    def __init__(self, value, axis):
        self.axis = axis
        self.count = lax.axis_size(axis)
        self.place = lax.axis_index(axis)
        self.step = [(index, (index + 1) % self.count) for index in range(self.count)]
        self.moving = value
        placed = jnp.zeros((self.count,) + value.shape, value.dtype)
        self.placed = lax.dynamic_update_index_in_dim(placed, value, self.place, 0)
        self.lap = 1

    def advance(self, tie=None):
        if self.lap >= self.count:
            return tie
        moved = lax.ppermute(self.moving, self.axis, self.step)
        if tie is not None:
            moved, tie = lax.optimization_barrier((moved, tie))
        source = (self.place + self.count - self.lap) % self.count
        self.placed = lax.dynamic_update_index_in_dim(self.placed, moved, source, 0)
        self.moving = moved
        self.lap += 1
        return tie

    def finish(self):
        while self.lap < self.count:
            self.advance()
        return self.placed


class ScatterRing:
    def __init__(self, value, axis):
        self.axis = axis
        self.count = lax.axis_size(axis)
        self.place = lax.axis_index(axis)
        self.step = [(index, (index + 1) % self.count) for index in range(self.count)]
        rows = value.shape[0] // self.count
        self.pieces = value.reshape((self.count, rows) + value.shape[1:])
        self.running = self.piece(self.place + self.count - 1)
        self.lap = 1

    def piece(self, index):
        return lax.dynamic_index_in_dim(
            self.pieces, index % self.count, 0, False
        ).astype(jnp.float32)

    def advance(self, tie=None):
        if self.lap >= self.count:
            return tie
        arrived = lax.ppermute(self.running.astype(jnp.bfloat16), self.axis, self.step)
        if tie is not None:
            arrived, tie = lax.optimization_barrier((arrived, tie))
        self.running = arrived.astype(jnp.float32) + self.piece(
            self.place + 2 * self.count - 1 - self.lap
        )
        self.lap += 1
        return tie

    def finish(self):
        while self.lap < self.count:
            self.advance()
        return self.running


def carried_in(value, axis, join, neutral):
    place = lax.axis_index(axis)
    gathered = lax.all_gather(value.astype(jnp.bfloat16), axis)
    state = jnp.zeros_like(value) + jnp.asarray(neutral, value.dtype)

    def carried_one(lap, state):
        return join(state, lax.dynamic_index_in_dim(gathered, lap, 0, False).astype(value.dtype))

    return lax.fori_loop(0, place, carried_one, state)


def entering(value, axis, join, neutral):
    count = lax.axis_size(axis)
    place = lax.axis_index(axis)
    ahead = count - 1 - place
    gathered = lax.all_gather(
        value.astype(jnp.bfloat16 if value.dtype == jnp.float32 else value.dtype), axis
    )
    state = jnp.zeros_like(value) + jnp.asarray(neutral, value.dtype)

    def entering_one(lap, state):
        source = count - 1 - lap
        return join(state, lax.dynamic_index_in_dim(gathered, source, 0, False).astype(value.dtype))

    return lax.fori_loop(0, ahead, entering_one, state)


def expand_blocks(blocks):
    row_blocks, col_blocks = blocks.shape
    spread = jnp.broadcast_to(
        blocks.astype(jnp.bfloat16)[:, None, :, None], (row_blocks, BLOCK, col_blocks, BLOCK)
    )
    return spread.reshape(row_blocks * BLOCK, col_blocks * BLOCK)


def qkv_keep_table(qkv_blocks):
    tables = [expand_blocks(qkv_blocks[projection]) for projection in range(3)]
    return jnp.stack(tables, axis=1)


def add_states(earlier, following):
    return earlier + following


def on_device(
    tokens, spike_query, spike_key, qkv_weight, qkv_blocks, out_weight, out_blocks, cotangent
):
    model_width = tokens.shape[1]
    block_rows = spike_query.shape[0]
    local_heads = spike_query.shape[1]
    features = qkv_weight.shape[2]
    head_width = features // local_heads
    row_blocks = model_width // BLOCK
    col_blocks = features // BLOCK
    highest = lax.Precision.HIGHEST
    qkv_planes = jnp.transpose(qkv_weight, (1, 0, 2))
    qkv_spread = jnp.broadcast_to(
        qkv_blocks.astype(jnp.bfloat16)[:, :, None, :, None],
        (3, row_blocks, 1, col_blocks, BLOCK),
    ).reshape(3, row_blocks, 1, features)
    out_planes = out_weight[None]
    out_spread = jnp.broadcast_to(
        out_blocks.astype(jnp.bfloat16)[None, :, None, :, None],
        (1, col_blocks, 1, row_blocks, BLOCK),
    ).reshape(1, col_blocks, 1, model_width)
    gathered, projected = ring_gather(
        tokens, "tp", lambda piece: masked_matmul_nn(piece, qkv_planes, qkv_spread, jnp.bfloat16)
    )
    gathered = gathered.reshape(block_rows, model_width)
    projected = projected.reshape(3, block_rows, features)
    gathered, cotangent_late = lax.optimization_barrier((gathered, cotangent))
    projected = projected.reshape(3, block_rows, local_heads, head_width)
    query_spikes = spike_query.astype(jnp.bfloat16)[:, :, None]
    key_spikes = spike_key.astype(jnp.bfloat16)[:, :, None]
    query_spiked = projected[0] * query_spikes
    key_spiked = projected[1] * key_spikes
    values = projected[2]
    query_wide = query_spiked.astype(jnp.float32)
    key_wide = key_spiked.astype(jnp.float32)
    local_state = jnp.einsum("shd,she->hde", key_spiked, values, preferred_element_type=jnp.float32)
    zeros_state = jnp.zeros_like(local_state)
    prior_state = carried_in(local_state, "ctx", add_states, zeros_state)
    positions = lax.iota(jnp.int32, block_rows)
    causal_keep = positions[:, None] >= positions[None, :]
    scores = jnp.einsum(
        "thd,shd->hts", query_spiked, key_spiked, preferred_element_type=jnp.float32
    )
    scores = jnp.where(causal_keep, scores, 0.0).astype(jnp.bfloat16)
    cotangent_ring = GatherRing(cotangent_late, "tp")
    scores = cotangent_ring.advance(scores)
    mixed_rows = jnp.einsum("hts,she->the", scores, values, preferred_element_type=jnp.float32)
    mixed_rows = mixed_rows + jnp.einsum("thd,hde->the", query_wide, prior_state, precision=highest)
    mixed_rows = cotangent_ring.advance(mixed_rows)
    inv_rms = lax.rsqrt(jnp.mean(mixed_rows * mixed_rows, axis=-1, keepdims=True) + EPSILON)
    normed = mixed_rows * inv_rms
    attended = normed.astype(jnp.bfloat16).reshape(block_rows, features)
    head_part = masked_matmul_nn(attended, out_planes, out_spread, jnp.bfloat16)[0]
    head_part = cotangent_ring.advance(head_part)
    grad_rows = cotangent_ring.finish().reshape(block_rows, model_width)
    head_part, grad_rows = lax.optimization_barrier((head_part, grad_rows))
    head_ring = ScatterRing(head_part, "tp")
    ctx_count = lax.axis_size("ctx")
    ctx_place = lax.axis_index("ctx")
    slice_rows = model_width // ctx_count
    slice_blocks = slice_rows // BLOCK
    norm_factor = 1.0 / math.sqrt(block_rows * ctx_count)
    out_part = jnp.einsum("tm,tf->mf", grad_rows, attended, preferred_element_type=jnp.float32)
    out_sum = lax.psum_scatter(
        out_part.astype(jnp.bfloat16), "ctx", scatter_dimension=0, tiled=True
    ).astype(jnp.float32)
    out_keep = lax.dynamic_slice_in_dim(out_blocks, ctx_place * slice_blocks, slice_blocks, 1)
    out_keep = jnp.broadcast_to(
        jnp.transpose(out_keep).astype(jnp.float32)[:, None, :, None],
        (slice_blocks, BLOCK, col_blocks, BLOCK),
    ).reshape(slice_rows, features)
    out_grad = jnp.transpose(out_sum * out_keep * norm_factor)
    grad_attended = masked_matmul_nt(grad_rows[None], out_planes, out_spread, jnp.float32)
    grad_attended = grad_attended.reshape(block_rows, local_heads, head_width)
    inner_mean = jnp.mean(grad_attended * normed, axis=-1, keepdims=True)
    grad_mixed = inv_rms * (grad_attended - normed * inner_mean)
    grad_low = grad_mixed.astype(jnp.bfloat16)
    local_adjoint = jnp.einsum("thd,the->hde", query_wide, grad_mixed, precision=highest)
    after_state = entering(local_adjoint, "ctx", add_states, zeros_state)
    adjoint_scores = jnp.einsum(
        "the,she->hts", grad_low, values, preferred_element_type=jnp.float32
    )
    adjoint_scores = jnp.where(causal_keep, adjoint_scores, 0.0).astype(jnp.bfloat16)
    adjoint_scores = head_ring.advance(adjoint_scores)
    grad_query = jnp.einsum(
        "hts,shd->thd", adjoint_scores, key_spiked, preferred_element_type=jnp.float32
    )
    grad_query = grad_query + jnp.einsum("the,hde->thd", grad_mixed, prior_state, precision=highest)
    grad_key = jnp.einsum(
        "hts,thd->shd", adjoint_scores, query_spiked, preferred_element_type=jnp.float32
    )
    grad_key = grad_key + jnp.einsum(
        "she,hde->shd", values.astype(jnp.float32), after_state, precision=highest
    )
    grad_value = jnp.einsum("hts,the->she", scores, grad_low, preferred_element_type=jnp.float32)
    grad_value = grad_value + jnp.einsum("shd,hde->she", key_wide, after_state, precision=highest)
    grad_proj = jnp.stack(
        [
            (grad_query * query_spikes.astype(jnp.float32)).astype(jnp.bfloat16),
            (grad_key * key_spikes.astype(jnp.float32)).astype(jnp.bfloat16),
            grad_value.astype(jnp.bfloat16),
        ],
        axis=0,
    ).reshape(3, block_rows, features)
    qkv_part = jnp.einsum("tm,ptc->mpc", gathered, grad_proj, preferred_element_type=jnp.float32)
    qkv_sum = lax.psum_scatter(
        qkv_part.astype(jnp.bfloat16), "ctx", scatter_dimension=0, tiled=True
    ).astype(jnp.float32)
    qkv_keep = lax.dynamic_slice_in_dim(qkv_blocks, ctx_place * slice_blocks, slice_blocks, 1)
    qkv_keep = jnp.broadcast_to(
        jnp.transpose(qkv_keep, (1, 0, 2)).astype(jnp.float32)[:, None, :, :, None],
        (slice_blocks, BLOCK, 3, col_blocks, BLOCK),
    ).reshape(slice_rows, 3, features)
    qkv_grad = qkv_sum * qkv_keep * norm_factor
    grad_proj = head_ring.advance(grad_proj)
    grad_proj_late = grad_proj
    token_sum = ring_scatter(
        masked_matmul_nt(grad_proj_late, qkv_planes, qkv_spread, jnp.bfloat16), "tp"
    )
    head_sum = head_ring.finish()
    layer_out = (tokens.astype(jnp.float32) + head_sum).astype(jnp.bfloat16)
    token_grad = (cotangent.astype(jnp.float32) + token_sum).astype(jnp.bfloat16)
    return (layer_out, token_grad, qkv_grad, out_grad)


def solution(mesh):
    placed = (
        P(("ctx", "tp"), None),
        P("ctx", "tp"),
        P("ctx", "tp"),
        P(None, None, "tp"),
        P(None, None, "tp"),
        P("tp", None),
        P("tp", None),
        P(("ctx", "tp"), None),
    )
    return jax.shard_map(
        on_device,
        mesh=mesh,
        in_specs=placed,
        out_specs=(
            P(("ctx", "tp"), None),
            P(("ctx", "tp"), None),
            P("ctx", None, "tp"),
            P("tp", "ctx"),
        ),
        check_vma=False,
    )
```

```python
import math

import jax
import jax.numpy as jnp
from jax import lax
from jax.experimental import pallas as pl
from jax.experimental.pallas import tpu as pltpu
from jax.sharding import PartitionSpec as P

BLOCK = 128


EPSILON = 1e-05

def _tile(n, choices=(1024, 512, 256, 128)):
    for c in choices:
        if n % c == 0:
            return c
    return n


def _masked_tile(w_ref, m_ref, wm_ref):
    for g in range(w_ref.shape[0] // BLOCK):
        rows = slice(g * BLOCK, (g + 1) * BLOCK)
        wm_ref[rows, :] = w_ref[rows, :] * m_ref[g]


def _nn_kernel(a_ref, w_ref, m_ref, o_ref, acc_ref, wm_ref):
    k = pl.program_id(2)

    @pl.when(k == 0)
    def _():
        acc_ref[...] = jnp.zeros_like(acc_ref)

    _masked_tile(w_ref, m_ref, wm_ref)
    acc_ref[...] += jnp.dot(a_ref[...], wm_ref[...], preferred_element_type=jnp.float32)

    @pl.when(k == pl.num_programs(2) - 1)
    def _():
        o_ref[...] = acc_ref[...].astype(o_ref.dtype)


def _nt_kernel(a_ref, w_ref, m_ref, o_ref, acc_ref, wm_ref):
    p = pl.program_id(1)
    k = pl.program_id(2)

    @pl.when((p == 0) & (k == 0))
    def _():
        acc_ref[...] = jnp.zeros_like(acc_ref)

    _masked_tile(w_ref, m_ref, wm_ref)
    acc_ref[...] += lax.dot_general(
        a_ref[...], wm_ref[...], (((1,), (1,)), ((), ())), preferred_element_type=jnp.float32
    )

    @pl.when((p == pl.num_programs(1) - 1) & (k == pl.num_programs(2) - 1))
    def _():
        o_ref[...] = acc_ref[...].astype(o_ref.dtype)


def masked_matmul_nn(a, w, mask, out_dtype):
    m = a.shape[0]
    planes, rows, cols = w.shape
    tk, tn = _tile(rows), _tile(cols)
    grid = (planes, cols // tn, rows // tk)
    return pl.pallas_call(
        _nn_kernel,
        grid=grid,
        in_specs=[
            pl.BlockSpec((m, tk), lambda p, j, k: (0, k)),
            pl.BlockSpec((None, tk, tn), lambda p, j, k: (p, k, j)),
            pl.BlockSpec((None, tk // BLOCK, 1, tn), lambda p, j, k: (p, k, 0, j)),
        ],
        out_specs=pl.BlockSpec((None, m, tn), lambda p, j, k: (p, 0, j)),
        out_shape=jax.ShapeDtypeStruct((planes, m, cols), out_dtype),
        scratch_shapes=[pltpu.VMEM((m, tn), jnp.float32), pltpu.VMEM((tk, tn), w.dtype)],
        compiler_params=pltpu.CompilerParams(
            dimension_semantics=("parallel", "parallel", "arbitrary"),
            vmem_limit_bytes=48 * 1024 * 1024,
        ),
        cost_estimate=pl.CostEstimate(
            flops=2 * m * planes * rows * cols,
            bytes_accessed=a.size * 2 * planes * (cols // tn) + w.size * 2
            + m * planes * cols * jnp.dtype(out_dtype).itemsize,
            transcendentals=0,
        ),
    )(a, w, mask)


def masked_matmul_nt(a, w, mask, out_dtype):
    planes, m, _ = a.shape
    _, rows, cols = w.shape
    tr, tk = _tile(rows), _tile(cols)
    grid = (rows // tr, planes, cols // tk)
    return pl.pallas_call(
        _nt_kernel,
        grid=grid,
        in_specs=[
            pl.BlockSpec((None, m, tk), lambda i, p, k: (p, 0, k)),
            pl.BlockSpec((None, tr, tk), lambda i, p, k: (p, i, k)),
            pl.BlockSpec((None, tr // BLOCK, 1, tk), lambda i, p, k: (p, i, 0, k)),
        ],
        out_specs=pl.BlockSpec((m, tr), lambda i, p, k: (0, i)),
        out_shape=jax.ShapeDtypeStruct((m, rows), out_dtype),
        scratch_shapes=[pltpu.VMEM((m, tr), jnp.float32), pltpu.VMEM((tr, tk), w.dtype)],
        compiler_params=pltpu.CompilerParams(
            dimension_semantics=("parallel", "arbitrary", "arbitrary"),
            vmem_limit_bytes=48 * 1024 * 1024,
        ),
        cost_estimate=pl.CostEstimate(
            flops=2 * m * planes * rows * cols,
            bytes_accessed=a.size * 2 * (rows // tr) + w.size * 2
            + m * rows * jnp.dtype(out_dtype).itemsize,
            transcendentals=0,
        ),
    )(a, w, mask)


def ring_gather(value, axis, work=None):
    count = lax.axis_size(axis)
    place = lax.axis_index(axis)
    step = [(index, (index + 1) % count) for index in range(count)]
    moving = value
    placed = jnp.zeros((count,) + value.shape, value.dtype)
    placed = lax.dynamic_update_index_in_dim(placed, value, place, 0)
    results = None
    if work is not None:
        done = work(value)
        results = jnp.zeros((done.shape[0], count) + done.shape[1:], done.dtype)
        results = lax.dynamic_update_index_in_dim(results, done, place, 1)
    for lap in range(1, count):
        moving = lax.ppermute(moving, axis, step)
        source = (place + count - lap) % count
        placed = lax.dynamic_update_index_in_dim(placed, moving, source, 0)
        if work is not None:
            results = lax.dynamic_update_index_in_dim(results, work(moving), source, 1)
    return placed, results


def ring_scatter(value, axis):
    count = lax.axis_size(axis)
    place = lax.axis_index(axis)
    step = [(index, (index + 1) % count) for index in range(count)]
    rows = value.shape[0] // count
    pieces = value.reshape((count, rows) + value.shape[1:])

    def piece(index):
        return lax.dynamic_index_in_dim(pieces, index % count, 0, False).astype(jnp.float32)

    running = piece(place + count - 1)
    for lap in range(1, count):
        arrived = lax.ppermute(running.astype(jnp.bfloat16), axis, step)
        running = arrived.astype(jnp.float32) + piece(place + 2 * count - 1 - lap)
    return running


class GatherRing:
    def __init__(self, value, axis):
        self.axis = axis
        self.count = lax.axis_size(axis)
        self.place = lax.axis_index(axis)
        self.step = [(index, (index + 1) % self.count) for index in range(self.count)]
        self.moving = value
        placed = jnp.zeros((self.count,) + value.shape, value.dtype)
        self.placed = lax.dynamic_update_index_in_dim(placed, value, self.place, 0)
        self.lap = 1

    def advance(self, tie=None):
        if self.lap >= self.count:
            return tie
        moved = lax.ppermute(self.moving, self.axis, self.step)
        if tie is not None:
            moved, tie = lax.optimization_barrier((moved, tie))
        source = (self.place + self.count - self.lap) % self.count
        self.placed = lax.dynamic_update_index_in_dim(self.placed, moved, source, 0)
        self.moving = moved
        self.lap += 1
        return tie

    def finish(self):
        while self.lap < self.count:
            self.advance()
        return self.placed


class ScatterRing:
    def __init__(self, value, axis):
        self.axis = axis
        self.count = lax.axis_size(axis)
        self.place = lax.axis_index(axis)
        self.step = [(index, (index + 1) % self.count) for index in range(self.count)]
        rows = value.shape[0] // self.count
        self.pieces = value.reshape((self.count, rows) + value.shape[1:])
        self.running = self.piece(self.place + self.count - 1)
        self.lap = 1

    def piece(self, index):
        return lax.dynamic_index_in_dim(
            self.pieces, index % self.count, 0, False
        ).astype(jnp.float32)

    def advance(self, tie=None):
        if self.lap >= self.count:
            return tie
        arrived = lax.ppermute(self.running.astype(jnp.bfloat16), self.axis, self.step)
        if tie is not None:
            arrived, tie = lax.optimization_barrier((arrived, tie))
        self.running = arrived.astype(jnp.float32) + self.piece(
            self.place + 2 * self.count - 1 - self.lap
        )
        self.lap += 1
        return tie

    def finish(self):
        while self.lap < self.count:
            self.advance()
        return self.running


def carried_in(value, axis, join, neutral):
    place = lax.axis_index(axis)
    gathered = lax.all_gather(value.astype(jnp.bfloat16), axis)
    state = jnp.zeros_like(value) + jnp.asarray(neutral, value.dtype)

    def carried_one(lap, state):
        return join(state, lax.dynamic_index_in_dim(gathered, lap, 0, False).astype(value.dtype))

    return lax.fori_loop(0, place, carried_one, state)


def entering(value, axis, join, neutral):
    count = lax.axis_size(axis)
    place = lax.axis_index(axis)
    ahead = count - 1 - place
    gathered = lax.all_gather(
        value.astype(jnp.bfloat16 if value.dtype == jnp.float32 else value.dtype), axis
    )
    state = jnp.zeros_like(value) + jnp.asarray(neutral, value.dtype)

    def entering_one(lap, state):
        source = count - 1 - lap
        return join(state, lax.dynamic_index_in_dim(gathered, source, 0, False).astype(value.dtype))

    return lax.fori_loop(0, ahead, entering_one, state)


def expand_blocks(blocks):
    row_blocks, col_blocks = blocks.shape
    spread = jnp.broadcast_to(
        blocks.astype(jnp.bfloat16)[:, None, :, None], (row_blocks, BLOCK, col_blocks, BLOCK)
    )
    return spread.reshape(row_blocks * BLOCK, col_blocks * BLOCK)


def qkv_keep_table(qkv_blocks):
    tables = [expand_blocks(qkv_blocks[projection]) for projection in range(3)]
    return jnp.stack(tables, axis=1)


def add_states(earlier, following):
    return earlier + following


def on_device(
    tokens, spike_query, spike_key, qkv_weight, qkv_blocks, out_weight, out_blocks, cotangent
):
    model_width = tokens.shape[1]
    block_rows = spike_query.shape[0]
    local_heads = spike_query.shape[1]
    features = qkv_weight.shape[2]
    head_width = features // local_heads
    row_blocks = model_width // BLOCK
    col_blocks = features // BLOCK
    highest = lax.Precision.HIGHEST
    qkv_planes = jnp.transpose(qkv_weight, (1, 0, 2))
    qkv_spread = jnp.broadcast_to(
        qkv_blocks.astype(jnp.bfloat16)[:, :, None, :, None],
        (3, row_blocks, 1, col_blocks, BLOCK),
    ).reshape(3, row_blocks, 1, features)
    out_planes = out_weight[None]
    out_spread = jnp.broadcast_to(
        out_blocks.astype(jnp.bfloat16)[None, :, None, :, None],
        (1, col_blocks, 1, row_blocks, BLOCK),
    ).reshape(1, col_blocks, 1, model_width)
    gathered, projected = ring_gather(
        tokens, "tp", lambda piece: masked_matmul_nn(piece, qkv_planes, qkv_spread, jnp.bfloat16)
    )
    gathered = gathered.reshape(block_rows, model_width)
    projected = projected.reshape(3, block_rows, features)
    projected, cotangent_late = lax.optimization_barrier((projected, cotangent))
    projected = projected.reshape(3, block_rows, local_heads, head_width)
    query_spikes = spike_query.astype(jnp.bfloat16)[:, :, None]
    key_spikes = spike_key.astype(jnp.bfloat16)[:, :, None]
    query_spiked = projected[0] * query_spikes
    key_spiked = projected[1] * key_spikes
    values = projected[2]
    query_wide = query_spiked.astype(jnp.float32)
    key_wide = key_spiked.astype(jnp.float32)
    local_state = jnp.einsum("shd,she->hde", key_spiked, values, preferred_element_type=jnp.float32)
    zeros_state = jnp.zeros_like(local_state)
    prior_state = carried_in(local_state, "ctx", add_states, zeros_state)
    positions = lax.iota(jnp.int32, block_rows)
    causal_keep = positions[:, None] >= positions[None, :]
    scores = jnp.einsum(
        "thd,shd->hts", query_spiked, key_spiked, preferred_element_type=jnp.float32
    )
    scores = jnp.where(causal_keep, scores, 0.0).astype(jnp.bfloat16)
    cotangent_ring = GatherRing(cotangent_late, "tp")
    scores = cotangent_ring.advance(scores)
    mixed_rows = jnp.einsum("hts,she->the", scores, values, preferred_element_type=jnp.float32)
    mixed_rows = mixed_rows + jnp.einsum("thd,hde->the", query_wide, prior_state, precision=highest)
    mixed_rows = cotangent_ring.advance(mixed_rows)
    inv_rms = lax.rsqrt(jnp.mean(mixed_rows * mixed_rows, axis=-1, keepdims=True) + EPSILON)
    normed = mixed_rows * inv_rms
    attended = normed.astype(jnp.bfloat16).reshape(block_rows, features)
    head_part = masked_matmul_nn(attended, out_planes, out_spread, jnp.bfloat16)[0]
    head_part = cotangent_ring.advance(head_part)
    grad_rows = cotangent_ring.finish().reshape(block_rows, model_width)
    head_part, grad_rows = lax.optimization_barrier((head_part, grad_rows))
    head_ring = ScatterRing(head_part, "tp")
    ctx_count = lax.axis_size("ctx")
    ctx_place = lax.axis_index("ctx")
    slice_rows = model_width // ctx_count
    slice_blocks = slice_rows // BLOCK
    norm_factor = 1.0 / math.sqrt(block_rows * ctx_count)
    out_part = jnp.einsum("tm,tf->mf", grad_rows, attended, preferred_element_type=jnp.float32)
    out_sum = lax.psum_scatter(
        out_part.astype(jnp.bfloat16), "ctx", scatter_dimension=0, tiled=True
    ).astype(jnp.float32)
    out_keep = lax.dynamic_slice_in_dim(out_blocks, ctx_place * slice_blocks, slice_blocks, 1)
    out_keep = jnp.broadcast_to(
        jnp.transpose(out_keep).astype(jnp.float32)[:, None, :, None],
        (slice_blocks, BLOCK, col_blocks, BLOCK),
    ).reshape(slice_rows, features)
    out_grad = jnp.transpose(out_sum * out_keep * norm_factor)
    grad_attended = masked_matmul_nt(grad_rows[None], out_planes, out_spread, jnp.float32)
    grad_attended = grad_attended.reshape(block_rows, local_heads, head_width)
    inner_mean = jnp.mean(grad_attended * normed, axis=-1, keepdims=True)
    grad_mixed = inv_rms * (grad_attended - normed * inner_mean)
    grad_low = grad_mixed.astype(jnp.bfloat16)
    local_adjoint = jnp.einsum("thd,the->hde", query_wide, grad_mixed, precision=highest)
    after_state = entering(local_adjoint, "ctx", add_states, zeros_state)
    adjoint_scores = jnp.einsum(
        "the,she->hts", grad_low, values, preferred_element_type=jnp.float32
    )
    adjoint_scores = jnp.where(causal_keep, adjoint_scores, 0.0).astype(jnp.bfloat16)
    adjoint_scores = head_ring.advance(adjoint_scores)
    grad_query = jnp.einsum(
        "hts,shd->thd", adjoint_scores, key_spiked, preferred_element_type=jnp.float32
    )
    grad_query = grad_query + jnp.einsum("the,hde->thd", grad_mixed, prior_state, precision=highest)
    grad_key = jnp.einsum(
        "hts,thd->shd", adjoint_scores, query_spiked, preferred_element_type=jnp.float32
    )
    grad_key = grad_key + jnp.einsum(
        "she,hde->shd", values.astype(jnp.float32), after_state, precision=highest
    )
    grad_value = jnp.einsum("hts,the->she", scores, grad_low, preferred_element_type=jnp.float32)
    grad_value = grad_value + jnp.einsum("shd,hde->she", key_wide, after_state, precision=highest)
    grad_proj = jnp.stack(
        [
            (grad_query * query_spikes.astype(jnp.float32)).astype(jnp.bfloat16),
            (grad_key * key_spikes.astype(jnp.float32)).astype(jnp.bfloat16),
            grad_value.astype(jnp.bfloat16),
        ],
        axis=0,
    ).reshape(3, block_rows, features)
    qkv_part = jnp.einsum("tm,ptc->mpc", gathered, grad_proj, preferred_element_type=jnp.float32)
    qkv_sum = lax.psum_scatter(
        qkv_part.astype(jnp.bfloat16), "ctx", scatter_dimension=0, tiled=True
    ).astype(jnp.float32)
    qkv_keep = lax.dynamic_slice_in_dim(qkv_blocks, ctx_place * slice_blocks, slice_blocks, 1)
    qkv_keep = jnp.broadcast_to(
        jnp.transpose(qkv_keep, (1, 0, 2)).astype(jnp.float32)[:, None, :, :, None],
        (slice_blocks, BLOCK, 3, col_blocks, BLOCK),
    ).reshape(slice_rows, 3, features)
    qkv_scale = lax.optimization_barrier(qkv_keep * norm_factor)
    qkv_grad = qkv_sum * qkv_scale
    grad_proj = head_ring.advance(grad_proj)
    grad_proj_late = grad_proj
    token_sum = ring_scatter(
        masked_matmul_nt(grad_proj_late, qkv_planes, qkv_spread, jnp.bfloat16), "tp"
    )
    head_sum = head_ring.finish()
    layer_out = (tokens.astype(jnp.float32) + head_sum).astype(jnp.bfloat16)
    token_grad = (cotangent.astype(jnp.float32) + token_sum).astype(jnp.bfloat16)
    return (layer_out, token_grad, qkv_grad, out_grad)


def solution(mesh):
    placed = (
        P(("ctx", "tp"), None),
        P("ctx", "tp"),
        P("ctx", "tp"),
        P(None, None, "tp"),
        P(None, None, "tp"),
        P("tp", None),
        P("tp", None),
        P(("ctx", "tp"), None),
    )
    return jax.shard_map(
        on_device,
        mesh=mesh,
        in_specs=placed,
        out_specs=(
            P(("ctx", "tp"), None),
            P(("ctx", "tp"), None),
            P("ctx", None, "tp"),
            P("tp", "ctx"),
        ),
        check_vma=False,
    )
```
